32 devices in a mesh: ex: 8 (over z, y), ey: 4 (over x, core).
Axes of the slice: x: 2, y: 2, z: 4, core: 2. Of those that a mesh axis runs over, the one named last changes fastest.
Arguments:
- source: float32 [8, 4, 8, 8, 8, 128], P('ex', 'ey'), may hold values from -8 to 8
- metric: float32 [4, 8, 4, 128], P(None, 'ex', 'ey'), may hold values from 0.5 to 2
- fac_point: int32 [8, 16384], P('ex', 'ey'), may hold values from 0 to 65535
- fac_strip: int32 [8, 16384, 1], P('ex', 'ey'), may hold values from 0 to 3; in each aligned block of 4096 rows (0 to 4095, 4096 to 8191, ..., all dimensions but the last counted through in order) at most 4096 rows name the same one
- fac_shell: int32 [8, 16384], P('ex', 'ey'), may hold values from 0 to 16383
- fac_area: float32 [8, 16384], P('ex', 'ey'), may hold values from 0.5 to 2
Outputs:
- pressure: float32 [8, 4, 8, 8, 8, 128], P('ex', 'ey')
- resid: float32 [8, 4, 8, 8, 8, 128], P('ex', 'ey')
- shell_load: float32 [65536], P('ey')
The draws below stay inside these ranges and needn't reach their ends.
Inputs may be any that keep to these rules, and one draw needn't show every extreme that they name: `fac_strip`: among the facade points of one device at most 4096 go to one strip, and in every draw some device sends exactly 4096 to some strip.
All inputs are finite; a program needn't handle non-finite values.
Results may differ from the reference program's by a relative error of at most 0.00021.
Values sent between devices are 32-bit elements; how exact they have to be, the bound alone decides.
No kernel may reach another device: no remote copies, remote signals or barrier semaphores. Data moves between devices by JAX's collectives and lax.ppermute only.
A program may use at most 64 MiB of HBM per device.

```python
import math
import jax
import jax.numpy as jnp
import numpy as np
from jax import lax

P_SIZE = 8
NXE = 1
NYE = 1
EZ = 128
SWEEPS = 4
FAC_DEV = 4096
SHELL_STRIP = 16384
NXG = 8
NYG = 4
SHELLS = 65536
CAP = 4096
BLOCK_PTS = 65536
N_EX = 8
N_EY = 4


def draw_source(key, part):
    dims = (NXG, NYG, P_SIZE, P_SIZE, P_SIZE, EZ)
    rough_part = jax.random.normal(key, dims, jnp.float32)
    return jnp.clip(rough_part, -6.0, 6.0)


def plant(drawn, stream_key, least, high):
    index_at = [jax.random.randint(jax.random.fold_in(stream_key, axis), (), 0, length) for axis, length in enumerate(drawn.shape)]
    main_axis = drawn.shape.index(max(drawn.shape))
    neighbour = index_at[:main_axis] + [(index_at[main_axis] + 1) % drawn.shape[main_axis]] + index_at[main_axis + 1:]
    return drawn.at[tuple(index_at)].set(least).at[tuple(neighbour)].set(high)


def steps_of(rng, shape, shards, least, high):
    loudness, own = 1.0, jax.random.fold_in(rng, 6)
    for dim, blocks in shards:
        draws = jnp.exp(jax.random.uniform(jax.random.fold_in(own, dim), (blocks,), jnp.float32, least / len(shards), high / len(shards)))
        loudness = loudness * jnp.repeat(draws, shape[dim] // blocks).reshape([-1 if axis == dim else 1 for axis in range(len(shape))])
    return loudness


def assign_block(own_key, own, number, rows, number_of, top, most, slope):
    order = jax.random.permutation(own_key, number_of)
    packed, common = portions_of(number_of, rows * top, most, slope, True), portions_of(number_of, rows * top, most, slope, False)
    places = jnp.arange(number_of)

    def named(lengths, rotation):
        used = int((lengths > 0).sum())
        fixed = max(1, used // 4)
        moved = fixed + (places - fixed + rotation * (used - fixed)) % max(1, number_of - fixed)
        return jnp.zeros((number_of,), jnp.int32).at[order[jnp.where(places < fixed, places, moved)]].set(jnp.asarray(lengths, jnp.int32))

    lengths = jnp.where(number % 4 == 0, named(packed, number // 4), named(common, number - number // 4 - 1))
    mixed = jax.random.permutation(jax.random.fold_in(own, 3), number_of)
    donor, sink = mixed[0:number_of // 2 * 2:2], mixed[1:number_of // 2 * 2:2]
    room = jnp.minimum(lengths[donor] - 1, most - lengths[sink]) // 2
    room = jnp.where((donor == order[0]) | (sink == order[0]) | (lengths[sink] == 0), 0, jnp.maximum(room, 0))
    moved = jax.random.randint(jax.random.fold_in(own, 4), (number_of // 2,), 0, 1 << 20) % (room + 1)
    lengths = lengths.at[donor].add(-moved).at[sink].add(moved)
    members = jnp.searchsorted(jnp.cumsum(lengths), jnp.arange(rows * top), side="right").astype(jnp.int32)
    table = members.reshape(top, rows).T
    table = table[jax.random.permutation(jax.random.fold_in(own, 1), rows)]
    rotation = jax.random.randint(jax.random.fold_in(own, 2), (rows, 1), 0, top)
    return jnp.take_along_axis(table, (jnp.arange(top)[None, :] + rotation) % top, axis=1)


def portions_of(number_of, total, reach, slope, full):
    portions = [(1 << 20) // math.isqrt(standing ** slope) + 1 for standing in range(1, number_of + 1)]
    largest = reach if full else min(reach, max(-(-total // number_of), total * portions[0] // sum(portions)))
    least = 1 if total - largest >= number_of - 1 else 0
    holding, spare = [largest] + [least] * (number_of - 1), total - largest - least * (number_of - 1)
    while spare > 0:
        free = [i for i in range(1, number_of) if holding[i] < largest] or [i for i in range(1, number_of) if holding[i] < reach]
        whole, left = sum([portions[i] for i in free]), spare
        for i in free:
            extra = min(reach - holding[i], max(1, left * portions[i] // whole), spare)
            holding[i] = holding[i] + extra
            spare = spare - extra
    return np.array(holding)


def setup_inputs(seed: int = 0) -> dict:
    splits = jax.random.split(jax.random.key(seed), 7)
    source = draw_source(jax.random.fold_in(splits[6], 71), 0)
    metric = jnp.clip(jnp.exp(math.log(2.0) - 1.3862944 * jax.random.uniform(splits[1], (4, NXG, NYG, EZ), jnp.float32) ** steps_of(splits[1], (4, NXG, NYG, EZ), ((1, 8), (2, 4)), -0.2, 0.2)), 0.5, 2.0)
    fac_point = plant(jax.random.randint(splits[2], (N_EX, N_EY * FAC_DEV), 0, BLOCK_PTS), jax.random.fold_in(splits[2], 1), 0, BLOCK_PTS - 1).astype(jnp.int32)
    fac_strip_keys = jax.random.split(jax.random.fold_in(splits[3], 1), N_EX * (N_EY * FAC_DEV) // FAC_DEV)
    fac_strip_turns = jax.random.permutation(jax.random.fold_in(splits[3], 3), N_EX * (N_EY * FAC_DEV) // FAC_DEV)
    fac_strip = jax.vmap(lambda own, number: assign_block(jax.random.fold_in(splits[3], 2), own, number, FAC_DEV, N_EY, 1, CAP, 2))(fac_strip_keys, fac_strip_turns).reshape((N_EX, N_EY * FAC_DEV, 1))
    fac_shell = plant(jax.random.randint(splits[4], (N_EX, N_EY * FAC_DEV), 0, SHELL_STRIP), jax.random.fold_in(splits[4], 1), 0, SHELL_STRIP - 1).astype(jnp.int32)
    fac_area = jnp.clip(jnp.exp(math.log(2.0) - 1.3862944 * jax.random.uniform(splits[5], (N_EX, N_EY * FAC_DEV), jnp.float32) ** steps_of(splits[5], (N_EX, N_EY * FAC_DEV), ((0, 8), (1, 4)), -0.2, 0.2)), 0.5, 2.0)
    return dict(source=source, metric=metric, fac_point=fac_point, fac_strip=fac_strip, fac_shell=fac_shell, fac_area=fac_area)


def gll_tables():
    degree = 7
    points = np.array([-1.0, -0.8717401485096066, -0.5917001814331423, -0.2092992179024789,
                       0.2092992179024789, 0.5917001814331423, 0.8717401485096066, 1.0])
    previous = points * 0.0 + 1.0
    current = points * 1.0
    for order in range(1, degree):
        following = ((2 * order + 1) * points * current - order * previous) / (order + 1)
        previous = current
        current = following
    legendre_at = current
    weights = 2.0 / (degree * (degree + 1) * legendre_at ** 2)
    count = degree + 1
    same = np.array([[1.0 if row == col else 0.0 for col in range(count)] for row in range(count)])
    between = points[:, None] - points[None, :] + same
    deriv = (legendre_at[:, None] / legendre_at[None, :]) / between * (1.0 - same)
    deriv[0, 0] = -degree * (degree + 1) / 4.0
    deriv[-1, -1] = degree * (degree + 1) / 4.0
    stiff = deriv.T @ (weights[:, None] * deriv)
    return jnp.asarray(weights, jnp.float32), jnp.asarray(stiff, jnp.float32)


def spread(metric, which):
    return metric[which][:, :, None, None, None, :]


def element_apply(values_in, metric, weights, stiff):
    top = lax.Precision.HIGHEST
    weight_i = weights[None, None, :, None, None, None]
    weight_j = weights[None, None, None, :, None, None]
    weight_k = weights[None, None, None, None, :, None]
    along_x = jnp.einsum('im,abmjkc->abijkc', stiff, values_in, precision=top)
    along_y = jnp.einsum('jm,abimkc->abijkc', stiff, values_in, precision=top)
    along_z = jnp.einsum('km,abijmc->abijkc', stiff, values_in, precision=top)
    return (spread(metric, 0) * weight_j * weight_k * along_x
            + spread(metric, 1) * weight_i * weight_k * along_y
            + spread(metric, 2) * weight_i * weight_j * along_z
            + spread(metric, 3) * weight_i * weight_j * weight_k * values_in)


def local_diagonal(metric, weights, stiff):
    stiff_diag = jnp.diagonal(stiff)
    weight_i = weights[None, None, :, None, None, None]
    weight_j = weights[None, None, None, :, None, None]
    weight_k = weights[None, None, None, None, :, None]
    diag_i = stiff_diag[None, None, :, None, None, None]
    diag_j = stiff_diag[None, None, None, :, None, None]
    diag_k = stiff_diag[None, None, None, None, :, None]
    return (spread(metric, 0) * diag_i * weight_j * weight_k
            + spread(metric, 1) * weight_i * diag_j * weight_k
            + spread(metric, 2) * weight_i * weight_j * diag_k
            + spread(metric, 3) * weight_i * weight_j * weight_k)


def faces(values_in, face_dim):
    last = values_in.shape[face_dim] - 1
    lower = lax.index_in_dim(values_in, 0, face_dim, keepdims=False)
    upper = lax.index_in_dim(values_in, last, face_dim, keepdims=False)
    return lower, upper


def combine(values_in, face_dim, elem_dim, lower, upper, before, after):
    total = lower.shape[elem_dim]
    upper_prev = jnp.concatenate([before, lax.slice_in_dim(upper, 0, total - 1, axis=elem_dim)], elem_dim)
    lower_next = jnp.concatenate([lax.slice_in_dim(lower, 1, total, axis=elem_dim), after], elem_dim)
    middle = lax.slice_in_dim(values_in, 1, values_in.shape[face_dim] - 1, axis=face_dim)
    return jnp.concatenate([jnp.expand_dims(lower + upper_prev, face_dim), middle,
                            jnp.expand_dims(upper + lower_next, face_dim)], face_dim)


def assemble(values_in):
    lower, upper = faces(values_in, 2)
    empty = jnp.zeros_like(upper[:1])
    values_in = combine(values_in, 2, 0, lower, upper, empty, empty)
    lower, upper = faces(values_in, 3)
    empty = jnp.zeros_like(upper[:, :1])
    values_in = combine(values_in, 3, 1, lower, upper, empty, empty)
    lower, upper = faces(values_in, 4)
    empty = jnp.zeros_like(upper[..., :1])
    return combine(values_in, 4, 4, lower, upper, empty, empty)


def reference(source, metric, fac_point, fac_strip, fac_shell, fac_area):
    weights, stiff = gll_tables()
    high, low = 2.0, 0.2
    theta = (high + low) / 2.0
    delta = (high - low) / 2.0
    sigma = theta / delta
    rho_now = 1.0 / sigma
    rhs = assemble(source)
    pinv = 1.0 / assemble(local_diagonal(metric, weights, stiff))
    pressure = jnp.zeros_like(source)
    resid = rhs
    update = pinv * resid / theta
    for step in range(SWEEPS):
        pressure = pressure + update
        resid = resid - assemble(element_apply(update, metric, weights, stiff))
        if step + 1 < SWEEPS:
            rho_new = 1.0 / (2.0 * sigma - rho_now)
            update = rho_new * rho_now * update + (2.0 * rho_new / delta) * pinv * resid
            rho_now = rho_new
    blocks = pressure.reshape(N_EX, NXE, N_EY, NYE, P_SIZE, P_SIZE, P_SIZE, EZ)
    blocks = blocks.transpose(0, 2, 1, 3, 4, 5, 6, 7).reshape(N_EX, N_EY, -1)
    picks = fac_point.reshape(N_EX, N_EY, FAC_DEV).astype(jnp.int32)
    samples = jnp.take_along_axis(blocks, picks, axis=2).reshape(-1)
    shell_ids = (fac_strip.reshape(-1) * SHELL_STRIP + fac_shell.reshape(-1)).astype(jnp.int32)
    areas = fac_area.reshape(-1)
    numer = jax.ops.segment_sum(areas * samples, shell_ids, SHELLS)
    denom = jax.ops.segment_sum(areas, shell_ids, SHELLS)
    shell_load = numer / jnp.maximum(denom, 1.0)
    return pressure, resid, shell_load
```

```python
import jax
import jax.numpy as jnp
import numpy as np
from jax import lax
from jax.sharding import PartitionSpec as P

SWEEPS = 4
SHELL_STRIP = 16384


def padded_2(block, sides, width):
    for axis, dim in sides:
        count = lax.axis_size(axis)
        forward = [(i, i + 1) for i in range(count - 1)]
        backward = [(target, source) for source, target in forward]
        low = lax.ppermute(
            lax.slice_in_dim(block, block.shape[dim] - width, None, axis=dim), axis, forward
        )
        high = lax.ppermute(lax.slice_in_dim(block, 0, width, axis=dim), axis, backward)
        block = jnp.concatenate([low, block, high], axis=dim)
    return block


def gll_tables():
    degree = 7
    points = np.array(
        [
            -1.0,
            -0.8717401485096066,
            -0.5917001814331423,
            -0.2092992179024789,
            0.2092992179024789,
            0.5917001814331423,
            0.8717401485096066,
            1.0,
        ]
    )
    previous = points * 0.0 + 1.0
    current = points * 1.0
    for order in range(1, degree):
        following = ((2 * order + 1) * points * current - order * previous) / (order + 1)
        previous = current
        current = following
    weights = 2.0 / (degree * (degree + 1) * current**2)
    count = degree + 1
    same = np.array([[1.0 if row == col else 0.0 for col in range(count)] for row in range(count)])
    between = points[:, None] - points[None, :] + same
    deriv = current[:, None] / current[None, :] / between * (1.0 - same)
    deriv[0, 0] = -degree * (degree + 1) / 4.0
    deriv[-1, -1] = degree * (degree + 1) / 4.0
    stiff = deriv.T @ (weights[:, None] * deriv)
    return (jnp.asarray(weights, jnp.float32), jnp.asarray(stiff, jnp.float32))


def spread(metric, which):
    return metric[which][:, :, None, None, None, :]


def element_apply(values_in, metric, weights, stiff):
    top = lax.Precision.HIGHEST
    weight_i = weights[None, None, :, None, None, None]
    weight_j = weights[None, None, None, :, None, None]
    weight_k = weights[None, None, None, None, :, None]
    along_x = jnp.einsum("im,abmjkc->abijkc", stiff, values_in, precision=top)
    along_y = jnp.einsum("jm,abimkc->abijkc", stiff, values_in, precision=top)
    along_z = jnp.einsum("km,abijmc->abijkc", stiff, values_in, precision=top)
    return (
        spread(metric, 0) * weight_j * weight_k * along_x
        + spread(metric, 1) * weight_i * weight_k * along_y
        + spread(metric, 2) * weight_i * weight_j * along_z
        + spread(metric, 3) * weight_i * weight_j * weight_k * values_in
    )


def local_diagonal(metric, weights, stiff):
    stiff_diag = jnp.diagonal(stiff)
    weight_i = weights[None, None, :, None, None, None]
    weight_j = weights[None, None, None, :, None, None]
    weight_k = weights[None, None, None, None, :, None]
    diag_i = stiff_diag[None, None, :, None, None, None]
    diag_j = stiff_diag[None, None, None, :, None, None]
    diag_k = stiff_diag[None, None, None, None, :, None]
    return (
        spread(metric, 0) * diag_i * weight_j * weight_k
        + spread(metric, 1) * weight_i * diag_j * weight_k
        + spread(metric, 2) * weight_i * weight_j * diag_k
        + spread(metric, 3) * weight_i * weight_j * weight_k
    )


def faces(values_in, face_dim):
    last = values_in.shape[face_dim] - 1
    lower = lax.index_in_dim(values_in, 0, face_dim, keepdims=False)
    upper = lax.index_in_dim(values_in, last, face_dim, keepdims=False)
    return (lower, upper)


def combine(values_in, face_dim, elem_dim, lower, upper, before, after):
    total = lower.shape[elem_dim]
    upper_prev = jnp.concatenate(
        [before, lax.slice_in_dim(upper, 0, total - 1, axis=elem_dim)], elem_dim
    )
    lower_next = jnp.concatenate(
        [lax.slice_in_dim(lower, 1, total, axis=elem_dim), after], elem_dim
    )
    middle = lax.slice_in_dim(values_in, 1, values_in.shape[face_dim] - 1, axis=face_dim)
    return jnp.concatenate(
        [
            jnp.expand_dims(lower + upper_prev, face_dim),
            middle,
            jnp.expand_dims(upper + lower_next, face_dim),
        ],
        face_dim,
    )


def assemble(values_in):
    lower, upper = faces(values_in, 3)
    rim_faces = jnp.concatenate([lower, upper], 1)
    padded = padded_2(rim_faces, (("ex", 1),), 1)
    values_in = combine(values_in, 3, 1, lower, upper, padded[:, :1], padded[:, 3:])
    lower, upper = faces(values_in, 4)
    rim_faces = jnp.concatenate([lower, upper], 2)
    padded = padded_2(rim_faces, (("ey", 2),), 1)
    values_in = combine(values_in, 4, 2, lower, upper, padded[:, :, :1], padded[:, :, 3:])
    lower, upper = faces(values_in, 5)
    empty = jnp.zeros_like(upper[..., :1])
    return combine(values_in, 5, 5, lower, upper, empty, empty)


def split3(values):
    first = lax.reduce_precision(values, exponent_bits=8, mantissa_bits=7)
    rest = values - first
    second = lax.reduce_precision(rest, exponent_bits=8, mantissa_bits=7)
    third = rest - second
    return [part.astype(jnp.bfloat16) for part in (first, second, third)]


def one_hot(index, count):
    return (index[:, None] == lax.broadcasted_iota(jnp.int32, (1, count), 1)).astype(jnp.bfloat16)


def gather_flat(values, picks, lanes):
    rows = values.shape[0] // lanes
    table = values.reshape(rows, lanes)
    parts = jnp.concatenate(split3(table), axis=1)
    hit_row = one_hot(picks // lanes, rows)
    picked = jnp.dot(hit_row, parts, preferred_element_type=jnp.float32)
    picked = picked[:, :lanes] + picked[:, lanes : 2 * lanes] + picked[:, 2 * lanes :]
    hit_lane = (picks % lanes)[:, None] == lax.broadcasted_iota(jnp.int32, (1, lanes), 1)
    return jnp.sum(jnp.where(hit_lane, picked, 0.0), axis=1)


def segment_pair(first, second, ids, bins, lanes):
    rows = bins // lanes
    hit_lane = one_hot(ids % lanes, lanes)
    spread_parts = [hit_lane * part[:, None] for part in split3(first) + split3(second)]
    rhs = jnp.concatenate(spread_parts, axis=1)
    hit_row = one_hot(ids // lanes, rows)
    sums = lax.dot_general(
        hit_row, rhs, (((0,), (0,)), ((), ())), preferred_element_type=jnp.float32
    )
    sums = sums.reshape(rows, 6, lanes)
    numer = sums[:, 0] + sums[:, 1] + sums[:, 2]
    denom = sums[:, 3] + sums[:, 4] + sums[:, 5]
    return jnp.stack([numer.reshape(-1), denom.reshape(-1)])


def strip_totals(partial, strips, strip_size):
    n_ex = lax.axis_size("ex")
    piece = -(-strip_size // n_ex)
    chunks = partial.reshape(2, strips, strip_size)
    if piece * n_ex != strip_size:
        chunks = jnp.pad(chunks, ((0, 0), (0, 0), (0, piece * n_ex - strip_size)))
    chunks = chunks.reshape(2, strips, n_ex, piece).transpose(2, 1, 0, 3)
    chunks = chunks.reshape(n_ex * strips, 2, piece)
    mine = lax.all_to_all(chunks, ("ex", "ey"), 0, 0, tiled=True).sum(0)
    spread_out = jnp.broadcast_to(mine[None], (n_ex, 2, piece))
    whole = lax.all_to_all(spread_out, "ex", 0, 0, tiled=True)
    return whole.transpose(1, 0, 2).reshape(2, n_ex * piece)[:, :strip_size]


def on_device(source, metric, fac_point, fac_strip, fac_shell, fac_area):
    weights, stiff = gll_tables()
    high, low = (2.0, 0.2)
    theta = (high + low) / 2.0
    delta = (high - low) / 2.0
    sigma = theta / delta
    rho_now = 1.0 / sigma
    both = assemble(jnp.stack([source, local_diagonal(metric, weights, stiff)]))
    rhs = both[0]
    pinv = 1.0 / both[1]
    pressure = jnp.zeros_like(source)
    resid = rhs
    update = pinv * resid / theta
    for step in range(SWEEPS):
        pressure = pressure + update
        resid = resid - assemble(element_apply(update, metric, weights, stiff)[None])[0]
        if step + 1 < SWEEPS:
            rho_new = 1.0 / (2.0 * sigma - rho_now)
            update = rho_new * rho_now * update + 2.0 * rho_new / delta * pinv * resid
            rho_now = rho_new
    picks = fac_point[0]
    samples = gather_flat(pressure.reshape(-1), picks, 256)
    areas = fac_area[0]
    weighted = areas * samples
    strip_of = fac_strip[0, :, 0]
    shell_of = fac_shell[0]
    strips = lax.axis_size("ey")
    global_ids = strip_of * SHELL_STRIP + shell_of
    partial = segment_pair(weighted, areas, global_ids, strips * SHELL_STRIP, 256)
    total = strip_totals(partial, strips, SHELL_STRIP)
    shell_load = total[0] / jnp.maximum(total[1], 1.0)
    return (pressure, resid, shell_load)


def solution(mesh):
    placed = (
        P("ex", "ey", None, None, None, None),
        P(None, "ex", "ey", None),
        P("ex", "ey"),
        P("ex", "ey", None),
        P("ex", "ey"),
        P("ex", "ey"),
    )
    return jax.shard_map(
        on_device,
        mesh=mesh,
        in_specs=placed,
        out_specs=(
            P("ex", "ey", None, None, None, None),
            P("ex", "ey", None, None, None, None),
            P("ey"),
        ),
        check_vma=False,
    )
```

```python
import itertools

import jax
import jax.numpy as jnp
import numpy as np
from jax import lax
from jax.sharding import PartitionSpec as P

SWEEPS = 4
SHELL_STRIP = 16384


def gll_tables():
    degree = 7
    points = np.array(
        [
            -1.0,
            -0.8717401485096066,
            -0.5917001814331423,
            -0.2092992179024789,
            0.2092992179024789,
            0.5917001814331423,
            0.8717401485096066,
            1.0,
        ]
    )
    previous = points * 0.0 + 1.0
    current = points * 1.0
    for order in range(1, degree):
        following = ((2 * order + 1) * points * current - order * previous) / (order + 1)
        previous = current
        current = following
    weights = 2.0 / (degree * (degree + 1) * current**2)
    count = degree + 1
    same = np.array([[1.0 if row == col else 0.0 for col in range(count)] for row in range(count)])
    between = points[:, None] - points[None, :] + same
    deriv = current[:, None] / current[None, :] / between * (1.0 - same)
    deriv[0, 0] = -degree * (degree + 1) / 4.0
    deriv[-1, -1] = degree * (degree + 1) / 4.0
    stiff = deriv.T @ (weights[:, None] * deriv)
    return (jnp.asarray(weights, jnp.float32), jnp.asarray(stiff, jnp.float32))


def spread(metric, which):
    return metric[which][:, :, None, None, None, :]


def element_apply(values_in, metric, weights, stiff):
    top = lax.Precision.HIGHEST
    weight_i = weights[None, None, :, None, None, None]
    weight_j = weights[None, None, None, :, None, None]
    weight_k = weights[None, None, None, None, :, None]
    along_x = jnp.einsum("im,abmjkc->abijkc", stiff, values_in, precision=top)
    along_y = jnp.einsum("jm,abimkc->abijkc", stiff, values_in, precision=top)
    along_z = jnp.einsum("km,abijmc->abijkc", stiff, values_in, precision=top)
    return (
        spread(metric, 0) * weight_j * weight_k * along_x
        + spread(metric, 1) * weight_i * weight_k * along_y
        + spread(metric, 2) * weight_i * weight_j * along_z
        + spread(metric, 3) * weight_i * weight_j * weight_k * values_in
    )


def local_diagonal(metric, weights, stiff):
    stiff_diag = jnp.diagonal(stiff)
    weight_i = weights[None, None, :, None, None, None]
    weight_j = weights[None, None, None, :, None, None]
    weight_k = weights[None, None, None, None, :, None]
    diag_i = stiff_diag[None, None, :, None, None, None]
    diag_j = stiff_diag[None, None, None, :, None, None]
    diag_k = stiff_diag[None, None, None, None, :, None]
    return (
        spread(metric, 0) * diag_i * weight_j * weight_k
        + spread(metric, 1) * weight_i * diag_j * weight_k
        + spread(metric, 2) * weight_i * weight_j * diag_k
        + spread(metric, 3) * weight_i * weight_j * weight_k
    )


def faces(values_in, face_dim):
    last = values_in.shape[face_dim] - 1
    lower = lax.index_in_dim(values_in, 0, face_dim, keepdims=False)
    upper = lax.index_in_dim(values_in, last, face_dim, keepdims=False)
    return (lower, upper)


def combine(values_in, face_dim, elem_dim, lower, upper, before, after):
    total = lower.shape[elem_dim]
    upper_prev = jnp.concatenate(
        [before, lax.slice_in_dim(upper, 0, total - 1, axis=elem_dim)], elem_dim
    )
    lower_next = jnp.concatenate(
        [lax.slice_in_dim(lower, 1, total, axis=elem_dim), after], elem_dim
    )
    middle = lax.slice_in_dim(values_in, 1, values_in.shape[face_dim] - 1, axis=face_dim)
    return jnp.concatenate(
        [
            jnp.expand_dims(lower + upper_prev, face_dim),
            middle,
            jnp.expand_dims(upper + lower_next, face_dim),
        ],
        face_dim,
    )


def shifted(block, axes, step, sizes):
    pairs = []
    for source in itertools.product(*[range(size) for size in sizes]):
        target = [s + d for s, d in zip(source, step)]
        if all(0 <= t < size for t, size in zip(target, sizes)):
            pairs.append((linear(source, sizes), linear(target, sizes)))
    name = axes[0] if len(axes) == 1 else axes
    return lax.ppermute(block, name, pairs)


def linear(place, sizes):
    index = 0
    for p, size in zip(place, sizes):
        index = index * size + p
    return index


def assemble(values_in):
    n_ex = lax.axis_size("ex")
    n_ey = lax.axis_size("ey")
    u = values_in[:, 0, 0]
    last = u.shape[1] - 1
    x_lo, x_hi = u[:, 0], u[:, last]
    y_lo, y_hi = u[:, :, 0], u[:, :, last]
    from_xm = shifted(x_hi, ("ex",), (1,), (n_ex,))
    from_xp = shifted(x_lo, ("ex",), (-1,), (n_ex,))
    from_ym = shifted(y_hi, ("ey",), (1,), (n_ey,))
    from_yp = shifted(y_lo, ("ey",), (-1,), (n_ey,))
    both = ("ex", "ey")
    sizes = (n_ex, n_ey)
    diag_mm = shifted(u[:, last, last], both, (1, 1), sizes)
    diag_mp = shifted(u[:, last, 0], both, (1, -1), sizes)
    diag_pm = shifted(u[:, 0, last], both, (-1, 1), sizes)
    diag_pp = shifted(u[:, 0, 0], both, (-1, -1), sizes)
    middle = u[:, 1:last]
    u1 = jnp.concatenate([(x_lo + from_xm)[:, None], middle, (x_hi + from_xp)[:, None]], 1)
    ym1 = jnp.concatenate(
        [(from_ym[:, 0] + diag_mm)[:, None], from_ym[:, 1:last], (from_ym[:, last] + diag_pm)[:, None]], 1
    )
    yp1 = jnp.concatenate(
        [(from_yp[:, 0] + diag_mp)[:, None], from_yp[:, 1:last], (from_yp[:, last] + diag_pp)[:, None]], 1
    )
    lo1, hi1 = u1[:, :, 0], u1[:, :, last]
    u2 = jnp.concatenate([(lo1 + ym1)[:, :, None], u1[:, :, 1:last], (hi1 + yp1)[:, :, None]], 2)
    values_in = u2[:, None, None]
    lower, upper = faces(values_in, 5)
    empty = jnp.zeros_like(upper[..., :1])
    return combine(values_in, 5, 5, lower, upper, empty, empty)


def split3(values):
    first = lax.reduce_precision(values, exponent_bits=8, mantissa_bits=7)
    rest = values - first
    second = lax.reduce_precision(rest, exponent_bits=8, mantissa_bits=7)
    third = rest - second
    return [part.astype(jnp.bfloat16) for part in (first, second, third)]


def one_hot(index, count):
    return (index[:, None] == lax.broadcasted_iota(jnp.int32, (1, count), 1)).astype(jnp.bfloat16)


def gather_flat(values, picks, lanes):
    rows = values.shape[0] // lanes
    table = values.reshape(rows, lanes)
    parts = jnp.concatenate(split3(table), axis=1)
    hit_row = one_hot(picks // lanes, rows)
    picked = jnp.dot(hit_row, parts, preferred_element_type=jnp.float32)
    picked = picked[:, :lanes] + picked[:, lanes : 2 * lanes] + picked[:, 2 * lanes :]
    hit_lane = (picks % lanes)[:, None] == lax.broadcasted_iota(jnp.int32, (1, lanes), 1)
    return jnp.sum(jnp.where(hit_lane, picked, 0.0), axis=1)


def segment_pair(first, second, ids, bins, lanes):
    rows = bins // lanes
    hit_lane = one_hot(ids % lanes, lanes)
    spread_parts = [hit_lane * part[:, None] for part in split3(first) + split3(second)]
    rhs = jnp.concatenate(spread_parts, axis=1)
    hit_row = one_hot(ids // lanes, rows)
    sums = lax.dot_general(
        hit_row, rhs, (((0,), (0,)), ((), ())), preferred_element_type=jnp.float32
    )
    sums = sums.reshape(rows, 6, lanes)
    numer = sums[:, 0] + sums[:, 1] + sums[:, 2]
    denom = sums[:, 3] + sums[:, 4] + sums[:, 5]
    return jnp.stack([numer.reshape(-1), denom.reshape(-1)])


def strip_totals(partial, strips, strip_size):
    n_ex = lax.axis_size("ex")
    piece = -(-strip_size // n_ex)
    chunks = partial.reshape(2, strips, strip_size)
    if piece * n_ex != strip_size:
        chunks = jnp.pad(chunks, ((0, 0), (0, 0), (0, piece * n_ex - strip_size)))
    chunks = chunks.reshape(2, strips, n_ex, piece).transpose(2, 1, 0, 3)
    chunks = chunks.reshape(n_ex * strips, 2, piece)
    mine = lax.all_to_all(chunks, ("ex", "ey"), 0, 0, tiled=True).sum(0)
    spread_out = jnp.broadcast_to(mine[None], (n_ex, 2, piece))
    whole = lax.all_to_all(spread_out, "ex", 0, 0, tiled=True)
    return whole.transpose(1, 0, 2).reshape(2, n_ex * piece)[:, :strip_size]


def on_device(source, metric, fac_point, fac_strip, fac_shell, fac_area):
    weights, stiff = gll_tables()
    high, low = (2.0, 0.2)
    theta = (high + low) / 2.0
    delta = (high - low) / 2.0
    sigma = theta / delta
    rho_now = 1.0 / sigma
    both = assemble(jnp.stack([source, local_diagonal(metric, weights, stiff)]))
    rhs = both[0]
    pinv = 1.0 / both[1]
    pressure = jnp.zeros_like(source)
    resid = rhs
    update = pinv * resid / theta
    for step in range(SWEEPS):
        pressure = pressure + update
        resid = resid - assemble(element_apply(update, metric, weights, stiff)[None])[0]
        if step + 1 < SWEEPS:
            rho_new = 1.0 / (2.0 * sigma - rho_now)
            update = rho_new * rho_now * update + 2.0 * rho_new / delta * pinv * resid
            rho_now = rho_new
    picks = fac_point[0]
    samples = gather_flat(pressure.reshape(-1), picks, 256)
    areas = fac_area[0]
    weighted = areas * samples
    strip_of = fac_strip[0, :, 0]
    shell_of = fac_shell[0]
    strips = lax.axis_size("ey")
    global_ids = strip_of * SHELL_STRIP + shell_of
    partial = segment_pair(weighted, areas, global_ids, strips * SHELL_STRIP, 256)
    total = strip_totals(partial, strips, SHELL_STRIP)
    shell_load = total[0] / jnp.maximum(total[1], 1.0)
    return (pressure, resid, shell_load)


def solution(mesh):
    placed = (
        P("ex", "ey", None, None, None, None),
        P(None, "ex", "ey", None),
        P("ex", "ey"),
        P("ex", "ey", None),
        P("ex", "ey"),
        P("ex", "ey"),
    )
    return jax.shard_map(
        on_device,
        mesh=mesh,
        in_specs=placed,
        out_specs=(
            P("ex", "ey", None, None, None, None),
            P("ex", "ey", None, None, None, None),
            P("ey"),
        ),
        check_vma=False,
    )
```

```python
import jax
import jax.numpy as jnp
import numpy as np
from jax import lax
from jax.sharding import PartitionSpec as P

SWEEPS = 4
SHELL_STRIP = 16384


def padded_2(block, sides, width):
    for axis, dim in sides:
        count = lax.axis_size(axis)
        forward = [(i, i + 1) for i in range(count - 1)]
        backward = [(target, source) for source, target in forward]
        low = lax.ppermute(
            lax.slice_in_dim(block, block.shape[dim] - width, None, axis=dim), axis, forward
        )
        high = lax.ppermute(lax.slice_in_dim(block, 0, width, axis=dim), axis, backward)
        block = jnp.concatenate([low, block, high], axis=dim)
    return block


def gll_tables():
    degree = 7
    points = np.array(
        [
            -1.0,
            -0.8717401485096066,
            -0.5917001814331423,
            -0.2092992179024789,
            0.2092992179024789,
            0.5917001814331423,
            0.8717401485096066,
            1.0,
        ]
    )
    previous = points * 0.0 + 1.0
    current = points * 1.0
    for order in range(1, degree):
        following = ((2 * order + 1) * points * current - order * previous) / (order + 1)
        previous = current
        current = following
    weights = 2.0 / (degree * (degree + 1) * current**2)
    count = degree + 1
    same = np.array([[1.0 if row == col else 0.0 for col in range(count)] for row in range(count)])
    between = points[:, None] - points[None, :] + same
    deriv = current[:, None] / current[None, :] / between * (1.0 - same)
    deriv[0, 0] = -degree * (degree + 1) / 4.0
    deriv[-1, -1] = degree * (degree + 1) / 4.0
    stiff = deriv.T @ (weights[:, None] * deriv)
    return (jnp.asarray(weights, jnp.float32), jnp.asarray(stiff, jnp.float32))


def spread(metric, which):
    return metric[which][:, :, None, None, None, :]


def element_apply(values_in, metric, weights, stiff):
    top = lax.Precision.HIGHEST
    weight_i = weights[None, None, :, None, None, None]
    weight_j = weights[None, None, None, :, None, None]
    weight_k = weights[None, None, None, None, :, None]
    along_x = jnp.einsum("im,abmjkc->abijkc", stiff, values_in, precision=top)
    along_y = jnp.einsum("jm,abimkc->abijkc", stiff, values_in, precision=top)
    along_z = jnp.einsum("km,abijmc->abijkc", stiff, values_in, precision=top)
    return (
        spread(metric, 0) * weight_j * weight_k * along_x
        + spread(metric, 1) * weight_i * weight_k * along_y
        + spread(metric, 2) * weight_i * weight_j * along_z
        + spread(metric, 3) * weight_i * weight_j * weight_k * values_in
    )


def local_diagonal(metric, weights, stiff):
    stiff_diag = jnp.diagonal(stiff)
    weight_i = weights[None, None, :, None, None, None]
    weight_j = weights[None, None, None, :, None, None]
    weight_k = weights[None, None, None, None, :, None]
    diag_i = stiff_diag[None, None, :, None, None, None]
    diag_j = stiff_diag[None, None, None, :, None, None]
    diag_k = stiff_diag[None, None, None, None, :, None]
    return (
        spread(metric, 0) * diag_i * weight_j * weight_k
        + spread(metric, 1) * weight_i * diag_j * weight_k
        + spread(metric, 2) * weight_i * weight_j * diag_k
        + spread(metric, 3) * weight_i * weight_j * weight_k
    )


def faces(values_in, face_dim):
    last = values_in.shape[face_dim] - 1
    lower = lax.index_in_dim(values_in, 0, face_dim, keepdims=False)
    upper = lax.index_in_dim(values_in, last, face_dim, keepdims=False)
    return (lower, upper)


def combine(values_in, face_dim, elem_dim, lower, upper, before, after):
    total = lower.shape[elem_dim]
    upper_prev = jnp.concatenate(
        [before, lax.slice_in_dim(upper, 0, total - 1, axis=elem_dim)], elem_dim
    )
    lower_next = jnp.concatenate(
        [lax.slice_in_dim(lower, 1, total, axis=elem_dim), after], elem_dim
    )
    middle = lax.slice_in_dim(values_in, 1, values_in.shape[face_dim] - 1, axis=face_dim)
    return jnp.concatenate(
        [
            jnp.expand_dims(lower + upper_prev, face_dim),
            middle,
            jnp.expand_dims(upper + lower_next, face_dim),
        ],
        face_dim,
    )


def assemble(values_in):
    lower, upper = faces(values_in, 3)
    rim_faces = jnp.concatenate([lower, upper], 1)
    padded = padded_2(rim_faces, (("ex", 1),), 1)
    values_in = combine(values_in, 3, 1, lower, upper, padded[:, :1], padded[:, 3:])
    lower, upper = faces(values_in, 4)
    rim_faces = jnp.concatenate([lower, upper], 2)
    padded = padded_2(rim_faces, (("ey", 2),), 1)
    values_in = combine(values_in, 4, 2, lower, upper, padded[:, :, :1], padded[:, :, 3:])
    lower, upper = faces(values_in, 5)
    empty = jnp.zeros_like(upper[..., :1])
    return combine(values_in, 5, 5, lower, upper, empty, empty)


def split3(values):
    first = lax.reduce_precision(values, exponent_bits=8, mantissa_bits=7)
    rest = values - first
    second = lax.reduce_precision(rest, exponent_bits=8, mantissa_bits=7)
    third = rest - second
    return [part.astype(jnp.bfloat16) for part in (first, second, third)]


def one_hot(index, count):
    return (index[:, None] == lax.broadcasted_iota(jnp.int32, (1, count), 1)).astype(jnp.bfloat16)


def gather_flat(values, picks, lanes):
    rows = values.shape[0] // lanes
    table = values.reshape(rows, lanes)
    parts = jnp.concatenate(split3(table), axis=1)
    hit_row = one_hot(picks // lanes, rows)
    picked = jnp.dot(hit_row, parts, preferred_element_type=jnp.float32)
    picked = picked[:, :lanes] + picked[:, lanes : 2 * lanes] + picked[:, 2 * lanes :]
    hit_lane = (picks % lanes)[:, None] == lax.broadcasted_iota(jnp.int32, (1, lanes), 1)
    return jnp.sum(jnp.where(hit_lane, picked, 0.0), axis=1)


def segment_sum(values, ids, bins, lanes):
    rows = bins // lanes
    hit_lane = one_hot(ids % lanes, lanes)
    rhs = jnp.concatenate([hit_lane * part[:, None] for part in split3(values)], axis=1)
    hit_row = one_hot(ids // lanes, rows)
    sums = lax.dot_general(
        hit_row, rhs, (((0,), (0,)), ((), ())), preferred_element_type=jnp.float32
    )
    return (sums[:, :lanes] + sums[:, lanes : 2 * lanes] + sums[:, 2 * lanes :]).reshape(-1)


def strip_totals(partial, strips, strip_size):
    n_ex = lax.axis_size("ex")
    piece = -(-strip_size // n_ex)
    chunks = partial.reshape(2, strips, strip_size)
    if piece * n_ex != strip_size:
        chunks = jnp.pad(chunks, ((0, 0), (0, 0), (0, piece * n_ex - strip_size)))
    chunks = chunks.reshape(2, strips, n_ex, piece).transpose(2, 1, 0, 3)
    chunks = chunks.reshape(n_ex * strips, 2, piece)
    mine = lax.all_to_all(chunks, ("ex", "ey"), 0, 0, tiled=True).sum(0)
    spread_out = jnp.broadcast_to(mine[None], (n_ex, 2, piece))
    whole = lax.all_to_all(spread_out, "ex", 0, 0, tiled=True)
    return whole.transpose(1, 0, 2).reshape(2, n_ex * piece)[:, :strip_size]


def on_device(source, metric, fac_point, fac_strip, fac_shell, fac_area):
    weights, stiff = gll_tables()
    high, low = (2.0, 0.2)
    theta = (high + low) / 2.0
    delta = (high - low) / 2.0
    sigma = theta / delta
    rho_now = 1.0 / sigma
    both = assemble(jnp.stack([source, local_diagonal(metric, weights, stiff)]))
    rhs = both[0]
    pinv = 1.0 / both[1]
    pressure = jnp.zeros_like(source)
    resid = rhs
    update = pinv * resid / theta
    picks = fac_point[0]
    areas = fac_area[0]
    strips = lax.axis_size("ey")
    global_ids = fac_strip[0, :, 0] * SHELL_STRIP + fac_shell[0]
    denom = segment_sum(areas, global_ids, strips * SHELL_STRIP, 256)
    for step in range(SWEEPS):
        if step + 1 == SWEEPS:
            early = gather_flat(pressure.reshape(-1), picks, 256)
            samples = early + gather_flat(update.reshape(-1), picks, 256)
        pressure = pressure + update
        resid = resid - assemble(element_apply(update, metric, weights, stiff)[None])[0]
        if step + 1 < SWEEPS:
            rho_new = 1.0 / (2.0 * sigma - rho_now)
            update = rho_new * rho_now * update + 2.0 * rho_new / delta * pinv * resid
            rho_now = rho_new
    weighted = areas * samples
    numer = segment_sum(weighted, global_ids, strips * SHELL_STRIP, 256)
    partial = jnp.stack([numer, denom])
    total = strip_totals(partial, strips, SHELL_STRIP)
    shell_load = total[0] / jnp.maximum(total[1], 1.0)
    return (pressure, resid, shell_load)


def solution(mesh):
    placed = (
        P("ex", "ey", None, None, None, None),
        P(None, "ex", "ey", None),
        P("ex", "ey"),
        P("ex", "ey", None),
        P("ex", "ey"),
        P("ex", "ey"),
    )
    return jax.shard_map(
        on_device,
        mesh=mesh,
        in_specs=placed,
        out_specs=(
            P("ex", "ey", None, None, None, None),
            P("ex", "ey", None, None, None, None),
            P("ey"),
        ),
        check_vma=False,
    )
```

```python
import jax
import jax.numpy as jnp
import numpy as np
from jax import lax
from jax.sharding import PartitionSpec as P

SWEEPS = 4
SHELL_STRIP = 16384


def padded_2(block, sides, width):
    for axis, dim in sides:
        count = lax.axis_size(axis)
        forward = [(i, i + 1) for i in range(count - 1)]
        backward = [(target, source) for source, target in forward]
        low = lax.ppermute(
            lax.slice_in_dim(block, block.shape[dim] - width, None, axis=dim), axis, forward
        )
        high = lax.ppermute(lax.slice_in_dim(block, 0, width, axis=dim), axis, backward)
        block = jnp.concatenate([low, block, high], axis=dim)
    return block


def gll_tables():
    degree = 7
    points = np.array(
        [
            -1.0,
            -0.8717401485096066,
            -0.5917001814331423,
            -0.2092992179024789,
            0.2092992179024789,
            0.5917001814331423,
            0.8717401485096066,
            1.0,
        ]
    )
    previous = points * 0.0 + 1.0
    current = points * 1.0
    for order in range(1, degree):
        following = ((2 * order + 1) * points * current - order * previous) / (order + 1)
        previous = current
        current = following
    weights = 2.0 / (degree * (degree + 1) * current**2)
    count = degree + 1
    same = np.array([[1.0 if row == col else 0.0 for col in range(count)] for row in range(count)])
    between = points[:, None] - points[None, :] + same
    deriv = current[:, None] / current[None, :] / between * (1.0 - same)
    deriv[0, 0] = -degree * (degree + 1) / 4.0
    deriv[-1, -1] = degree * (degree + 1) / 4.0
    stiff = deriv.T @ (weights[:, None] * deriv)
    return (jnp.asarray(weights, jnp.float32), jnp.asarray(stiff, jnp.float32))


def spread(metric, which):
    return metric[which][:, :, None, None, None, :]


def element_apply(values_in, metric, weights, stiff):
    top = lax.Precision.HIGHEST
    weight_i = weights[None, None, :, None, None, None]
    weight_j = weights[None, None, None, :, None, None]
    weight_k = weights[None, None, None, None, :, None]
    along_x = jnp.einsum("im,abmjkc->abijkc", stiff, values_in, precision=top)
    along_y = jnp.einsum("jm,abimkc->abijkc", stiff, values_in, precision=top)
    along_z = jnp.einsum("km,abijmc->abijkc", stiff, values_in, precision=top)
    return (
        spread(metric, 0) * weight_j * weight_k * along_x
        + spread(metric, 1) * weight_i * weight_k * along_y
        + spread(metric, 2) * weight_i * weight_j * along_z
        + spread(metric, 3) * weight_i * weight_j * weight_k * values_in
    )


def local_diagonal(metric, weights, stiff):
    stiff_diag = jnp.diagonal(stiff)
    weight_i = weights[None, None, :, None, None, None]
    weight_j = weights[None, None, None, :, None, None]
    weight_k = weights[None, None, None, None, :, None]
    diag_i = stiff_diag[None, None, :, None, None, None]
    diag_j = stiff_diag[None, None, None, :, None, None]
    diag_k = stiff_diag[None, None, None, None, :, None]
    return (
        spread(metric, 0) * diag_i * weight_j * weight_k
        + spread(metric, 1) * weight_i * diag_j * weight_k
        + spread(metric, 2) * weight_i * weight_j * diag_k
        + spread(metric, 3) * weight_i * weight_j * weight_k
    )


def faces(values_in, face_dim):
    last = values_in.shape[face_dim] - 1
    lower = lax.index_in_dim(values_in, 0, face_dim, keepdims=False)
    upper = lax.index_in_dim(values_in, last, face_dim, keepdims=False)
    return (lower, upper)


def combine(values_in, face_dim, elem_dim, lower, upper, before, after):
    total = lower.shape[elem_dim]
    upper_prev = jnp.concatenate(
        [before, lax.slice_in_dim(upper, 0, total - 1, axis=elem_dim)], elem_dim
    )
    lower_next = jnp.concatenate(
        [lax.slice_in_dim(lower, 1, total, axis=elem_dim), after], elem_dim
    )
    middle = lax.slice_in_dim(values_in, 1, values_in.shape[face_dim] - 1, axis=face_dim)
    return jnp.concatenate(
        [
            jnp.expand_dims(lower + upper_prev, face_dim),
            middle,
            jnp.expand_dims(upper + lower_next, face_dim),
        ],
        face_dim,
    )


def assemble(values_in):
    lower, upper = faces(values_in, 3)
    rim_faces = jnp.concatenate([lower, upper], 1)
    padded = padded_2(rim_faces, (("ex", 1),), 1)
    values_in = combine(values_in, 3, 1, lower, upper, padded[:, :1], padded[:, 3:])
    lower, upper = faces(values_in, 4)
    rim_faces = jnp.concatenate([lower, upper], 2)
    padded = padded_2(rim_faces, (("ey", 2),), 1)
    values_in = combine(values_in, 4, 2, lower, upper, padded[:, :, :1], padded[:, :, 3:])
    lower, upper = faces(values_in, 5)
    empty = jnp.zeros_like(upper[..., :1])
    return combine(values_in, 5, 5, lower, upper, empty, empty)


def split3(values):
    first = lax.reduce_precision(values, exponent_bits=8, mantissa_bits=7)
    rest = values - first
    second = lax.reduce_precision(rest, exponent_bits=8, mantissa_bits=7)
    third = rest - second
    return [part.astype(jnp.bfloat16) for part in (first, second, third)]


def one_hot(index, count):
    return (index[:, None] == lax.broadcasted_iota(jnp.int32, (1, count), 1)).astype(jnp.bfloat16)


def gather_flat(values, picks, lanes):
    rows = values.shape[0] // lanes
    table = values.reshape(rows, lanes)
    parts = jnp.concatenate(split3(table), axis=1)
    hit_row = one_hot(picks // lanes, rows)
    picked = jnp.dot(hit_row, parts, preferred_element_type=jnp.float32)
    picked = picked[:, :lanes] + picked[:, lanes : 2 * lanes] + picked[:, 2 * lanes :]
    hit_lane = (picks % lanes)[:, None] == lax.broadcasted_iota(jnp.int32, (1, lanes), 1)
    return jnp.sum(jnp.where(hit_lane, picked, 0.0), axis=1)


def segment_sum(values, ids, bins, lanes):
    rows = bins // lanes
    hit_lane = one_hot(ids % lanes, lanes)
    rhs = jnp.concatenate([hit_lane * part[:, None] for part in split3(values)], axis=1)
    hit_row = one_hot(ids // lanes, rows)
    sums = lax.dot_general(
        hit_row, rhs, (((0,), (0,)), ((), ())), preferred_element_type=jnp.float32
    )
    return (sums[:, :lanes] + sums[:, lanes : 2 * lanes] + sums[:, 2 * lanes :]).reshape(-1)


def strip_totals(partial, strips, strip_size):
    n_ex = lax.axis_size("ex")
    piece = -(-strip_size // n_ex)
    chunks = partial.reshape(2, strips, strip_size)
    if piece * n_ex != strip_size:
        chunks = jnp.pad(chunks, ((0, 0), (0, 0), (0, piece * n_ex - strip_size)))
    chunks = chunks.reshape(2, strips, n_ex, piece).transpose(2, 1, 0, 3)
    chunks = chunks.reshape(n_ex * strips, 2, piece)
    mine = lax.all_to_all(chunks, ("ex", "ey"), 0, 0, tiled=True).sum(0)
    spread_out = jnp.broadcast_to(mine[None], (n_ex, 2, piece))
    whole = lax.all_to_all(spread_out, "ex", 0, 0, tiled=True)
    return whole.transpose(1, 0, 2).reshape(2, n_ex * piece)[:, :strip_size]


def on_device(source, metric, fac_point, fac_strip, fac_shell, fac_area):
    weights, stiff = gll_tables()
    high, low = (2.0, 0.2)
    theta = (high + low) / 2.0
    delta = (high - low) / 2.0
    sigma = theta / delta
    rho_now = 1.0 / sigma
    both = assemble(jnp.stack([source, local_diagonal(metric, weights, stiff)]))
    rhs = both[0]
    pinv = 1.0 / both[1]
    pressure = jnp.zeros_like(source)
    resid = rhs
    update = pinv * resid / theta
    picks = fac_point[0]
    areas = fac_area[0]
    strips = lax.axis_size("ey")
    global_ids = fac_strip[0, :, 0] * SHELL_STRIP + fac_shell[0]
    denom = segment_sum(areas, global_ids, strips * SHELL_STRIP, 256)
    for step in range(SWEEPS):
        pressure = pressure + update
        if step + 2 == SWEEPS:
            early = gather_flat(pressure.reshape(-1), picks, 256)
        applied = element_apply(update, metric, weights, stiff)
        if step + 1 == SWEEPS:
            samples = early + gather_flat(update.reshape(-1), picks, 256)
            numer = segment_sum(areas * samples, global_ids, strips * SHELL_STRIP, 256)
            partial = jnp.stack([numer, denom])
            applied, partial = lax.optimization_barrier((applied, partial))
        assembled = assemble(applied[None])[0]
        if step + 2 == SWEEPS:
            assembled, early = lax.optimization_barrier((assembled, early))
        resid = resid - assembled
        if step + 1 < SWEEPS:
            rho_new = 1.0 / (2.0 * sigma - rho_now)
            update = rho_new * rho_now * update + 2.0 * rho_new / delta * pinv * resid
            rho_now = rho_new
    total = strip_totals(partial, strips, SHELL_STRIP)
    shell_load = total[0] / jnp.maximum(total[1], 1.0)
    return (pressure, resid, shell_load)


def solution(mesh):
    placed = (
        P("ex", "ey", None, None, None, None),
        P(None, "ex", "ey", None),
        P("ex", "ey"),
        P("ex", "ey", None),
        P("ex", "ey"),
        P("ex", "ey"),
    )
    return jax.shard_map(
        on_device,
        mesh=mesh,
        in_specs=placed,
        out_specs=(
            P("ex", "ey", None, None, None, None),
            P("ex", "ey", None, None, None, None),
            P("ey"),
        ),
        check_vma=False,
    )
```

```python
import jax
import jax.numpy as jnp
import numpy as np
from jax import lax
from jax.sharding import PartitionSpec as P

SWEEPS = 4
SHELL_STRIP = 16384


def padded_2(block, sides, width):
    for axis, dim in sides:
        count = lax.axis_size(axis)
        forward = [(i, i + 1) for i in range(count - 1)]
        backward = [(target, source) for source, target in forward]
        low = lax.ppermute(
            lax.slice_in_dim(block, block.shape[dim] - width, None, axis=dim), axis, forward
        )
        high = lax.ppermute(lax.slice_in_dim(block, 0, width, axis=dim), axis, backward)
        block = jnp.concatenate([low, block, high], axis=dim)
    return block


def gll_tables():
    degree = 7
    points = np.array(
        [
            -1.0,
            -0.8717401485096066,
            -0.5917001814331423,
            -0.2092992179024789,
            0.2092992179024789,
            0.5917001814331423,
            0.8717401485096066,
            1.0,
        ]
    )
    previous = points * 0.0 + 1.0
    current = points * 1.0
    for order in range(1, degree):
        following = ((2 * order + 1) * points * current - order * previous) / (order + 1)
        previous = current
        current = following
    weights = 2.0 / (degree * (degree + 1) * current**2)
    count = degree + 1
    same = np.array([[1.0 if row == col else 0.0 for col in range(count)] for row in range(count)])
    between = points[:, None] - points[None, :] + same
    deriv = current[:, None] / current[None, :] / between * (1.0 - same)
    deriv[0, 0] = -degree * (degree + 1) / 4.0
    deriv[-1, -1] = degree * (degree + 1) / 4.0
    stiff = deriv.T @ (weights[:, None] * deriv)
    return (jnp.asarray(weights, jnp.float32), jnp.asarray(stiff, jnp.float32))


def spread(metric, which):
    return metric[which][:, :, None, None, None, :]


def element_apply(values_in, metric, weights, stiff):
    top = lax.Precision.HIGHEST
    weight_i = weights[None, None, :, None, None, None]
    weight_j = weights[None, None, None, :, None, None]
    weight_k = weights[None, None, None, None, :, None]
    along_x = jnp.einsum("im,abmjkc->abijkc", stiff, values_in, precision=top)
    along_y = jnp.einsum("jm,abimkc->abijkc", stiff, values_in, precision=top)
    along_z = jnp.einsum("km,abijmc->abijkc", stiff, values_in, precision=top)
    return (
        spread(metric, 0) * weight_j * weight_k * along_x
        + spread(metric, 1) * weight_i * weight_k * along_y
        + spread(metric, 2) * weight_i * weight_j * along_z
        + spread(metric, 3) * weight_i * weight_j * weight_k * values_in
    )


def local_diagonal(metric, weights, stiff):
    stiff_diag = jnp.diagonal(stiff)
    weight_i = weights[None, None, :, None, None, None]
    weight_j = weights[None, None, None, :, None, None]
    weight_k = weights[None, None, None, None, :, None]
    diag_i = stiff_diag[None, None, :, None, None, None]
    diag_j = stiff_diag[None, None, None, :, None, None]
    diag_k = stiff_diag[None, None, None, None, :, None]
    return (
        spread(metric, 0) * diag_i * weight_j * weight_k
        + spread(metric, 1) * weight_i * diag_j * weight_k
        + spread(metric, 2) * weight_i * weight_j * diag_k
        + spread(metric, 3) * weight_i * weight_j * weight_k
    )


def faces(values_in, face_dim):
    last = values_in.shape[face_dim] - 1
    lower = lax.index_in_dim(values_in, 0, face_dim, keepdims=False)
    upper = lax.index_in_dim(values_in, last, face_dim, keepdims=False)
    return (lower, upper)


def combine(values_in, face_dim, elem_dim, lower, upper, before, after):
    total = lower.shape[elem_dim]
    upper_prev = jnp.concatenate(
        [before, lax.slice_in_dim(upper, 0, total - 1, axis=elem_dim)], elem_dim
    )
    lower_next = jnp.concatenate(
        [lax.slice_in_dim(lower, 1, total, axis=elem_dim), after], elem_dim
    )
    middle = lax.slice_in_dim(values_in, 1, values_in.shape[face_dim] - 1, axis=face_dim)
    return jnp.concatenate(
        [
            jnp.expand_dims(lower + upper_prev, face_dim),
            middle,
            jnp.expand_dims(upper + lower_next, face_dim),
        ],
        face_dim,
    )


def assemble(values_in):
    lower, upper = faces(values_in, 3)
    rim_faces = jnp.concatenate([lower, upper], 1)
    padded = padded_2(rim_faces, (("ex", 1),), 1)
    values_in = combine(values_in, 3, 1, lower, upper, padded[:, :1], padded[:, 3:])
    lower, upper = faces(values_in, 4)
    rim_faces = jnp.concatenate([lower, upper], 2)
    padded = padded_2(rim_faces, (("ey", 2),), 1)
    values_in = combine(values_in, 4, 2, lower, upper, padded[:, :, :1], padded[:, :, 3:])
    lower, upper = faces(values_in, 5)
    empty = jnp.zeros_like(upper[..., :1])
    return combine(values_in, 5, 5, lower, upper, empty, empty)


def split3(values):
    first = lax.reduce_precision(values, exponent_bits=8, mantissa_bits=7)
    rest = values - first
    second = lax.reduce_precision(rest, exponent_bits=8, mantissa_bits=7)
    third = rest - second
    return [part.astype(jnp.bfloat16) for part in (first, second, third)]


def one_hot(index, count):
    return (index[:, None] == lax.broadcasted_iota(jnp.int32, (1, count), 1)).astype(jnp.bfloat16)


def gather_flat(values, picks, lanes):
    rows = values.shape[0] // lanes
    table = values.reshape(rows, lanes)
    parts = jnp.concatenate(split3(table), axis=1)
    hit_row = one_hot(picks // lanes, rows)
    picked = jnp.dot(hit_row, parts, preferred_element_type=jnp.float32)
    picked = picked[:, :lanes] + picked[:, lanes : 2 * lanes] + picked[:, 2 * lanes :]
    hit_lane = (picks % lanes)[:, None] == lax.broadcasted_iota(jnp.int32, (1, lanes), 1)
    return jnp.sum(jnp.where(hit_lane, picked, 0.0), axis=1)


def segment_sum(values, ids, bins, lanes):
    rows = bins // lanes
    hit_lane = one_hot(ids % lanes, lanes)
    rhs = jnp.concatenate([hit_lane * part[:, None] for part in split3(values)], axis=1)
    hit_row = one_hot(ids // lanes, rows)
    sums = lax.dot_general(
        hit_row, rhs, (((0,), (0,)), ((), ())), preferred_element_type=jnp.float32
    )
    return (sums[:, :lanes] + sums[:, lanes : 2 * lanes] + sums[:, 2 * lanes :]).reshape(-1)


def strip_totals(partial, strips, strip_size):
    n_ex = lax.axis_size("ex")
    piece = -(-strip_size // n_ex)
    chunks = partial.reshape(2, strips, strip_size)
    if piece * n_ex != strip_size:
        chunks = jnp.pad(chunks, ((0, 0), (0, 0), (0, piece * n_ex - strip_size)))
    chunks = chunks.reshape(2, strips, n_ex, piece).transpose(2, 1, 0, 3)
    chunks = chunks.reshape(n_ex * strips, 2, piece)
    mine = lax.all_to_all(chunks, ("ex", "ey"), 0, 0, tiled=True).sum(0)
    spread_out = jnp.broadcast_to(mine[None], (n_ex, 2, piece))
    whole = lax.all_to_all(spread_out, "ex", 0, 0, tiled=True)
    return whole.transpose(1, 0, 2).reshape(2, n_ex * piece)[:, :strip_size]


def on_device(source, metric, fac_point, fac_strip, fac_shell, fac_area):
    weights, stiff = gll_tables()
    high, low = (2.0, 0.2)
    theta = (high + low) / 2.0
    delta = (high - low) / 2.0
    sigma = theta / delta
    rho_now = 1.0 / sigma
    both = assemble(jnp.stack([source, local_diagonal(metric, weights, stiff)]))
    rhs = both[0]
    pinv = 1.0 / both[1]
    pressure = jnp.zeros_like(source)
    resid = rhs
    update = pinv * resid / theta
    picks = fac_point[0]
    areas = fac_area[0]
    strips = lax.axis_size("ey")
    global_ids = fac_strip[0, :, 0] * SHELL_STRIP + fac_shell[0]
    denom = segment_sum(areas, global_ids, strips * SHELL_STRIP, 256)
    for step in range(SWEEPS):
        pressure = pressure + update
        if step + 2 == SWEEPS:
            early = gather_flat(pressure.reshape(-1), picks, 256)
        applied = element_apply(update, metric, weights, stiff)
        if step + 1 == SWEEPS:
            samples = early + gather_flat(update.reshape(-1), picks, 256)
            numer = segment_sum(areas * samples, global_ids, strips * SHELL_STRIP, 256)
            partial = jnp.stack([numer, denom])
        assembled = assemble(applied[None])[0]
        if step + 2 == SWEEPS:
            assembled, early = lax.optimization_barrier((assembled, early))
        if step == 0:
            assembled, denom = lax.optimization_barrier((assembled, denom))
        resid = resid - assembled
        if step + 1 < SWEEPS:
            rho_new = 1.0 / (2.0 * sigma - rho_now)
            update = rho_new * rho_now * update + 2.0 * rho_new / delta * pinv * resid
            rho_now = rho_new
    total = strip_totals(partial, strips, SHELL_STRIP)
    shell_load = total[0] / jnp.maximum(total[1], 1.0)
    return (pressure, resid, shell_load)


def solution(mesh):
    placed = (
        P("ex", "ey", None, None, None, None),
        P(None, "ex", "ey", None),
        P("ex", "ey"),
        P("ex", "ey", None),
        P("ex", "ey"),
        P("ex", "ey"),
    )
    return jax.shard_map(
        on_device,
        mesh=mesh,
        in_specs=placed,
        out_specs=(
            P("ex", "ey", None, None, None, None),
            P("ex", "ey", None, None, None, None),
            P("ey"),
        ),
        check_vma=False,
    )
```

```python
import jax
import jax.numpy as jnp
import numpy as np
from jax import lax
from jax.sharding import PartitionSpec as P

SWEEPS = 4
SHELL_STRIP = 16384


def padded_2(block, sides, width):
    for axis, dim in sides:
        count = lax.axis_size(axis)
        forward = [(i, i + 1) for i in range(count - 1)]
        backward = [(target, source) for source, target in forward]
        low = lax.ppermute(
            lax.slice_in_dim(block, block.shape[dim] - width, None, axis=dim), axis, forward
        )
        high = lax.ppermute(lax.slice_in_dim(block, 0, width, axis=dim), axis, backward)
        block = jnp.concatenate([low, block, high], axis=dim)
    return block


def gll_tables():
    degree = 7
    points = np.array(
        [
            -1.0,
            -0.8717401485096066,
            -0.5917001814331423,
            -0.2092992179024789,
            0.2092992179024789,
            0.5917001814331423,
            0.8717401485096066,
            1.0,
        ]
    )
    previous = points * 0.0 + 1.0
    current = points * 1.0
    for order in range(1, degree):
        following = ((2 * order + 1) * points * current - order * previous) / (order + 1)
        previous = current
        current = following
    weights = 2.0 / (degree * (degree + 1) * current**2)
    count = degree + 1
    same = np.array([[1.0 if row == col else 0.0 for col in range(count)] for row in range(count)])
    between = points[:, None] - points[None, :] + same
    deriv = current[:, None] / current[None, :] / between * (1.0 - same)
    deriv[0, 0] = -degree * (degree + 1) / 4.0
    deriv[-1, -1] = degree * (degree + 1) / 4.0
    stiff = deriv.T @ (weights[:, None] * deriv)
    return (jnp.asarray(weights, jnp.float32), jnp.asarray(stiff, jnp.float32))


def spread(metric, which):
    return metric[which][:, :, None, None, None, :]


def element_apply(values_in, metric, weights, stiff):
    top = lax.Precision.HIGHEST
    weight_i = weights[None, None, :, None, None, None]
    weight_j = weights[None, None, None, :, None, None]
    weight_k = weights[None, None, None, None, :, None]
    along_x = jnp.einsum("im,abmjkc->abijkc", stiff, values_in, precision=top)
    along_y = jnp.einsum("jm,abimkc->abijkc", stiff, values_in, precision=top)
    along_z = jnp.einsum("km,abijmc->abijkc", stiff, values_in, precision=top)
    return (
        spread(metric, 0) * weight_j * weight_k * along_x
        + spread(metric, 1) * weight_i * weight_k * along_y
        + spread(metric, 2) * weight_i * weight_j * along_z
        + spread(metric, 3) * weight_i * weight_j * weight_k * values_in
    )


def local_diagonal(metric, weights, stiff):
    stiff_diag = jnp.diagonal(stiff)
    weight_i = weights[None, None, :, None, None, None]
    weight_j = weights[None, None, None, :, None, None]
    weight_k = weights[None, None, None, None, :, None]
    diag_i = stiff_diag[None, None, :, None, None, None]
    diag_j = stiff_diag[None, None, None, :, None, None]
    diag_k = stiff_diag[None, None, None, None, :, None]
    return (
        spread(metric, 0) * diag_i * weight_j * weight_k
        + spread(metric, 1) * weight_i * diag_j * weight_k
        + spread(metric, 2) * weight_i * weight_j * diag_k
        + spread(metric, 3) * weight_i * weight_j * weight_k
    )


def faces(values_in, face_dim):
    last = values_in.shape[face_dim] - 1
    lower = lax.index_in_dim(values_in, 0, face_dim, keepdims=False)
    upper = lax.index_in_dim(values_in, last, face_dim, keepdims=False)
    return (lower, upper)


def combine(values_in, face_dim, elem_dim, lower, upper, before, after):
    total = lower.shape[elem_dim]
    upper_prev = jnp.concatenate(
        [before, lax.slice_in_dim(upper, 0, total - 1, axis=elem_dim)], elem_dim
    )
    lower_next = jnp.concatenate(
        [lax.slice_in_dim(lower, 1, total, axis=elem_dim), after], elem_dim
    )
    middle = lax.slice_in_dim(values_in, 1, values_in.shape[face_dim] - 1, axis=face_dim)
    return jnp.concatenate(
        [
            jnp.expand_dims(lower + upper_prev, face_dim),
            middle,
            jnp.expand_dims(upper + lower_next, face_dim),
        ],
        face_dim,
    )


def assemble(values_in):
    lower, upper = faces(values_in, 3)
    rim_faces = jnp.concatenate([lower, upper], 1)
    padded = padded_2(rim_faces, (("ex", 1),), 1)
    values_in = combine(values_in, 3, 1, lower, upper, padded[:, :1], padded[:, 3:])
    lower, upper = faces(values_in, 4)
    rim_faces = jnp.concatenate([lower, upper], 2)
    padded = padded_2(rim_faces, (("ey", 2),), 1)
    values_in = combine(values_in, 4, 2, lower, upper, padded[:, :, :1], padded[:, :, 3:])
    lower, upper = faces(values_in, 5)
    empty = jnp.zeros_like(upper[..., :1])
    return combine(values_in, 5, 5, lower, upper, empty, empty)


def split3(values):
    first = lax.reduce_precision(values, exponent_bits=8, mantissa_bits=7)
    rest = values - first
    second = lax.reduce_precision(rest, exponent_bits=8, mantissa_bits=7)
    third = rest - second
    return [part.astype(jnp.bfloat16) for part in (first, second, third)]


def one_hot(index, count):
    return (index[:, None] == lax.broadcasted_iota(jnp.int32, (1, count), 1)).astype(jnp.bfloat16)


def gather_flat(values, picks, lanes):
    rows = values.shape[0] // lanes
    table = values.reshape(rows, lanes)
    parts = jnp.concatenate(split3(table), axis=1)
    hit_row = one_hot(picks // lanes, rows)
    picked = jnp.dot(hit_row, parts, preferred_element_type=jnp.float32)
    picked = picked[:, :lanes] + picked[:, lanes : 2 * lanes] + picked[:, 2 * lanes :]
    hit_lane = (picks % lanes)[:, None] == lax.broadcasted_iota(jnp.int32, (1, lanes), 1)
    return jnp.sum(jnp.where(hit_lane, picked, 0.0), axis=1)


def segment_sum(values, ids, bins, lanes):
    rows = bins // lanes
    hit_lane = one_hot(ids % lanes, lanes)
    rhs = jnp.concatenate([hit_lane * part[:, None] for part in split3(values)], axis=1)
    hit_row = one_hot(ids // lanes, rows)
    sums = lax.dot_general(
        hit_row, rhs, (((0,), (0,)), ((), ())), preferred_element_type=jnp.float32
    )
    return (sums[:, :lanes] + sums[:, lanes : 2 * lanes] + sums[:, 2 * lanes :]).reshape(-1)


def strip_totals(partial, strips, strip_size):
    n_ex = lax.axis_size("ex")
    piece = -(-strip_size // n_ex)
    count = partial.shape[0]
    chunks = partial.reshape(count, strips, strip_size)
    if piece * n_ex != strip_size:
        chunks = jnp.pad(chunks, ((0, 0), (0, 0), (0, piece * n_ex - strip_size)))
    chunks = chunks.reshape(count, strips, n_ex, piece).transpose(2, 1, 0, 3)
    chunks = chunks.reshape(n_ex * strips, count, piece)
    mine = lax.all_to_all(chunks, ("ex", "ey"), 0, 0, tiled=True).sum(0)
    spread_out = jnp.broadcast_to(mine[None], (n_ex, count, piece))
    whole = lax.all_to_all(spread_out, "ex", 0, 0, tiled=True)
    return whole.transpose(1, 0, 2).reshape(count, n_ex * piece)[:, :strip_size]


def on_device(source, metric, fac_point, fac_strip, fac_shell, fac_area):
    weights, stiff = gll_tables()
    high, low = (2.0, 0.2)
    theta = (high + low) / 2.0
    delta = (high - low) / 2.0
    sigma = theta / delta
    rho_now = 1.0 / sigma
    both = assemble(jnp.stack([source, local_diagonal(metric, weights, stiff)]))
    rhs = both[0]
    pinv = 1.0 / both[1]
    pressure = jnp.zeros_like(source)
    resid = rhs
    update = pinv * resid / theta
    picks = fac_point[0]
    areas = fac_area[0]
    strips = lax.axis_size("ey")
    global_ids = fac_strip[0, :, 0] * SHELL_STRIP + fac_shell[0]
    denom = segment_sum(areas, global_ids, strips * SHELL_STRIP, 256)
    for step in range(SWEEPS):
        pressure = pressure + update
        if step + 2 == SWEEPS:
            early = gather_flat(pressure.reshape(-1), picks, 256)
        applied = element_apply(update, metric, weights, stiff)
        if step + 1 == SWEEPS:
            samples = early + gather_flat(update.reshape(-1), picks, 256)
            numer = segment_sum(areas * samples, global_ids, strips * SHELL_STRIP, 256)
        assembled = assemble(applied[None])[0]
        if step + 2 == SWEEPS:
            assembled, early = lax.optimization_barrier((assembled, early))
        if step == 0:
            assembled, denom = lax.optimization_barrier((assembled, denom))
            denom_total = strip_totals(denom[None], strips, SHELL_STRIP)[0]
        resid = resid - assembled
        if step + 1 < SWEEPS:
            rho_new = 1.0 / (2.0 * sigma - rho_now)
            update = rho_new * rho_now * update + 2.0 * rho_new / delta * pinv * resid
            rho_now = rho_new
    numer_total = strip_totals(numer[None], strips, SHELL_STRIP)[0]
    shell_load = numer_total / jnp.maximum(denom_total, 1.0)
    return (pressure, resid, shell_load)


def solution(mesh):
    placed = (
        P("ex", "ey", None, None, None, None),
        P(None, "ex", "ey", None),
        P("ex", "ey"),
        P("ex", "ey", None),
        P("ex", "ey"),
        P("ex", "ey"),
    )
    return jax.shard_map(
        on_device,
        mesh=mesh,
        in_specs=placed,
        out_specs=(
            P("ex", "ey", None, None, None, None),
            P("ex", "ey", None, None, None, None),
            P("ey"),
        ),
        check_vma=False,
    )
```

```python
import jax
import jax.numpy as jnp
import numpy as np
from jax import lax
from jax.sharding import PartitionSpec as P

SWEEPS = 4
SHELL_STRIP = 16384


def padded_2(block, sides, width):
    for axis, dim in sides:
        count = lax.axis_size(axis)
        forward = [(i, i + 1) for i in range(count - 1)]
        backward = [(target, source) for source, target in forward]
        low = lax.ppermute(
            lax.slice_in_dim(block, block.shape[dim] - width, None, axis=dim), axis, forward
        )
        high = lax.ppermute(lax.slice_in_dim(block, 0, width, axis=dim), axis, backward)
        block = jnp.concatenate([low, block, high], axis=dim)
    return block


def gll_tables():
    degree = 7
    points = np.array(
        [
            -1.0,
            -0.8717401485096066,
            -0.5917001814331423,
            -0.2092992179024789,
            0.2092992179024789,
            0.5917001814331423,
            0.8717401485096066,
            1.0,
        ]
    )
    previous = points * 0.0 + 1.0
    current = points * 1.0
    for order in range(1, degree):
        following = ((2 * order + 1) * points * current - order * previous) / (order + 1)
        previous = current
        current = following
    weights = 2.0 / (degree * (degree + 1) * current**2)
    count = degree + 1
    same = np.array([[1.0 if row == col else 0.0 for col in range(count)] for row in range(count)])
    between = points[:, None] - points[None, :] + same
    deriv = current[:, None] / current[None, :] / between * (1.0 - same)
    deriv[0, 0] = -degree * (degree + 1) / 4.0
    deriv[-1, -1] = degree * (degree + 1) / 4.0
    stiff = deriv.T @ (weights[:, None] * deriv)
    return (np.asarray(weights, np.float32), np.asarray(stiff, np.float32))


def spread(metric, which):
    return metric[which][:, :, None, None, None, :]


def element_apply(values_in, metric, weights, stiff):
    top = lax.Precision.HIGHEST
    weight_i = weights[None, None, :, None, None, None]
    weight_j = weights[None, None, None, :, None, None]
    weight_k = weights[None, None, None, None, :, None]
    along_x = jnp.einsum("im,abmjkc->abijkc", stiff, values_in, precision=top)
    along_y = jnp.einsum("jm,abimkc->abijkc", stiff, values_in, precision=top)
    along_z = jnp.einsum("km,abijmc->abijkc", stiff, values_in, precision=top)
    return (
        spread(metric, 0) * weight_j * weight_k * along_x
        + spread(metric, 1) * weight_i * weight_k * along_y
        + spread(metric, 2) * weight_i * weight_j * along_z
        + spread(metric, 3) * weight_i * weight_j * weight_k * values_in
    )


def local_diagonal(metric, weights, stiff):
    stiff_diag = np.diagonal(stiff)
    weight_i = weights[None, None, :, None, None, None]
    weight_j = weights[None, None, None, :, None, None]
    weight_k = weights[None, None, None, None, :, None]
    diag_i = stiff_diag[None, None, :, None, None, None]
    diag_j = stiff_diag[None, None, None, :, None, None]
    diag_k = stiff_diag[None, None, None, None, :, None]
    return (
        spread(metric, 0) * diag_i * weight_j * weight_k
        + spread(metric, 1) * weight_i * diag_j * weight_k
        + spread(metric, 2) * weight_i * weight_j * diag_k
        + spread(metric, 3) * weight_i * weight_j * weight_k
    )


def faces(values_in, face_dim):
    last = values_in.shape[face_dim] - 1
    lower = lax.index_in_dim(values_in, 0, face_dim, keepdims=False)
    upper = lax.index_in_dim(values_in, last, face_dim, keepdims=False)
    return (lower, upper)


def combine(values_in, face_dim, elem_dim, lower, upper, before, after):
    total = lower.shape[elem_dim]
    upper_prev = jnp.concatenate(
        [before, lax.slice_in_dim(upper, 0, total - 1, axis=elem_dim)], elem_dim
    )
    lower_next = jnp.concatenate(
        [lax.slice_in_dim(lower, 1, total, axis=elem_dim), after], elem_dim
    )
    middle = lax.slice_in_dim(values_in, 1, values_in.shape[face_dim] - 1, axis=face_dim)
    return jnp.concatenate(
        [
            jnp.expand_dims(lower + upper_prev, face_dim),
            middle,
            jnp.expand_dims(upper + lower_next, face_dim),
        ],
        face_dim,
    )


def assemble(values_in, ride=None):
    lower, upper = faces(values_in, 3)
    rim_faces = jnp.concatenate([lower, upper], 1)
    padded = padded_2(rim_faces, (("ex", 1),), 1)
    if ride is not None:
        padded, ride = lax.optimization_barrier((padded, ride))
    values_in = combine(values_in, 3, 1, lower, upper, padded[:, :1], padded[:, 3:])
    lower, upper = faces(values_in, 4)
    rim_faces = jnp.concatenate([lower, upper], 2)
    padded = padded_2(rim_faces, (("ey", 2),), 1)
    values_in = combine(values_in, 4, 2, lower, upper, padded[:, :, :1], padded[:, :, 3:])
    lower, upper = faces(values_in, 5)
    empty = jnp.zeros_like(upper[..., :1])
    return combine(values_in, 5, 5, lower, upper, empty, empty), ride


def split3(values):
    first = lax.reduce_precision(values, exponent_bits=8, mantissa_bits=7)
    rest = values - first
    second = lax.reduce_precision(rest, exponent_bits=8, mantissa_bits=7)
    third = rest - second
    return [part.astype(jnp.bfloat16) for part in (first, second, third)]


def one_hot(index, count):
    return (index[:, None] == lax.broadcasted_iota(jnp.int32, (1, count), 1)).astype(jnp.bfloat16)


def gather_flat(values, picks, lanes):
    rows = values.shape[0] // lanes
    table = values.reshape(rows, lanes)
    parts = jnp.concatenate(split3(table), axis=1)
    hit_row = one_hot(picks // lanes, rows)
    picked = jnp.dot(hit_row, parts, preferred_element_type=jnp.float32)
    picked = picked[:, :lanes] + picked[:, lanes : 2 * lanes] + picked[:, 2 * lanes :]
    hit_lane = (picks % lanes)[:, None] == lax.broadcasted_iota(jnp.int32, (1, lanes), 1)
    return jnp.sum(jnp.where(hit_lane, picked, 0.0), axis=1)


def segment_sum(values, ids, bins, lanes):
    rows = bins // lanes
    hit_lane = one_hot(ids % lanes, lanes)
    rhs = jnp.concatenate([hit_lane * part[:, None] for part in split3(values)], axis=1)
    hit_row = one_hot(ids // lanes, rows)
    sums = lax.dot_general(
        hit_row, rhs, (((0,), (0,)), ((), ())), preferred_element_type=jnp.float32
    )
    return (sums[:, :lanes] + sums[:, lanes : 2 * lanes] + sums[:, 2 * lanes :]).reshape(-1)


def strip_reduce(partial, strips, strip_size):
    n_ex = lax.axis_size("ex")
    piece = -(-strip_size // n_ex)
    chunks = partial.reshape(2, strips, strip_size)
    if piece * n_ex != strip_size:
        chunks = jnp.pad(chunks, ((0, 0), (0, 0), (0, piece * n_ex - strip_size)))
    chunks = chunks.reshape(2, strips, n_ex, piece).transpose(2, 1, 0, 3)
    chunks = chunks.reshape(n_ex * strips, 2, piece)
    return lax.all_to_all(chunks, ("ex", "ey"), 0, 0, tiled=True).sum(0)


def strip_gather(mine, strip_size):
    n_ex = lax.axis_size("ex")
    count, piece = mine.shape
    spread_out = jnp.broadcast_to(mine[None], (n_ex, 2, piece))
    whole = lax.all_to_all(spread_out, "ex", 0, 0, tiled=True)
    return whole.transpose(1, 0, 2).reshape(2, n_ex * piece)[:, :strip_size]


def on_device(source, metric, fac_point, fac_strip, fac_shell, fac_area):
    weights, stiff = gll_tables()
    high, low = (2.0, 0.2)
    theta = (high + low) / 2.0
    delta = (high - low) / 2.0
    sigma = theta / delta
    rho_now = 1.0 / sigma
    both, _ = assemble(jnp.stack([source, local_diagonal(metric, weights, stiff)]))
    rhs = both[0]
    pinv = 1.0 / both[1]
    pressure = jnp.zeros_like(source)
    resid = rhs
    update = pinv * resid / theta
    picks = fac_point[0]
    areas = fac_area[0]
    strips = lax.axis_size("ey")
    global_ids = fac_strip[0, :, 0] * SHELL_STRIP + fac_shell[0]
    denom = segment_sum(areas, global_ids, strips * SHELL_STRIP, 256)
    for step in range(SWEEPS):
        pressure = pressure + update
        if step + 2 == SWEEPS:
            early = gather_flat(pressure.reshape(-1), picks, 256)
        applied = element_apply(update, metric, weights, stiff)
        if step + 1 == SWEEPS:
            samples = early + gather_flat(update.reshape(-1), picks, 256)
            numer = segment_sum(areas * samples, global_ids, strips * SHELL_STRIP, 256)
            partial = jnp.stack([numer, denom])
            assembled, mine = assemble(applied[None], strip_reduce(partial, strips, SHELL_STRIP))
        else:
            assembled, _ = assemble(applied[None])
        assembled = assembled[0]
        if step + 2 == SWEEPS:
            assembled, early = lax.optimization_barrier((assembled, early))
        if step == 0:
            assembled, denom = lax.optimization_barrier((assembled, denom))
        resid = resid - assembled
        if step + 1 < SWEEPS:
            rho_new = 1.0 / (2.0 * sigma - rho_now)
            update = rho_new * rho_now * update + 2.0 * rho_new / delta * pinv * resid
            rho_now = rho_new
    total = strip_gather(mine, SHELL_STRIP)
    shell_load = total[0] / jnp.maximum(total[1], 1.0)
    return (pressure, resid, shell_load)


def solution(mesh):
    placed = (
        P("ex", "ey", None, None, None, None),
        P(None, "ex", "ey", None),
        P("ex", "ey"),
        P("ex", "ey", None),
        P("ex", "ey"),
        P("ex", "ey"),
    )
    return jax.shard_map(
        on_device,
        mesh=mesh,
        in_specs=placed,
        out_specs=(
            P("ex", "ey", None, None, None, None),
            P("ex", "ey", None, None, None, None),
            P("ey"),
        ),
        check_vma=False,
    )
```

```python
import jax
import jax.numpy as jnp
import numpy as np
from jax import lax
from jax.sharding import PartitionSpec as P

SWEEPS = 4
SHELL_STRIP = 16384


def padded_2(block, sides, width):
    for axis, dim in sides:
        count = lax.axis_size(axis)
        forward = [(i, i + 1) for i in range(count - 1)]
        backward = [(target, source) for source, target in forward]
        low = lax.ppermute(
            lax.slice_in_dim(block, block.shape[dim] - width, None, axis=dim), axis, forward
        )
        high = lax.ppermute(lax.slice_in_dim(block, 0, width, axis=dim), axis, backward)
        block = jnp.concatenate([low, block, high], axis=dim)
    return block


def padded_swap(block, axis, dim):
    count = lax.axis_size(axis)
    here = lax.axis_index(axis)
    lower = lax.slice_in_dim(block, 0, 1, axis=dim)
    upper = lax.slice_in_dim(block, block.shape[dim] - 1, None, axis=dim)
    slots = lax.broadcasted_iota(jnp.int32, (count,) + (1,) * lower.ndim, 0)
    zero = jnp.zeros_like(upper)
    outgoing = jnp.where(slots == here + 1, upper[None], jnp.where(slots == here - 1, lower[None], zero[None]))
    incoming = lax.all_to_all(outgoing, axis, 0, 0, tiled=True)
    low = jnp.sum(jnp.where(slots == here - 1, incoming, 0.0), axis=0)
    high = jnp.sum(jnp.where(slots == here + 1, incoming, 0.0), axis=0)
    return jnp.concatenate([low, block, high], axis=dim)


def gll_tables():
    degree = 7
    points = np.array(
        [
            -1.0,
            -0.8717401485096066,
            -0.5917001814331423,
            -0.2092992179024789,
            0.2092992179024789,
            0.5917001814331423,
            0.8717401485096066,
            1.0,
        ]
    )
    previous = points * 0.0 + 1.0
    current = points * 1.0
    for order in range(1, degree):
        following = ((2 * order + 1) * points * current - order * previous) / (order + 1)
        previous = current
        current = following
    weights = 2.0 / (degree * (degree + 1) * current**2)
    count = degree + 1
    same = np.array([[1.0 if row == col else 0.0 for col in range(count)] for row in range(count)])
    between = points[:, None] - points[None, :] + same
    deriv = current[:, None] / current[None, :] / between * (1.0 - same)
    deriv[0, 0] = -degree * (degree + 1) / 4.0
    deriv[-1, -1] = degree * (degree + 1) / 4.0
    stiff = deriv.T @ (weights[:, None] * deriv)
    return (np.asarray(weights, np.float32), np.asarray(stiff, np.float32))


def spread(metric, which):
    return metric[which][:, :, None, None, None, :]


def element_apply(values_in, metric, weights, stiff):
    top = lax.Precision.HIGHEST
    weight_i = weights[None, None, :, None, None, None]
    weight_j = weights[None, None, None, :, None, None]
    weight_k = weights[None, None, None, None, :, None]
    along_x = jnp.einsum("im,abmjkc->abijkc", stiff, values_in, precision=top)
    along_y = jnp.einsum("jm,abimkc->abijkc", stiff, values_in, precision=top)
    along_z = jnp.einsum("km,abijmc->abijkc", stiff, values_in, precision=top)
    return (
        spread(metric, 0) * weight_j * weight_k * along_x
        + spread(metric, 1) * weight_i * weight_k * along_y
        + spread(metric, 2) * weight_i * weight_j * along_z
        + spread(metric, 3) * weight_i * weight_j * weight_k * values_in
    )


def local_diagonal(metric, weights, stiff):
    stiff_diag = np.diagonal(stiff)
    weight_i = weights[None, None, :, None, None, None]
    weight_j = weights[None, None, None, :, None, None]
    weight_k = weights[None, None, None, None, :, None]
    diag_i = stiff_diag[None, None, :, None, None, None]
    diag_j = stiff_diag[None, None, None, :, None, None]
    diag_k = stiff_diag[None, None, None, None, :, None]
    return (
        spread(metric, 0) * diag_i * weight_j * weight_k
        + spread(metric, 1) * weight_i * diag_j * weight_k
        + spread(metric, 2) * weight_i * weight_j * diag_k
        + spread(metric, 3) * weight_i * weight_j * weight_k
    )


def faces(values_in, face_dim):
    last = values_in.shape[face_dim] - 1
    lower = lax.index_in_dim(values_in, 0, face_dim, keepdims=False)
    upper = lax.index_in_dim(values_in, last, face_dim, keepdims=False)
    return (lower, upper)


def combine(values_in, face_dim, elem_dim, lower, upper, before, after):
    total = lower.shape[elem_dim]
    upper_prev = jnp.concatenate(
        [before, lax.slice_in_dim(upper, 0, total - 1, axis=elem_dim)], elem_dim
    )
    lower_next = jnp.concatenate(
        [lax.slice_in_dim(lower, 1, total, axis=elem_dim), after], elem_dim
    )
    middle = lax.slice_in_dim(values_in, 1, values_in.shape[face_dim] - 1, axis=face_dim)
    return jnp.concatenate(
        [
            jnp.expand_dims(lower + upper_prev, face_dim),
            middle,
            jnp.expand_dims(upper + lower_next, face_dim),
        ],
        face_dim,
    )


def assemble(values_in, ride=None):
    lower, upper = faces(values_in, 3)
    rim_faces = jnp.concatenate([lower, upper], 1)
    padded = padded_2(rim_faces, (("ex", 1),), 1)
    if ride is not None:
        padded, ride = lax.optimization_barrier((padded, ride))
    values_in = combine(values_in, 3, 1, lower, upper, padded[:, :1], padded[:, 3:])
    lower, upper = faces(values_in, 4)
    rim_faces = jnp.concatenate([lower, upper], 2)
    padded = padded_swap(rim_faces, "ey", 2)
    values_in = combine(values_in, 4, 2, lower, upper, padded[:, :, :1], padded[:, :, 3:])
    lower, upper = faces(values_in, 5)
    empty = jnp.zeros_like(upper[..., :1])
    return combine(values_in, 5, 5, lower, upper, empty, empty), ride


def split3(values):
    first = lax.reduce_precision(values, exponent_bits=8, mantissa_bits=7)
    rest = values - first
    second = lax.reduce_precision(rest, exponent_bits=8, mantissa_bits=7)
    third = rest - second
    return [part.astype(jnp.bfloat16) for part in (first, second, third)]


def one_hot(index, count):
    return (index[:, None] == lax.broadcasted_iota(jnp.int32, (1, count), 1)).astype(jnp.bfloat16)


def gather_flat(values, picks, lanes):
    rows = values.shape[0] // lanes
    table = values.reshape(rows, lanes)
    parts = jnp.concatenate(split3(table), axis=1)
    hit_row = one_hot(picks // lanes, rows)
    picked = jnp.dot(hit_row, parts, preferred_element_type=jnp.float32)
    picked = picked[:, :lanes] + picked[:, lanes : 2 * lanes] + picked[:, 2 * lanes :]
    hit_lane = (picks % lanes)[:, None] == lax.broadcasted_iota(jnp.int32, (1, lanes), 1)
    return jnp.sum(jnp.where(hit_lane, picked, 0.0), axis=1)


def segment_sum(values, ids, bins, lanes):
    rows = bins // lanes
    hit_lane = one_hot(ids % lanes, lanes)
    rhs = jnp.concatenate([hit_lane * part[:, None] for part in split3(values)], axis=1)
    hit_row = one_hot(ids // lanes, rows)
    sums = lax.dot_general(
        hit_row, rhs, (((0,), (0,)), ((), ())), preferred_element_type=jnp.float32
    )
    return (sums[:, :lanes] + sums[:, lanes : 2 * lanes] + sums[:, 2 * lanes :]).reshape(-1)


def strip_reduce(partial, strips, strip_size):
    n_ex = lax.axis_size("ex")
    piece = -(-strip_size // n_ex)
    chunks = partial.reshape(2, strips, strip_size)
    if piece * n_ex != strip_size:
        chunks = jnp.pad(chunks, ((0, 0), (0, 0), (0, piece * n_ex - strip_size)))
    chunks = chunks.reshape(2, strips, n_ex, piece).transpose(2, 1, 0, 3)
    chunks = chunks.reshape(n_ex * strips, 2, piece)
    return lax.all_to_all(chunks, ("ex", "ey"), 0, 0, tiled=True).sum(0)


def strip_gather(mine, strip_size):
    n_ex = lax.axis_size("ex")
    count, piece = mine.shape
    spread_out = jnp.broadcast_to(mine[None], (n_ex, 2, piece))
    whole = lax.all_to_all(spread_out, "ex", 0, 0, tiled=True)
    return whole.transpose(1, 0, 2).reshape(2, n_ex * piece)[:, :strip_size]


def on_device(source, metric, fac_point, fac_strip, fac_shell, fac_area):
    weights, stiff = gll_tables()
    high, low = (2.0, 0.2)
    theta = (high + low) / 2.0
    delta = (high - low) / 2.0
    sigma = theta / delta
    rho_now = 1.0 / sigma
    both, _ = assemble(jnp.stack([source, local_diagonal(metric, weights, stiff)]))
    rhs = both[0]
    pinv = 1.0 / both[1]
    pressure = jnp.zeros_like(source)
    resid = rhs
    update = pinv * resid / theta
    picks = fac_point[0]
    areas = fac_area[0]
    strips = lax.axis_size("ey")
    global_ids = fac_strip[0, :, 0] * SHELL_STRIP + fac_shell[0]
    denom = segment_sum(areas, global_ids, strips * SHELL_STRIP, 256)
    for step in range(SWEEPS):
        pressure = pressure + update
        if step + 2 == SWEEPS:
            early = gather_flat(pressure.reshape(-1), picks, 256)
        applied = element_apply(update, metric, weights, stiff)
        if step + 1 == SWEEPS:
            samples = early + gather_flat(update.reshape(-1), picks, 256)
            numer = segment_sum(areas * samples, global_ids, strips * SHELL_STRIP, 256)
            partial = jnp.stack([numer, denom])
            assembled, mine = assemble(applied[None], strip_reduce(partial, strips, SHELL_STRIP))
        else:
            assembled, _ = assemble(applied[None])
        assembled = assembled[0]
        if step + 2 == SWEEPS:
            assembled, early = lax.optimization_barrier((assembled, early))
        if step == 0:
            assembled, denom = lax.optimization_barrier((assembled, denom))
        resid = resid - assembled
        if step + 1 < SWEEPS:
            rho_new = 1.0 / (2.0 * sigma - rho_now)
            update = rho_new * rho_now * update + 2.0 * rho_new / delta * pinv * resid
            rho_now = rho_new
    total = strip_gather(mine, SHELL_STRIP)
    shell_load = total[0] / jnp.maximum(total[1], 1.0)
    return (pressure, resid, shell_load)


def solution(mesh):
    placed = (
        P("ex", "ey", None, None, None, None),
        P(None, "ex", "ey", None),
        P("ex", "ey"),
        P("ex", "ey", None),
        P("ex", "ey"),
        P("ex", "ey"),
    )
    return jax.shard_map(
        on_device,
        mesh=mesh,
        in_specs=placed,
        out_specs=(
            P("ex", "ey", None, None, None, None),
            P("ex", "ey", None, None, None, None),
            P("ey"),
        ),
        check_vma=False,
    )
```

```python
import jax
import jax.numpy as jnp
import numpy as np
from jax import lax
from jax.sharding import PartitionSpec as P

SWEEPS = 4
SHELL_STRIP = 16384


def padded_2(block, sides, width):
    for axis, dim in sides:
        count = lax.axis_size(axis)
        forward = [(i, i + 1) for i in range(count - 1)]
        backward = [(target, source) for source, target in forward]
        low = lax.ppermute(
            lax.slice_in_dim(block, block.shape[dim] - width, None, axis=dim), axis, forward
        )
        high = lax.ppermute(lax.slice_in_dim(block, 0, width, axis=dim), axis, backward)
        block = jnp.concatenate([low, block, high], axis=dim)
    return block


def gll_tables():
    degree = 7
    points = np.array(
        [
            -1.0,
            -0.8717401485096066,
            -0.5917001814331423,
            -0.2092992179024789,
            0.2092992179024789,
            0.5917001814331423,
            0.8717401485096066,
            1.0,
        ]
    )
    previous = points * 0.0 + 1.0
    current = points * 1.0
    for order in range(1, degree):
        following = ((2 * order + 1) * points * current - order * previous) / (order + 1)
        previous = current
        current = following
    weights = 2.0 / (degree * (degree + 1) * current**2)
    count = degree + 1
    same = np.array([[1.0 if row == col else 0.0 for col in range(count)] for row in range(count)])
    between = points[:, None] - points[None, :] + same
    deriv = current[:, None] / current[None, :] / between * (1.0 - same)
    deriv[0, 0] = -degree * (degree + 1) / 4.0
    deriv[-1, -1] = degree * (degree + 1) / 4.0
    stiff = deriv.T @ (weights[:, None] * deriv)
    return (np.asarray(weights, np.float32), np.asarray(stiff, np.float32))


def spread(metric, which):
    return metric[which][:, :, None, None, None, :]


def element_apply(values_in, metric, weights, stiff):
    top = lax.Precision.HIGHEST
    weight_i = weights[None, None, :, None, None, None]
    weight_j = weights[None, None, None, :, None, None]
    weight_k = weights[None, None, None, None, :, None]
    along_x = jnp.einsum("im,abmjkc->abijkc", stiff, values_in, precision=top)
    along_y = jnp.einsum("jm,abimkc->abijkc", stiff, values_in, precision=top)
    along_z = jnp.einsum("km,abijmc->abijkc", stiff, values_in, precision=top)
    return (
        spread(metric, 0) * weight_j * weight_k * along_x
        + spread(metric, 1) * weight_i * weight_k * along_y
        + spread(metric, 2) * weight_i * weight_j * along_z
        + spread(metric, 3) * weight_i * weight_j * weight_k * values_in
    )


def local_diagonal(metric, weights, stiff):
    stiff_diag = np.diagonal(stiff)
    weight_i = weights[None, None, :, None, None, None]
    weight_j = weights[None, None, None, :, None, None]
    weight_k = weights[None, None, None, None, :, None]
    diag_i = stiff_diag[None, None, :, None, None, None]
    diag_j = stiff_diag[None, None, None, :, None, None]
    diag_k = stiff_diag[None, None, None, None, :, None]
    return (
        spread(metric, 0) * diag_i * weight_j * weight_k
        + spread(metric, 1) * weight_i * diag_j * weight_k
        + spread(metric, 2) * weight_i * weight_j * diag_k
        + spread(metric, 3) * weight_i * weight_j * weight_k
    )


def faces(values_in, face_dim):
    last = values_in.shape[face_dim] - 1
    lower = lax.index_in_dim(values_in, 0, face_dim, keepdims=False)
    upper = lax.index_in_dim(values_in, last, face_dim, keepdims=False)
    return (lower, upper)


def combine(values_in, face_dim, elem_dim, lower, upper, before, after):
    total = lower.shape[elem_dim]
    upper_prev = jnp.concatenate(
        [before, lax.slice_in_dim(upper, 0, total - 1, axis=elem_dim)], elem_dim
    )
    lower_next = jnp.concatenate(
        [lax.slice_in_dim(lower, 1, total, axis=elem_dim), after], elem_dim
    )
    middle = lax.slice_in_dim(values_in, 1, values_in.shape[face_dim] - 1, axis=face_dim)
    return jnp.concatenate(
        [
            jnp.expand_dims(lower + upper_prev, face_dim),
            middle,
            jnp.expand_dims(upper + lower_next, face_dim),
        ],
        face_dim,
    )


def assemble(values_in, ride=None):
    lower, upper = faces(values_in, 3)
    rim_faces = jnp.concatenate([lower, upper], 1)
    padded = padded_2(rim_faces, (("ex", 1),), 1)
    if ride is not None:
        padded, ride = lax.optimization_barrier((padded, ride))
    values_in = combine(values_in, 3, 1, lower, upper, padded[:, :1], padded[:, 3:])
    lower, upper = faces(values_in, 4)
    rim_faces = jnp.concatenate([lower, upper], 2)
    padded = padded_2(rim_faces, (("ey", 2),), 1)
    values_in = combine(values_in, 4, 2, lower, upper, padded[:, :, :1], padded[:, :, 3:])
    lower, upper = faces(values_in, 5)
    empty = jnp.zeros_like(upper[..., :1])
    return combine(values_in, 5, 5, lower, upper, empty, empty), ride


def split_parts(values, count):
    parts = []
    rest = values
    for _ in range(count - 1):
        part = lax.reduce_precision(rest, exponent_bits=8, mantissa_bits=7)
        parts.append(part)
        rest = rest - part
    parts.append(lax.reduce_precision(rest, exponent_bits=8, mantissa_bits=7))
    return [part.astype(jnp.bfloat16) for part in parts]


def one_hot(index, count):
    return (index[:, None] == lax.broadcasted_iota(jnp.int32, (1, count), 1)).astype(jnp.bfloat16)


def gather_flat(values, picks, lanes, count=3):
    rows = values.shape[0] // lanes
    table = values.reshape(rows, lanes)
    parts = jnp.concatenate(split_parts(table, count), axis=1)
    hit_row = one_hot(picks // lanes, rows)
    picked = jnp.dot(hit_row, parts, preferred_element_type=jnp.float32)
    pieces = [picked[:, n * lanes : (n + 1) * lanes] for n in range(count)]
    picked = pieces[0]
    for piece in pieces[1:]:
        picked = picked + piece
    hit_lane = (picks % lanes)[:, None] == lax.broadcasted_iota(jnp.int32, (1, lanes), 1)
    return jnp.sum(jnp.where(hit_lane, picked, 0.0), axis=1)


def segment_sum(values, ids, bins, lanes, count=3):
    rows = bins // lanes
    hit_lane = one_hot(ids % lanes, lanes)
    rhs = jnp.concatenate([hit_lane * part[:, None] for part in split_parts(values, count)], axis=1)
    hit_row = one_hot(ids // lanes, rows)
    sums = lax.dot_general(
        hit_row, rhs, (((0,), (0,)), ((), ())), preferred_element_type=jnp.float32
    )
    total = sums[:, :lanes]
    for n in range(1, count):
        total = total + sums[:, n * lanes : (n + 1) * lanes]
    return total.reshape(-1)


def strip_reduce(partial, strips, strip_size):
    n_ex = lax.axis_size("ex")
    piece = -(-strip_size // n_ex)
    chunks = partial.reshape(2, strips, strip_size)
    if piece * n_ex != strip_size:
        chunks = jnp.pad(chunks, ((0, 0), (0, 0), (0, piece * n_ex - strip_size)))
    chunks = chunks.reshape(2, strips, n_ex, piece).transpose(2, 1, 0, 3)
    chunks = chunks.reshape(n_ex * strips, 2, piece)
    return lax.all_to_all(chunks, ("ex", "ey"), 0, 0, tiled=True).sum(0)


def strip_gather(mine, strip_size):
    n_ex = lax.axis_size("ex")
    count, piece = mine.shape
    spread_out = jnp.broadcast_to(mine[None], (n_ex, 2, piece))
    whole = lax.all_to_all(spread_out, "ex", 0, 0, tiled=True)
    return whole.transpose(1, 0, 2).reshape(2, n_ex * piece)[:, :strip_size]


def on_device(source, metric, fac_point, fac_strip, fac_shell, fac_area):
    weights, stiff = gll_tables()
    high, low = (2.0, 0.2)
    theta = (high + low) / 2.0
    delta = (high - low) / 2.0
    sigma = theta / delta
    rho_now = 1.0 / sigma
    both, _ = assemble(jnp.stack([source, local_diagonal(metric, weights, stiff)]))
    rhs = both[0]
    pinv = 1.0 / both[1]
    pressure = jnp.zeros_like(source)
    resid = rhs
    update = pinv * resid / theta
    picks = fac_point[0]
    areas = fac_area[0]
    strips = lax.axis_size("ey")
    global_ids = fac_strip[0, :, 0] * SHELL_STRIP + fac_shell[0]
    denom = segment_sum(areas, global_ids, strips * SHELL_STRIP, 256)
    for step in range(SWEEPS):
        pressure = pressure + update
        if step + 2 == SWEEPS:
            early = gather_flat(pressure.reshape(-1), picks, 256)
        applied = element_apply(update, metric, weights, stiff)
        if step + 1 == SWEEPS:
            samples = early + gather_flat(update.reshape(-1), picks, 256, 2)
            numer = segment_sum(areas * samples, global_ids, strips * SHELL_STRIP, 256, 2)
            partial = jnp.stack([numer, denom])
            assembled, mine = assemble(applied[None], strip_reduce(partial, strips, SHELL_STRIP))
        else:
            assembled, _ = assemble(applied[None])
        assembled = assembled[0]
        if step + 2 == SWEEPS:
            assembled, early = lax.optimization_barrier((assembled, early))
        if step == 0:
            assembled, denom = lax.optimization_barrier((assembled, denom))
        resid = resid - assembled
        if step + 1 < SWEEPS:
            rho_new = 1.0 / (2.0 * sigma - rho_now)
            update = rho_new * rho_now * update + 2.0 * rho_new / delta * pinv * resid
            rho_now = rho_new
    total = strip_gather(mine, SHELL_STRIP)
    shell_load = total[0] / jnp.maximum(total[1], 1.0)
    return (pressure, resid, shell_load)


def solution(mesh):
    placed = (
        P("ex", "ey", None, None, None, None),
        P(None, "ex", "ey", None),
        P("ex", "ey"),
        P("ex", "ey", None),
        P("ex", "ey"),
        P("ex", "ey"),
    )
    return jax.shard_map(
        on_device,
        mesh=mesh,
        in_specs=placed,
        out_specs=(
            P("ex", "ey", None, None, None, None),
            P("ex", "ey", None, None, None, None),
            P("ey"),
        ),
        check_vma=False,
    )
```

```python
import jax
import jax.numpy as jnp
import numpy as np
from jax import lax
from jax.sharding import PartitionSpec as P

SWEEPS = 4
SHELL_STRIP = 16384


def padded_2(block, sides, width):
    for axis, dim in sides:
        count = lax.axis_size(axis)
        forward = [(i, i + 1) for i in range(count - 1)]
        backward = [(target, source) for source, target in forward]
        low = lax.ppermute(
            lax.slice_in_dim(block, block.shape[dim] - width, None, axis=dim), axis, forward
        )
        high = lax.ppermute(lax.slice_in_dim(block, 0, width, axis=dim), axis, backward)
        block = jnp.concatenate([low, block, high], axis=dim)
    return block


def gll_tables():
    degree = 7
    points = np.array(
        [
            -1.0,
            -0.8717401485096066,
            -0.5917001814331423,
            -0.2092992179024789,
            0.2092992179024789,
            0.5917001814331423,
            0.8717401485096066,
            1.0,
        ]
    )
    previous = points * 0.0 + 1.0
    current = points * 1.0
    for order in range(1, degree):
        following = ((2 * order + 1) * points * current - order * previous) / (order + 1)
        previous = current
        current = following
    weights = 2.0 / (degree * (degree + 1) * current**2)
    count = degree + 1
    same = np.array([[1.0 if row == col else 0.0 for col in range(count)] for row in range(count)])
    between = points[:, None] - points[None, :] + same
    deriv = current[:, None] / current[None, :] / between * (1.0 - same)
    deriv[0, 0] = -degree * (degree + 1) / 4.0
    deriv[-1, -1] = degree * (degree + 1) / 4.0
    stiff = deriv.T @ (weights[:, None] * deriv)
    return (np.asarray(weights, np.float32), np.asarray(stiff, np.float32))


def spread(metric, which):
    return metric[which][:, :, None, None, None, :]


def element_apply(values_in, metric, weights, stiff):
    top = lax.Precision.HIGHEST
    weight_i = weights[None, None, :, None, None, None]
    weight_j = weights[None, None, None, :, None, None]
    weight_k = weights[None, None, None, None, :, None]
    along_x = jnp.einsum("im,abmjkc->abijkc", stiff, values_in, precision=top)
    along_y = jnp.einsum("jm,abimkc->abijkc", stiff, values_in, precision=top)
    along_z = jnp.einsum("km,abijmc->abijkc", stiff, values_in, precision=top)
    return (
        spread(metric, 0) * weight_j * weight_k * along_x
        + spread(metric, 1) * weight_i * weight_k * along_y
        + spread(metric, 2) * weight_i * weight_j * along_z
        + spread(metric, 3) * weight_i * weight_j * weight_k * values_in
    )


def local_diagonal(metric, weights, stiff):
    stiff_diag = np.diagonal(stiff)
    weight_i = weights[None, None, :, None, None, None]
    weight_j = weights[None, None, None, :, None, None]
    weight_k = weights[None, None, None, None, :, None]
    diag_i = stiff_diag[None, None, :, None, None, None]
    diag_j = stiff_diag[None, None, None, :, None, None]
    diag_k = stiff_diag[None, None, None, None, :, None]
    return (
        spread(metric, 0) * diag_i * weight_j * weight_k
        + spread(metric, 1) * weight_i * diag_j * weight_k
        + spread(metric, 2) * weight_i * weight_j * diag_k
        + spread(metric, 3) * weight_i * weight_j * weight_k
    )


def faces(values_in, face_dim):
    last = values_in.shape[face_dim] - 1
    lower = lax.index_in_dim(values_in, 0, face_dim, keepdims=False)
    upper = lax.index_in_dim(values_in, last, face_dim, keepdims=False)
    return (lower, upper)


def combine(values_in, face_dim, elem_dim, lower, upper, before, after):
    total = lower.shape[elem_dim]
    upper_prev = jnp.concatenate(
        [before, lax.slice_in_dim(upper, 0, total - 1, axis=elem_dim)], elem_dim
    )
    lower_next = jnp.concatenate(
        [lax.slice_in_dim(lower, 1, total, axis=elem_dim), after], elem_dim
    )
    middle = lax.slice_in_dim(values_in, 1, values_in.shape[face_dim] - 1, axis=face_dim)
    return jnp.concatenate(
        [
            jnp.expand_dims(lower + upper_prev, face_dim),
            middle,
            jnp.expand_dims(upper + lower_next, face_dim),
        ],
        face_dim,
    )


def assemble(values_in, ride=None):
    lower, upper = faces(values_in, 3)
    rim_faces = jnp.concatenate([lower, upper], 1)
    padded = padded_2(rim_faces, (("ex", 1),), 1)
    if ride is not None:
        padded, ride = lax.optimization_barrier((padded, ride))
    values_in = combine(values_in, 3, 1, lower, upper, padded[:, :1], padded[:, 3:])
    lower, upper = faces(values_in, 4)
    rim_faces = jnp.concatenate([lower, upper], 2)
    padded = padded_2(rim_faces, (("ey", 2),), 1)
    values_in = combine(values_in, 4, 2, lower, upper, padded[:, :, :1], padded[:, :, 3:])
    lower, upper = faces(values_in, 5)
    empty = jnp.zeros_like(upper[..., :1])
    return combine(values_in, 5, 5, lower, upper, empty, empty), ride


def split_parts(values, count):
    parts = []
    rest = values
    for _ in range(count - 1):
        part = lax.reduce_precision(rest, exponent_bits=8, mantissa_bits=7)
        parts.append(part)
        rest = rest - part
    parts.append(lax.reduce_precision(rest, exponent_bits=8, mantissa_bits=7))
    return [part.astype(jnp.bfloat16) for part in parts]


def one_hot(index, count):
    return (index[:, None] == lax.broadcasted_iota(jnp.int32, (1, count), 1)).astype(jnp.bfloat16)


def gather_flat(values, picks, lanes, count=3):
    rows = values.shape[0] // lanes
    table = values.reshape(rows, lanes)
    parts = jnp.concatenate(split_parts(table, count), axis=1)
    hit_row = one_hot(picks // lanes, rows)
    picked = jnp.dot(hit_row, parts, preferred_element_type=jnp.float32)
    pieces = [picked[:, n * lanes : (n + 1) * lanes] for n in range(count)]
    picked = pieces[0]
    for piece in pieces[1:]:
        picked = picked + piece
    hit_lane = (picks % lanes)[:, None] == lax.broadcasted_iota(jnp.int32, (1, lanes), 1)
    return jnp.sum(jnp.where(hit_lane, picked, 0.0), axis=1)


def segment_sum(values, ids, bins, lanes, count=3):
    rows = bins // lanes
    hit_lane = one_hot(ids % lanes, lanes)
    rhs = jnp.concatenate([hit_lane * part[:, None] for part in split_parts(values, count)], axis=1)
    hit_row_t = (lax.broadcasted_iota(jnp.int32, (rows, 1), 0) == (ids // lanes)[None, :]).astype(jnp.bfloat16)
    sums = jnp.dot(hit_row_t, rhs, preferred_element_type=jnp.float32)
    total = sums[:, :lanes]
    for n in range(1, count):
        total = total + sums[:, n * lanes : (n + 1) * lanes]
    return total.reshape(-1)


def strip_reduce(partial, strips, strip_size):
    n_ex = lax.axis_size("ex")
    piece = -(-strip_size // n_ex)
    chunks = partial.reshape(2, strips, strip_size)
    if piece * n_ex != strip_size:
        chunks = jnp.pad(chunks, ((0, 0), (0, 0), (0, piece * n_ex - strip_size)))
    chunks = chunks.reshape(2, strips, n_ex, piece).transpose(2, 1, 0, 3)
    chunks = chunks.reshape(n_ex * strips, 2, piece)
    return lax.all_to_all(chunks, ("ex", "ey"), 0, 0, tiled=True).sum(0)


def strip_gather(mine, strip_size):
    n_ex = lax.axis_size("ex")
    count, piece = mine.shape
    spread_out = jnp.broadcast_to(mine[None], (n_ex, 2, piece))
    whole = lax.all_to_all(spread_out, "ex", 0, 0, tiled=True)
    return whole.transpose(1, 0, 2).reshape(2, n_ex * piece)[:, :strip_size]


def on_device(source, metric, fac_point, fac_strip, fac_shell, fac_area):
    weights, stiff = gll_tables()
    high, low = (2.0, 0.2)
    theta = (high + low) / 2.0
    delta = (high - low) / 2.0
    sigma = theta / delta
    rho_now = 1.0 / sigma
    both, _ = assemble(jnp.stack([source, local_diagonal(metric, weights, stiff)]))
    rhs = both[0]
    pinv = 1.0 / both[1]
    pressure = jnp.zeros_like(source)
    resid = rhs
    update = pinv * resid / theta
    picks = fac_point[0]
    areas = fac_area[0]
    strips = lax.axis_size("ey")
    global_ids = fac_strip[0, :, 0] * SHELL_STRIP + fac_shell[0]
    denom = segment_sum(areas, global_ids, strips * SHELL_STRIP, 256)
    for step in range(SWEEPS):
        pressure = pressure + update
        if step + 2 == SWEEPS:
            early = gather_flat(pressure.reshape(-1), picks, 256)
        applied = element_apply(update, metric, weights, stiff)
        if step + 1 == SWEEPS:
            samples = early + gather_flat(update.reshape(-1), picks, 256, 2)
            numer = segment_sum(areas * samples, global_ids, strips * SHELL_STRIP, 256, 2)
            partial = jnp.stack([numer, denom])
            assembled, mine = assemble(applied[None], strip_reduce(partial, strips, SHELL_STRIP))
        else:
            assembled, _ = assemble(applied[None])
        assembled = assembled[0]
        if step + 2 == SWEEPS:
            assembled, early = lax.optimization_barrier((assembled, early))
        if step == 0:
            assembled, denom = lax.optimization_barrier((assembled, denom))
        resid = resid - assembled
        if step + 1 < SWEEPS:
            rho_new = 1.0 / (2.0 * sigma - rho_now)
            update = rho_new * rho_now * update + 2.0 * rho_new / delta * pinv * resid
            rho_now = rho_new
    total = strip_gather(mine, SHELL_STRIP)
    shell_load = total[0] / jnp.maximum(total[1], 1.0)
    return (pressure, resid, shell_load)


def solution(mesh):
    placed = (
        P("ex", "ey", None, None, None, None),
        P(None, "ex", "ey", None),
        P("ex", "ey"),
        P("ex", "ey", None),
        P("ex", "ey"),
        P("ex", "ey"),
    )
    return jax.shard_map(
        on_device,
        mesh=mesh,
        in_specs=placed,
        out_specs=(
            P("ex", "ey", None, None, None, None),
            P("ex", "ey", None, None, None, None),
            P("ey"),
        ),
        check_vma=False,
    )
```

```python
import jax
import jax.numpy as jnp
import numpy as np
from jax import lax
from jax.sharding import PartitionSpec as P

SWEEPS = 4
SHELL_STRIP = 16384


def padded_2(block, sides, width):
    for axis, dim in sides:
        count = lax.axis_size(axis)
        forward = [(i, i + 1) for i in range(count - 1)]
        backward = [(target, source) for source, target in forward]
        low = lax.ppermute(
            lax.slice_in_dim(block, block.shape[dim] - width, None, axis=dim), axis, forward
        )
        high = lax.ppermute(lax.slice_in_dim(block, 0, width, axis=dim), axis, backward)
        block = jnp.concatenate([low, block, high], axis=dim)
    return block


def gll_tables():
    degree = 7
    points = np.array(
        [
            -1.0,
            -0.8717401485096066,
            -0.5917001814331423,
            -0.2092992179024789,
            0.2092992179024789,
            0.5917001814331423,
            0.8717401485096066,
            1.0,
        ]
    )
    previous = points * 0.0 + 1.0
    current = points * 1.0
    for order in range(1, degree):
        following = ((2 * order + 1) * points * current - order * previous) / (order + 1)
        previous = current
        current = following
    weights = 2.0 / (degree * (degree + 1) * current**2)
    count = degree + 1
    same = np.array([[1.0 if row == col else 0.0 for col in range(count)] for row in range(count)])
    between = points[:, None] - points[None, :] + same
    deriv = current[:, None] / current[None, :] / between * (1.0 - same)
    deriv[0, 0] = -degree * (degree + 1) / 4.0
    deriv[-1, -1] = degree * (degree + 1) / 4.0
    stiff = deriv.T @ (weights[:, None] * deriv)
    return (np.asarray(weights, np.float32), np.asarray(stiff, np.float32))


def spread(metric, which):
    return metric[which][:, :, None, None, None, :]


def element_apply(values_in, metric, weights, stiff):
    top = lax.Precision.HIGHEST
    weight_i = weights[None, None, :, None, None, None]
    weight_j = weights[None, None, None, :, None, None]
    weight_k = weights[None, None, None, None, :, None]
    along_x = jnp.einsum("im,abmjkc->abijkc", stiff, values_in, precision=top)
    along_y = jnp.einsum("jm,abimkc->abijkc", stiff, values_in, precision=top)
    along_z = jnp.einsum("km,abijmc->abijkc", stiff, values_in, precision=top)
    return (
        spread(metric, 0) * weight_j * weight_k * along_x
        + spread(metric, 1) * weight_i * weight_k * along_y
        + spread(metric, 2) * weight_i * weight_j * along_z
        + spread(metric, 3) * weight_i * weight_j * weight_k * values_in
    )


def local_diagonal(metric, weights, stiff):
    stiff_diag = np.diagonal(stiff)
    weight_i = weights[None, None, :, None, None, None]
    weight_j = weights[None, None, None, :, None, None]
    weight_k = weights[None, None, None, None, :, None]
    diag_i = stiff_diag[None, None, :, None, None, None]
    diag_j = stiff_diag[None, None, None, :, None, None]
    diag_k = stiff_diag[None, None, None, None, :, None]
    return (
        spread(metric, 0) * diag_i * weight_j * weight_k
        + spread(metric, 1) * weight_i * diag_j * weight_k
        + spread(metric, 2) * weight_i * weight_j * diag_k
        + spread(metric, 3) * weight_i * weight_j * weight_k
    )


def faces(values_in, face_dim):
    last = values_in.shape[face_dim] - 1
    lower = lax.index_in_dim(values_in, 0, face_dim, keepdims=False)
    upper = lax.index_in_dim(values_in, last, face_dim, keepdims=False)
    return (lower, upper)


def combine(values_in, face_dim, elem_dim, lower, upper, before, after):
    total = lower.shape[elem_dim]
    upper_prev = jnp.concatenate(
        [before, lax.slice_in_dim(upper, 0, total - 1, axis=elem_dim)], elem_dim
    )
    lower_next = jnp.concatenate(
        [lax.slice_in_dim(lower, 1, total, axis=elem_dim), after], elem_dim
    )
    middle = lax.slice_in_dim(values_in, 1, values_in.shape[face_dim] - 1, axis=face_dim)
    return jnp.concatenate(
        [
            jnp.expand_dims(lower + upper_prev, face_dim),
            middle,
            jnp.expand_dims(upper + lower_next, face_dim),
        ],
        face_dim,
    )


def assemble(values_in, ride=None):
    lower, upper = faces(values_in, 3)
    rim_faces = jnp.concatenate([lower, upper], 1)
    padded = padded_2(rim_faces, (("ex", 1),), 1)
    if ride is not None:
        padded, ride = lax.optimization_barrier((padded, ride))
    values_in = combine(values_in, 3, 1, lower, upper, padded[:, :1], padded[:, 3:])
    lower, upper = faces(values_in, 4)
    rim_faces = jnp.concatenate([lower, upper], 2)
    padded = padded_2(rim_faces, (("ey", 2),), 1)
    values_in = combine(values_in, 4, 2, lower, upper, padded[:, :, :1], padded[:, :, 3:])
    lower, upper = faces(values_in, 5)
    empty = jnp.zeros_like(upper[..., :1])
    return combine(values_in, 5, 5, lower, upper, empty, empty), ride


def split_parts(values, count):
    parts = []
    rest = values
    for _ in range(count - 1):
        part = lax.reduce_precision(rest, exponent_bits=8, mantissa_bits=7)
        parts.append(part)
        rest = rest - part
    parts.append(lax.reduce_precision(rest, exponent_bits=8, mantissa_bits=7))
    return [part.astype(jnp.bfloat16) for part in parts]


def one_hot(index, count):
    return (index[:, None] == lax.broadcasted_iota(jnp.int32, (1, count), 1)).astype(jnp.bfloat16)


def gather_flat(values, picks, lanes, count=3):
    rows = values.shape[0] // lanes
    table = values.reshape(rows, lanes)
    parts = jnp.concatenate(split_parts(table, count), axis=1)
    hit_row = one_hot(picks // lanes, rows)
    picked = jnp.dot(hit_row, parts, preferred_element_type=jnp.float32)
    pieces = [picked[:, n * lanes : (n + 1) * lanes] for n in range(count)]
    picked = pieces[0]
    for piece in pieces[1:]:
        picked = picked + piece
    hit_lane = (picks % lanes)[:, None] == lax.broadcasted_iota(jnp.int32, (1, lanes), 1)
    return jnp.sum(jnp.where(hit_lane, picked, 0.0), axis=1)


def segment_sum(values, ids, bins, lanes, count=3):
    rows = bins // lanes
    hit_row_t = lax.broadcasted_iota(jnp.int32, (rows, 1), 0) == (ids // lanes)[None, :]
    lhs = jnp.concatenate(
        [jnp.where(hit_row_t, part[None, :], jnp.bfloat16(0)) for part in split_parts(values, count)], axis=0
    )
    sums = jnp.dot(lhs, one_hot(ids % lanes, lanes), preferred_element_type=jnp.float32)
    total = sums[:rows]
    for n in range(1, count):
        total = total + sums[n * rows : (n + 1) * rows]
    return total.reshape(-1)


def strip_reduce(partial, strips, strip_size):
    n_ex = lax.axis_size("ex")
    piece = -(-strip_size // n_ex)
    chunks = partial.reshape(2, strips, strip_size)
    if piece * n_ex != strip_size:
        chunks = jnp.pad(chunks, ((0, 0), (0, 0), (0, piece * n_ex - strip_size)))
    chunks = chunks.reshape(2, strips, n_ex, piece).transpose(2, 1, 0, 3)
    chunks = chunks.reshape(n_ex * strips, 2, piece)
    return lax.all_to_all(chunks, ("ex", "ey"), 0, 0, tiled=True).sum(0)


def strip_gather(mine, strip_size):
    n_ex = lax.axis_size("ex")
    count, piece = mine.shape
    spread_out = jnp.broadcast_to(mine[None], (n_ex, 2, piece))
    whole = lax.all_to_all(spread_out, "ex", 0, 0, tiled=True)
    return whole.transpose(1, 0, 2).reshape(2, n_ex * piece)[:, :strip_size]


def on_device(source, metric, fac_point, fac_strip, fac_shell, fac_area):
    weights, stiff = gll_tables()
    high, low = (2.0, 0.2)
    theta = (high + low) / 2.0
    delta = (high - low) / 2.0
    sigma = theta / delta
    rho_now = 1.0 / sigma
    both, _ = assemble(jnp.stack([source, local_diagonal(metric, weights, stiff)]))
    rhs = both[0]
    pinv = 1.0 / both[1]
    pressure = jnp.zeros_like(source)
    resid = rhs
    update = pinv * resid / theta
    picks = fac_point[0]
    areas = fac_area[0]
    strips = lax.axis_size("ey")
    global_ids = fac_strip[0, :, 0] * SHELL_STRIP + fac_shell[0]
    denom = segment_sum(areas, global_ids, strips * SHELL_STRIP, 256)
    for step in range(SWEEPS):
        pressure = pressure + update
        if step + 2 == SWEEPS:
            early = gather_flat(pressure.reshape(-1), picks, 256)
        applied = element_apply(update, metric, weights, stiff)
        if step + 1 == SWEEPS:
            samples = early + gather_flat(update.reshape(-1), picks, 256, 2)
            numer = segment_sum(areas * samples, global_ids, strips * SHELL_STRIP, 256, 2)
            partial = jnp.stack([numer, denom])
            assembled, mine = assemble(applied[None], strip_reduce(partial, strips, SHELL_STRIP))
        else:
            assembled, _ = assemble(applied[None])
        assembled = assembled[0]
        if step + 2 == SWEEPS:
            assembled, early = lax.optimization_barrier((assembled, early))
        if step == 0:
            assembled, denom = lax.optimization_barrier((assembled, denom))
        resid = resid - assembled
        if step + 1 < SWEEPS:
            rho_new = 1.0 / (2.0 * sigma - rho_now)
            update = rho_new * rho_now * update + 2.0 * rho_new / delta * pinv * resid
            rho_now = rho_new
    total = strip_gather(mine, SHELL_STRIP)
    shell_load = total[0] / jnp.maximum(total[1], 1.0)
    return (pressure, resid, shell_load)


def solution(mesh):
    placed = (
        P("ex", "ey", None, None, None, None),
        P(None, "ex", "ey", None),
        P("ex", "ey"),
        P("ex", "ey", None),
        P("ex", "ey"),
        P("ex", "ey"),
    )
    return jax.shard_map(
        on_device,
        mesh=mesh,
        in_specs=placed,
        out_specs=(
            P("ex", "ey", None, None, None, None),
            P("ex", "ey", None, None, None, None),
            P("ey"),
        ),
        check_vma=False,
    )
```

```python
import jax
import jax.numpy as jnp
import numpy as np
from jax import lax
from jax.sharding import PartitionSpec as P

SWEEPS = 4
SHELL_STRIP = 16384


def padded_2(block, sides, width):
    for axis, dim in sides:
        count = lax.axis_size(axis)
        forward = [(i, i + 1) for i in range(count - 1)]
        backward = [(target, source) for source, target in forward]
        low = lax.ppermute(
            lax.slice_in_dim(block, block.shape[dim] - width, None, axis=dim), axis, forward
        )
        high = lax.ppermute(lax.slice_in_dim(block, 0, width, axis=dim), axis, backward)
        block = jnp.concatenate([low, block, high], axis=dim)
    return block


def gll_tables():
    degree = 7
    points = np.array(
        [
            -1.0,
            -0.8717401485096066,
            -0.5917001814331423,
            -0.2092992179024789,
            0.2092992179024789,
            0.5917001814331423,
            0.8717401485096066,
            1.0,
        ]
    )
    previous = points * 0.0 + 1.0
    current = points * 1.0
    for order in range(1, degree):
        following = ((2 * order + 1) * points * current - order * previous) / (order + 1)
        previous = current
        current = following
    weights = 2.0 / (degree * (degree + 1) * current**2)
    count = degree + 1
    same = np.array([[1.0 if row == col else 0.0 for col in range(count)] for row in range(count)])
    between = points[:, None] - points[None, :] + same
    deriv = current[:, None] / current[None, :] / between * (1.0 - same)
    deriv[0, 0] = -degree * (degree + 1) / 4.0
    deriv[-1, -1] = degree * (degree + 1) / 4.0
    stiff = deriv.T @ (weights[:, None] * deriv)
    return (np.asarray(weights, np.float32), np.asarray(stiff, np.float32))


def spread(metric, which):
    return metric[which][:, :, None, None, None, :]


def element_apply(values_in, metric, weights, stiff):
    top = lax.Precision.HIGHEST
    weight_i = weights[None, None, :, None, None, None]
    weight_j = weights[None, None, None, :, None, None]
    weight_k = weights[None, None, None, None, :, None]
    along_x = jnp.einsum("im,abmjkc->abijkc", stiff, values_in, precision=top)
    along_y = jnp.einsum("jm,abimkc->abijkc", stiff, values_in, precision=top)
    along_z = jnp.einsum("km,abijmc->abijkc", stiff, values_in, precision=top)
    return (
        spread(metric, 0) * weight_j * weight_k * along_x
        + spread(metric, 1) * weight_i * weight_k * along_y
        + spread(metric, 2) * weight_i * weight_j * along_z
        + spread(metric, 3) * weight_i * weight_j * weight_k * values_in
    )


def local_diagonal(metric, weights, stiff):
    stiff_diag = np.diagonal(stiff)
    weight_i = weights[None, None, :, None, None, None]
    weight_j = weights[None, None, None, :, None, None]
    weight_k = weights[None, None, None, None, :, None]
    diag_i = stiff_diag[None, None, :, None, None, None]
    diag_j = stiff_diag[None, None, None, :, None, None]
    diag_k = stiff_diag[None, None, None, None, :, None]
    return (
        spread(metric, 0) * diag_i * weight_j * weight_k
        + spread(metric, 1) * weight_i * diag_j * weight_k
        + spread(metric, 2) * weight_i * weight_j * diag_k
        + spread(metric, 3) * weight_i * weight_j * weight_k
    )


def faces(values_in, face_dim):
    last = values_in.shape[face_dim] - 1
    lower = lax.index_in_dim(values_in, 0, face_dim, keepdims=False)
    upper = lax.index_in_dim(values_in, last, face_dim, keepdims=False)
    return (lower, upper)


def combine(values_in, face_dim, elem_dim, lower, upper, before, after):
    total = lower.shape[elem_dim]
    upper_prev = jnp.concatenate(
        [before, lax.slice_in_dim(upper, 0, total - 1, axis=elem_dim)], elem_dim
    )
    lower_next = jnp.concatenate(
        [lax.slice_in_dim(lower, 1, total, axis=elem_dim), after], elem_dim
    )
    middle = lax.slice_in_dim(values_in, 1, values_in.shape[face_dim] - 1, axis=face_dim)
    return jnp.concatenate(
        [
            jnp.expand_dims(lower + upper_prev, face_dim),
            middle,
            jnp.expand_dims(upper + lower_next, face_dim),
        ],
        face_dim,
    )


def assemble(values_in, ride=None):
    lower, upper = faces(values_in, 3)
    rim_faces = jnp.concatenate([lower, upper], 1)
    padded = padded_2(rim_faces, (("ex", 1),), 1)
    if ride is not None:
        padded, ride = lax.optimization_barrier((padded, ride))
    values_in = combine(values_in, 3, 1, lower, upper, padded[:, :1], padded[:, 3:])
    lower, upper = faces(values_in, 4)
    rim_faces = jnp.concatenate([lower, upper], 2)
    padded = padded_2(rim_faces, (("ey", 2),), 1)
    values_in = combine(values_in, 4, 2, lower, upper, padded[:, :, :1], padded[:, :, 3:])
    lower, upper = faces(values_in, 5)
    empty = jnp.zeros_like(upper[..., :1])
    return combine(values_in, 5, 5, lower, upper, empty, empty), ride


def split_parts(values, count):
    parts = []
    rest = values
    for _ in range(count - 1):
        part = lax.reduce_precision(rest, exponent_bits=8, mantissa_bits=7)
        parts.append(part)
        rest = rest - part
    parts.append(lax.reduce_precision(rest, exponent_bits=8, mantissa_bits=7))
    return [part.astype(jnp.bfloat16) for part in parts]


def one_hot(index, count):
    return (index[:, None] == lax.broadcasted_iota(jnp.int32, (1, count), 1)).astype(jnp.bfloat16)


def gather_flat(values, picks, lanes, count=3):
    rows = values.shape[0] // lanes
    table = values.reshape(rows, lanes)
    parts = jnp.concatenate(split_parts(table, count), axis=1)
    hit_row_t = (lax.broadcasted_iota(jnp.int32, (rows, 1), 0) == (picks // lanes)[None, :]).astype(jnp.bfloat16)
    picked = lax.dot_general(parts, hit_row_t, (((0,), (0,)), ((), ())), preferred_element_type=jnp.float32)
    total = picked[:lanes]
    for n in range(1, count):
        total = total + picked[n * lanes : (n + 1) * lanes]
    hit_lane_t = lax.broadcasted_iota(jnp.int32, (lanes, 1), 0) == (picks % lanes)[None, :]
    return jnp.sum(jnp.where(hit_lane_t, total, 0.0), axis=0)


def segment_sum(values, ids, bins, lanes, count=3):
    rows = bins // lanes
    hit_row_t = lax.broadcasted_iota(jnp.int32, (rows, 1), 0) == (ids // lanes)[None, :]
    lhs = jnp.concatenate(
        [jnp.where(hit_row_t, part[None, :], jnp.bfloat16(0)) for part in split_parts(values, count)], axis=0
    )
    sums = jnp.dot(lhs, one_hot(ids % lanes, lanes), preferred_element_type=jnp.float32)
    total = sums[:rows]
    for n in range(1, count):
        total = total + sums[n * rows : (n + 1) * rows]
    return total.reshape(-1)


def strip_reduce(partial, strips, strip_size):
    n_ex = lax.axis_size("ex")
    piece = -(-strip_size // n_ex)
    chunks = partial.reshape(2, strips, strip_size)
    if piece * n_ex != strip_size:
        chunks = jnp.pad(chunks, ((0, 0), (0, 0), (0, piece * n_ex - strip_size)))
    chunks = chunks.reshape(2, strips, n_ex, piece).transpose(2, 1, 0, 3)
    chunks = chunks.reshape(n_ex * strips, 2, piece)
    return lax.all_to_all(chunks, ("ex", "ey"), 0, 0, tiled=True).sum(0)


def strip_gather(mine, strip_size):
    n_ex = lax.axis_size("ex")
    count, piece = mine.shape
    spread_out = jnp.broadcast_to(mine[None], (n_ex, 2, piece))
    whole = lax.all_to_all(spread_out, "ex", 0, 0, tiled=True)
    return whole.transpose(1, 0, 2).reshape(2, n_ex * piece)[:, :strip_size]


def on_device(source, metric, fac_point, fac_strip, fac_shell, fac_area):
    weights, stiff = gll_tables()
    high, low = (2.0, 0.2)
    theta = (high + low) / 2.0
    delta = (high - low) / 2.0
    sigma = theta / delta
    rho_now = 1.0 / sigma
    both, _ = assemble(jnp.stack([source, local_diagonal(metric, weights, stiff)]))
    rhs = both[0]
    pinv = 1.0 / both[1]
    pressure = jnp.zeros_like(source)
    resid = rhs
    update = pinv * resid / theta
    picks = fac_point[0]
    areas = fac_area[0]
    strips = lax.axis_size("ey")
    global_ids = fac_strip[0, :, 0] * SHELL_STRIP + fac_shell[0]
    denom = segment_sum(areas, global_ids, strips * SHELL_STRIP, 256)
    for step in range(SWEEPS):
        pressure = pressure + update
        if step + 2 == SWEEPS:
            early = gather_flat(pressure.reshape(-1), picks, 256)
        applied = element_apply(update, metric, weights, stiff)
        if step + 1 == SWEEPS:
            samples = early + gather_flat(update.reshape(-1), picks, 256, 2)
            numer = segment_sum(areas * samples, global_ids, strips * SHELL_STRIP, 256, 2)
            partial = jnp.stack([numer, denom])
            assembled, mine = assemble(applied[None], strip_reduce(partial, strips, SHELL_STRIP))
        else:
            assembled, _ = assemble(applied[None])
        assembled = assembled[0]
        if step + 2 == SWEEPS:
            assembled, early = lax.optimization_barrier((assembled, early))
        if step == 0:
            assembled, denom = lax.optimization_barrier((assembled, denom))
        resid = resid - assembled
        if step + 1 < SWEEPS:
            rho_new = 1.0 / (2.0 * sigma - rho_now)
            update = rho_new * rho_now * update + 2.0 * rho_new / delta * pinv * resid
            rho_now = rho_new
    total = strip_gather(mine, SHELL_STRIP)
    shell_load = total[0] / jnp.maximum(total[1], 1.0)
    return (pressure, resid, shell_load)


def solution(mesh):
    placed = (
        P("ex", "ey", None, None, None, None),
        P(None, "ex", "ey", None),
        P("ex", "ey"),
        P("ex", "ey", None),
        P("ex", "ey"),
        P("ex", "ey"),
    )
    return jax.shard_map(
        on_device,
        mesh=mesh,
        in_specs=placed,
        out_specs=(
            P("ex", "ey", None, None, None, None),
            P("ex", "ey", None, None, None, None),
            P("ey"),
        ),
        check_vma=False,
    )
```

```python
import jax
import jax.numpy as jnp
import numpy as np
from jax import lax
from jax.sharding import PartitionSpec as P

SWEEPS = 4
SHELL_STRIP = 16384


def padded_2(block, sides, width):
    for axis, dim in sides:
        count = lax.axis_size(axis)
        forward = [(i, i + 1) for i in range(count - 1)]
        backward = [(target, source) for source, target in forward]
        low = lax.ppermute(
            lax.slice_in_dim(block, block.shape[dim] - width, None, axis=dim), axis, forward
        )
        high = lax.ppermute(lax.slice_in_dim(block, 0, width, axis=dim), axis, backward)
        block = jnp.concatenate([low, block, high], axis=dim)
    return block


def gll_tables():
    degree = 7
    points = np.array(
        [
            -1.0,
            -0.8717401485096066,
            -0.5917001814331423,
            -0.2092992179024789,
            0.2092992179024789,
            0.5917001814331423,
            0.8717401485096066,
            1.0,
        ]
    )
    previous = points * 0.0 + 1.0
    current = points * 1.0
    for order in range(1, degree):
        following = ((2 * order + 1) * points * current - order * previous) / (order + 1)
        previous = current
        current = following
    weights = 2.0 / (degree * (degree + 1) * current**2)
    count = degree + 1
    same = np.array([[1.0 if row == col else 0.0 for col in range(count)] for row in range(count)])
    between = points[:, None] - points[None, :] + same
    deriv = current[:, None] / current[None, :] / between * (1.0 - same)
    deriv[0, 0] = -degree * (degree + 1) / 4.0
    deriv[-1, -1] = degree * (degree + 1) / 4.0
    stiff = deriv.T @ (weights[:, None] * deriv)
    return (np.asarray(weights, np.float32), np.asarray(stiff, np.float32))


def spread(metric, which):
    return metric[which][:, :, None, None, None, :]


def element_apply(values_in, metric, weights, stiff):
    top = lax.Precision.HIGHEST
    weight_i = weights[None, None, :, None, None, None]
    weight_j = weights[None, None, None, :, None, None]
    weight_k = weights[None, None, None, None, :, None]
    along_x = jnp.einsum("im,abmjkc->abijkc", stiff, values_in, precision=top)
    along_y = jnp.einsum("jm,abimkc->abijkc", stiff, values_in, precision=top)
    along_z = jnp.einsum("km,abijmc->abijkc", stiff, values_in, precision=top)
    return (
        spread(metric, 0) * weight_j * weight_k * along_x
        + spread(metric, 1) * weight_i * weight_k * along_y
        + spread(metric, 2) * weight_i * weight_j * along_z
        + spread(metric, 3) * weight_i * weight_j * weight_k * values_in
    )


def local_diagonal(metric, weights, stiff):
    stiff_diag = np.diagonal(stiff)
    weight_i = weights[None, None, :, None, None, None]
    weight_j = weights[None, None, None, :, None, None]
    weight_k = weights[None, None, None, None, :, None]
    diag_i = stiff_diag[None, None, :, None, None, None]
    diag_j = stiff_diag[None, None, None, :, None, None]
    diag_k = stiff_diag[None, None, None, None, :, None]
    return (
        spread(metric, 0) * diag_i * weight_j * weight_k
        + spread(metric, 1) * weight_i * diag_j * weight_k
        + spread(metric, 2) * weight_i * weight_j * diag_k
        + spread(metric, 3) * weight_i * weight_j * weight_k
    )


def faces(values_in, face_dim):
    last = values_in.shape[face_dim] - 1
    lower = lax.index_in_dim(values_in, 0, face_dim, keepdims=False)
    upper = lax.index_in_dim(values_in, last, face_dim, keepdims=False)
    return (lower, upper)


def combine(values_in, face_dim, elem_dim, lower, upper, before, after):
    total = lower.shape[elem_dim]
    upper_prev = jnp.concatenate(
        [before, lax.slice_in_dim(upper, 0, total - 1, axis=elem_dim)], elem_dim
    )
    lower_next = jnp.concatenate(
        [lax.slice_in_dim(lower, 1, total, axis=elem_dim), after], elem_dim
    )
    middle = lax.slice_in_dim(values_in, 1, values_in.shape[face_dim] - 1, axis=face_dim)
    return jnp.concatenate(
        [
            jnp.expand_dims(lower + upper_prev, face_dim),
            middle,
            jnp.expand_dims(upper + lower_next, face_dim),
        ],
        face_dim,
    )


def assemble(values_in, ride=None):
    lower, upper = faces(values_in, 3)
    rim_faces = jnp.concatenate([lower, upper], 1)
    padded = padded_2(rim_faces, (("ex", 1),), 1)
    values_in = combine(values_in, 3, 1, lower, upper, padded[:, :1], padded[:, 3:])
    lower, upper = faces(values_in, 4)
    rim_faces = jnp.concatenate([lower, upper], 2)
    padded = padded_2(rim_faces, (("ey", 2),), 1)
    if ride is not None:
        padded, ride = lax.optimization_barrier((padded, ride))
    values_in = combine(values_in, 4, 2, lower, upper, padded[:, :, :1], padded[:, :, 3:])
    lower, upper = faces(values_in, 5)
    empty = jnp.zeros_like(upper[..., :1])
    return combine(values_in, 5, 5, lower, upper, empty, empty), ride


def split_parts(values, count):
    parts = []
    rest = values
    for _ in range(count - 1):
        part = lax.reduce_precision(rest, exponent_bits=8, mantissa_bits=7)
        parts.append(part)
        rest = rest - part
    parts.append(lax.reduce_precision(rest, exponent_bits=8, mantissa_bits=7))
    return [part.astype(jnp.bfloat16) for part in parts]


def one_hot(index, count):
    return (index[:, None] == lax.broadcasted_iota(jnp.int32, (1, count), 1)).astype(jnp.bfloat16)


def gather_flat(values, picks, lanes, count=3):
    rows = values.shape[0] // lanes
    table = values.reshape(rows, lanes)
    parts = jnp.concatenate(split_parts(table, count), axis=1)
    hit_row_t = (lax.broadcasted_iota(jnp.int32, (rows, 1), 0) == (picks // lanes)[None, :]).astype(jnp.bfloat16)
    picked = lax.dot_general(parts, hit_row_t, (((0,), (0,)), ((), ())), preferred_element_type=jnp.float32)
    total = picked[:lanes]
    for n in range(1, count):
        total = total + picked[n * lanes : (n + 1) * lanes]
    hit_lane_t = lax.broadcasted_iota(jnp.int32, (lanes, 1), 0) == (picks % lanes)[None, :]
    return jnp.sum(jnp.where(hit_lane_t, total, 0.0), axis=0)


def segment_sum(values, ids, bins, lanes, count=3):
    rows = bins // lanes
    hit_row_t = lax.broadcasted_iota(jnp.int32, (rows, 1), 0) == (ids // lanes)[None, :]
    lhs = jnp.concatenate(
        [jnp.where(hit_row_t, part[None, :], jnp.bfloat16(0)) for part in split_parts(values, count)], axis=0
    )
    sums = jnp.dot(lhs, one_hot(ids % lanes, lanes), preferred_element_type=jnp.float32)
    total = sums[:rows]
    for n in range(1, count):
        total = total + sums[n * rows : (n + 1) * rows]
    return total.reshape(-1)


def strip_reduce(partial, strips, strip_size):
    n_ex = lax.axis_size("ex")
    piece = -(-strip_size // n_ex)
    chunks = partial.reshape(2, strips, strip_size)
    if piece * n_ex != strip_size:
        chunks = jnp.pad(chunks, ((0, 0), (0, 0), (0, piece * n_ex - strip_size)))
    chunks = chunks.reshape(2, strips, n_ex, piece).transpose(2, 1, 0, 3)
    chunks = chunks.reshape(n_ex * strips, 2, piece)
    return lax.all_to_all(chunks, ("ex", "ey"), 0, 0, tiled=True).sum(0)


def strip_gather(mine, strip_size):
    n_ex = lax.axis_size("ex")
    count, piece = mine.shape
    spread_out = jnp.broadcast_to(mine[None], (n_ex, 2, piece))
    whole = lax.all_to_all(spread_out, "ex", 0, 0, tiled=True)
    return whole.transpose(1, 0, 2).reshape(2, n_ex * piece)[:, :strip_size]


def on_device(source, metric, fac_point, fac_strip, fac_shell, fac_area):
    weights, stiff = gll_tables()
    high, low = (2.0, 0.2)
    theta = (high + low) / 2.0
    delta = (high - low) / 2.0
    sigma = theta / delta
    rho_now = 1.0 / sigma
    both, _ = assemble(jnp.stack([source, local_diagonal(metric, weights, stiff)]))
    rhs = both[0]
    pinv = 1.0 / both[1]
    pressure = jnp.zeros_like(source)
    resid = rhs
    update = pinv * resid / theta
    picks = fac_point[0]
    areas = fac_area[0]
    strips = lax.axis_size("ey")
    global_ids = fac_strip[0, :, 0] * SHELL_STRIP + fac_shell[0]
    denom = segment_sum(areas, global_ids, strips * SHELL_STRIP, 256)
    for step in range(SWEEPS):
        pressure = pressure + update
        if step + 2 == SWEEPS:
            early = gather_flat(pressure.reshape(-1), picks, 256)
        applied = element_apply(update, metric, weights, stiff)
        if step + 1 == SWEEPS:
            samples = early + gather_flat(update.reshape(-1), picks, 256, 2)
            numer = segment_sum(areas * samples, global_ids, strips * SHELL_STRIP, 256, 2)
            partial = jnp.stack([numer, denom])
            assembled, mine = assemble(applied[None], strip_reduce(partial, strips, SHELL_STRIP))
        else:
            assembled, _ = assemble(applied[None])
        assembled = assembled[0]
        if step + 2 == SWEEPS:
            assembled, early = lax.optimization_barrier((assembled, early))
        if step == 0:
            assembled, denom = lax.optimization_barrier((assembled, denom))
        resid = resid - assembled
        if step + 1 < SWEEPS:
            rho_new = 1.0 / (2.0 * sigma - rho_now)
            update = rho_new * rho_now * update + 2.0 * rho_new / delta * pinv * resid
            rho_now = rho_new
    total = strip_gather(mine, SHELL_STRIP)
    shell_load = total[0] / jnp.maximum(total[1], 1.0)
    return (pressure, resid, shell_load)


def solution(mesh):
    placed = (
        P("ex", "ey", None, None, None, None),
        P(None, "ex", "ey", None),
        P("ex", "ey"),
        P("ex", "ey", None),
        P("ex", "ey"),
        P("ex", "ey"),
    )
    return jax.shard_map(
        on_device,
        mesh=mesh,
        in_specs=placed,
        out_specs=(
            P("ex", "ey", None, None, None, None),
            P("ex", "ey", None, None, None, None),
            P("ey"),
        ),
        check_vma=False,
    )
```

```python
import jax
import jax.numpy as jnp
import numpy as np
from jax import lax
from jax.sharding import PartitionSpec as P

SWEEPS = 4
SHELL_STRIP = 16384


def padded_2(block, sides, width):
    for axis, dim in sides:
        count = lax.axis_size(axis)
        forward = [(i, i + 1) for i in range(count - 1)]
        backward = [(target, source) for source, target in forward]
        low = lax.ppermute(
            lax.slice_in_dim(block, block.shape[dim] - width, None, axis=dim), axis, forward
        )
        high = lax.ppermute(lax.slice_in_dim(block, 0, width, axis=dim), axis, backward)
        block = jnp.concatenate([low, block, high], axis=dim)
    return block


def gll_tables():
    degree = 7
    points = np.array(
        [
            -1.0,
            -0.8717401485096066,
            -0.5917001814331423,
            -0.2092992179024789,
            0.2092992179024789,
            0.5917001814331423,
            0.8717401485096066,
            1.0,
        ]
    )
    previous = points * 0.0 + 1.0
    current = points * 1.0
    for order in range(1, degree):
        following = ((2 * order + 1) * points * current - order * previous) / (order + 1)
        previous = current
        current = following
    weights = 2.0 / (degree * (degree + 1) * current**2)
    count = degree + 1
    same = np.array([[1.0 if row == col else 0.0 for col in range(count)] for row in range(count)])
    between = points[:, None] - points[None, :] + same
    deriv = current[:, None] / current[None, :] / between * (1.0 - same)
    deriv[0, 0] = -degree * (degree + 1) / 4.0
    deriv[-1, -1] = degree * (degree + 1) / 4.0
    stiff = deriv.T @ (weights[:, None] * deriv)
    return (np.asarray(weights, np.float32), np.asarray(stiff, np.float32))


def spread(metric, which):
    return metric[which][:, :, None, None, None, :]


def element_apply(values_in, metric, weights, stiff):
    top = lax.Precision.HIGHEST
    weight_i = weights[None, None, :, None, None, None]
    weight_j = weights[None, None, None, :, None, None]
    weight_k = weights[None, None, None, None, :, None]
    along_x = jnp.einsum("im,abmjkc->abijkc", stiff, values_in, precision=top)
    along_y = jnp.einsum("jm,abimkc->abijkc", stiff, values_in, precision=top)
    along_z = jnp.einsum("km,abijmc->abijkc", stiff, values_in, precision=top)
    return (
        spread(metric, 0) * weight_j * weight_k * along_x
        + spread(metric, 1) * weight_i * weight_k * along_y
        + spread(metric, 2) * weight_i * weight_j * along_z
        + spread(metric, 3) * weight_i * weight_j * weight_k * values_in
    )


def local_diagonal(metric, weights, stiff):
    stiff_diag = np.diagonal(stiff)
    weight_i = weights[None, None, :, None, None, None]
    weight_j = weights[None, None, None, :, None, None]
    weight_k = weights[None, None, None, None, :, None]
    diag_i = stiff_diag[None, None, :, None, None, None]
    diag_j = stiff_diag[None, None, None, :, None, None]
    diag_k = stiff_diag[None, None, None, None, :, None]
    return (
        spread(metric, 0) * diag_i * weight_j * weight_k
        + spread(metric, 1) * weight_i * diag_j * weight_k
        + spread(metric, 2) * weight_i * weight_j * diag_k
        + spread(metric, 3) * weight_i * weight_j * weight_k
    )


def faces(values_in, face_dim):
    last = values_in.shape[face_dim] - 1
    lower = lax.index_in_dim(values_in, 0, face_dim, keepdims=False)
    upper = lax.index_in_dim(values_in, last, face_dim, keepdims=False)
    return (lower, upper)


def combine(values_in, face_dim, elem_dim, lower, upper, before, after):
    total = lower.shape[elem_dim]
    upper_prev = jnp.concatenate(
        [before, lax.slice_in_dim(upper, 0, total - 1, axis=elem_dim)], elem_dim
    )
    lower_next = jnp.concatenate(
        [lax.slice_in_dim(lower, 1, total, axis=elem_dim), after], elem_dim
    )
    middle = lax.slice_in_dim(values_in, 1, values_in.shape[face_dim] - 1, axis=face_dim)
    return jnp.concatenate(
        [
            jnp.expand_dims(lower + upper_prev, face_dim),
            middle,
            jnp.expand_dims(upper + lower_next, face_dim),
        ],
        face_dim,
    )


def assemble(values_in, ride=None):
    lower, upper = faces(values_in, 3)
    rim_faces = jnp.concatenate([lower, upper], 1)
    padded = padded_2(rim_faces, (("ex", 1),), 1)
    if ride is not None:
        padded, ride = lax.optimization_barrier((padded, ride))
    values_in = combine(values_in, 3, 1, lower, upper, padded[:, :1], padded[:, 3:])
    lower, upper = faces(values_in, 4)
    rim_faces = jnp.concatenate([lower, upper], 2)
    padded = padded_2(rim_faces, (("ey", 2),), 1)
    values_in = combine(values_in, 4, 2, lower, upper, padded[:, :, :1], padded[:, :, 3:])
    lower, upper = faces(values_in, 5)
    empty = jnp.zeros_like(upper[..., :1])
    return combine(values_in, 5, 5, lower, upper, empty, empty), ride


def split_parts(values, count):
    parts = []
    rest = values
    for _ in range(count - 1):
        part = lax.reduce_precision(rest, exponent_bits=8, mantissa_bits=7)
        parts.append(part)
        rest = rest - part
    parts.append(lax.reduce_precision(rest, exponent_bits=8, mantissa_bits=7))
    return [part.astype(jnp.bfloat16) for part in parts]


def one_hot(index, count):
    return (index[:, None] == lax.broadcasted_iota(jnp.int32, (1, count), 1)).astype(jnp.bfloat16)


def gather_flat(values, picks, lanes, count=3):
    rows = values.shape[0] // lanes
    table = values.reshape(rows, lanes)
    parts = jnp.concatenate(split_parts(table, count), axis=1)
    hit_row_t = (lax.broadcasted_iota(jnp.int32, (rows, 1), 0) == (picks // lanes)[None, :]).astype(jnp.bfloat16)
    picked = lax.dot_general(parts, hit_row_t, (((0,), (0,)), ((), ())), preferred_element_type=jnp.float32)
    total = picked[:lanes]
    for n in range(1, count):
        total = total + picked[n * lanes : (n + 1) * lanes]
    hit_lane_t = lax.broadcasted_iota(jnp.int32, (lanes, 1), 0) == (picks % lanes)[None, :]
    return jnp.sum(jnp.where(hit_lane_t, total, 0.0), axis=0)


def segment_sum(values, ids, bins, lanes, count=3):
    rows = -(-bins // lanes)
    hit_row_t = lax.broadcasted_iota(jnp.int32, (rows, 1), 0) == (ids // lanes)[None, :]
    lhs = jnp.concatenate(
        [jnp.where(hit_row_t, part[None, :], jnp.bfloat16(0)) for part in split_parts(values, count)], axis=0
    )
    sums = jnp.dot(lhs, one_hot(ids % lanes, lanes), preferred_element_type=jnp.float32)
    total = sums[:rows]
    for n in range(1, count):
        total = total + sums[n * rows : (n + 1) * rows]
    return total.reshape(-1)[:bins]


def chunk_ids(ids, strips, strip_size):
    n_ex = lax.axis_size("ex")
    piece = -(-strip_size // n_ex)
    strip, offset = ids // strip_size, ids % strip_size
    return ((offset // piece) * strips + strip) * piece + offset % piece, n_ex * strips * piece


def strip_reduce(partial, strips, strip_size):
    n_ex = lax.axis_size("ex")
    piece = -(-strip_size // n_ex)
    chunks = partial.reshape(2, n_ex * strips, piece)
    if piece % 128:
        chunks = chunks.transpose(1, 0, 2)
        return lax.all_to_all(chunks, ("ex", "ey"), 0, 0, tiled=True).sum(0)
    return lax.all_to_all(chunks, ("ex", "ey"), 1, 1, tiled=True).sum(1)


def strip_gather(mine, strip_size):
    n_ex = lax.axis_size("ex")
    count, piece = mine.shape
    spread_out = jnp.broadcast_to(mine[None], (n_ex, 2, piece))
    whole = lax.all_to_all(spread_out, "ex", 0, 0, tiled=True)
    return whole.transpose(1, 0, 2).reshape(2, n_ex * piece)[:, :strip_size]


def on_device(source, metric, fac_point, fac_strip, fac_shell, fac_area):
    weights, stiff = gll_tables()
    high, low = (2.0, 0.2)
    theta = (high + low) / 2.0
    delta = (high - low) / 2.0
    sigma = theta / delta
    rho_now = 1.0 / sigma
    both, _ = assemble(jnp.stack([source, local_diagonal(metric, weights, stiff)]))
    rhs = both[0]
    pinv = 1.0 / both[1]
    pressure = jnp.zeros_like(source)
    resid = rhs
    update = pinv * resid / theta
    picks = fac_point[0]
    areas = fac_area[0]
    strips = lax.axis_size("ey")
    global_ids, bins = chunk_ids(fac_strip[0, :, 0] * SHELL_STRIP + fac_shell[0], strips, SHELL_STRIP)
    lanes = 128 * int(np.ceil(np.sqrt(bins) / 128))
    denom = segment_sum(areas, global_ids, bins, lanes)
    for step in range(SWEEPS):
        pressure = pressure + update
        if step + 2 == SWEEPS:
            early = gather_flat(pressure.reshape(-1), picks, 256)
        applied = element_apply(update, metric, weights, stiff)
        if step + 1 == SWEEPS:
            samples = early + gather_flat(update.reshape(-1), picks, 256, 2)
            numer = segment_sum(areas * samples, global_ids, bins, lanes, 2)
            partial = jnp.stack([numer, denom])
            assembled, mine = assemble(applied[None], strip_reduce(partial, strips, SHELL_STRIP))
        else:
            assembled, _ = assemble(applied[None])
        assembled = assembled[0]
        if step + 2 == SWEEPS:
            assembled, early = lax.optimization_barrier((assembled, early))
        if step == 0:
            assembled, denom = lax.optimization_barrier((assembled, denom))
        resid = resid - assembled
        if step + 1 < SWEEPS:
            rho_new = 1.0 / (2.0 * sigma - rho_now)
            update = rho_new * rho_now * update + 2.0 * rho_new / delta * pinv * resid
            rho_now = rho_new
    total = strip_gather(mine, SHELL_STRIP)
    shell_load = total[0] / jnp.maximum(total[1], 1.0)
    return (pressure, resid, shell_load)


def solution(mesh):
    placed = (
        P("ex", "ey", None, None, None, None),
        P(None, "ex", "ey", None),
        P("ex", "ey"),
        P("ex", "ey", None),
        P("ex", "ey"),
        P("ex", "ey"),
    )
    return jax.shard_map(
        on_device,
        mesh=mesh,
        in_specs=placed,
        out_specs=(
            P("ex", "ey", None, None, None, None),
            P("ex", "ey", None, None, None, None),
            P("ey"),
        ),
        check_vma=False,
    )
```

```python
import jax
import jax.numpy as jnp
import numpy as np
from jax import lax
from jax.sharding import PartitionSpec as P

SWEEPS = 4
SHELL_STRIP = 16384


def padded_2(block, sides, width):
    for axis, dim in sides:
        count = lax.axis_size(axis)
        forward = [(i, i + 1) for i in range(count - 1)]
        backward = [(target, source) for source, target in forward]
        low = lax.ppermute(
            lax.slice_in_dim(block, block.shape[dim] - width, None, axis=dim), axis, forward
        )
        high = lax.ppermute(lax.slice_in_dim(block, 0, width, axis=dim), axis, backward)
        block = jnp.concatenate([low, block, high], axis=dim)
    return block


def gll_tables():
    degree = 7
    points = np.array(
        [
            -1.0,
            -0.8717401485096066,
            -0.5917001814331423,
            -0.2092992179024789,
            0.2092992179024789,
            0.5917001814331423,
            0.8717401485096066,
            1.0,
        ]
    )
    previous = points * 0.0 + 1.0
    current = points * 1.0
    for order in range(1, degree):
        following = ((2 * order + 1) * points * current - order * previous) / (order + 1)
        previous = current
        current = following
    weights = 2.0 / (degree * (degree + 1) * current**2)
    count = degree + 1
    same = np.array([[1.0 if row == col else 0.0 for col in range(count)] for row in range(count)])
    between = points[:, None] - points[None, :] + same
    deriv = current[:, None] / current[None, :] / between * (1.0 - same)
    deriv[0, 0] = -degree * (degree + 1) / 4.0
    deriv[-1, -1] = degree * (degree + 1) / 4.0
    stiff = deriv.T @ (weights[:, None] * deriv)
    return (np.asarray(weights, np.float32), np.asarray(stiff, np.float32))


def spread(metric, which):
    return metric[which][:, :, None, None, None, :]


def element_apply(values_in, metric, weights, stiff):
    top = lax.Precision.HIGHEST
    weight_i = weights[None, None, :, None, None, None]
    weight_j = weights[None, None, None, :, None, None]
    weight_k = weights[None, None, None, None, :, None]
    along_x = jnp.einsum("im,abmjkc->abijkc", stiff, values_in, precision=top)
    along_y = jnp.einsum("jm,abimkc->abijkc", stiff, values_in, precision=top)
    along_z = jnp.einsum("km,abijmc->abijkc", stiff, values_in, precision=top)
    return (
        spread(metric, 0) * weight_j * weight_k * along_x
        + spread(metric, 1) * weight_i * weight_k * along_y
        + spread(metric, 2) * weight_i * weight_j * along_z
        + spread(metric, 3) * weight_i * weight_j * weight_k * values_in
    )


def x_faces_apply(values_in, metric, weights, stiff):
    top = lax.Precision.HIGHEST
    last = values_in.shape[2] - 1
    weight_j = weights[None, None, :, None, None]
    weight_k = weights[None, None, None, :, None]
    out = []
    for edge in (0, last):
        plane = values_in[:, :, edge]
        along_x = jnp.einsum("m,abmjkc->abjkc", stiff[edge], values_in, precision=top)
        along_y = jnp.einsum("jm,abmkc->abjkc", stiff, plane, precision=top)
        along_z = jnp.einsum("km,abjmc->abjkc", stiff, plane, precision=top)
        weight_i = weights[edge]
        out.append(
            metric[0][:, :, None, None, :] * weight_j * weight_k * along_x
            + metric[1][:, :, None, None, :] * weight_i * weight_k * along_y
            + metric[2][:, :, None, None, :] * weight_i * weight_j * along_z
            + metric[3][:, :, None, None, :] * weight_i * weight_j * weight_k * plane
        )
    return out


def local_diagonal(metric, weights, stiff):
    stiff_diag = np.diagonal(stiff)
    weight_i = weights[None, None, :, None, None, None]
    weight_j = weights[None, None, None, :, None, None]
    weight_k = weights[None, None, None, None, :, None]
    diag_i = stiff_diag[None, None, :, None, None, None]
    diag_j = stiff_diag[None, None, None, :, None, None]
    diag_k = stiff_diag[None, None, None, None, :, None]
    return (
        spread(metric, 0) * diag_i * weight_j * weight_k
        + spread(metric, 1) * weight_i * diag_j * weight_k
        + spread(metric, 2) * weight_i * weight_j * diag_k
        + spread(metric, 3) * weight_i * weight_j * weight_k
    )


def faces(values_in, face_dim):
    last = values_in.shape[face_dim] - 1
    lower = lax.index_in_dim(values_in, 0, face_dim, keepdims=False)
    upper = lax.index_in_dim(values_in, last, face_dim, keepdims=False)
    return (lower, upper)


def combine(values_in, face_dim, elem_dim, lower, upper, before, after):
    total = lower.shape[elem_dim]
    upper_prev = jnp.concatenate(
        [before, lax.slice_in_dim(upper, 0, total - 1, axis=elem_dim)], elem_dim
    )
    lower_next = jnp.concatenate(
        [lax.slice_in_dim(lower, 1, total, axis=elem_dim), after], elem_dim
    )
    middle = lax.slice_in_dim(values_in, 1, values_in.shape[face_dim] - 1, axis=face_dim)
    return jnp.concatenate(
        [
            jnp.expand_dims(lower + upper_prev, face_dim),
            middle,
            jnp.expand_dims(upper + lower_next, face_dim),
        ],
        face_dim,
    )


def assemble(values_in, ride=None, x_faces=None):
    lower, upper = faces(values_in, 3) if x_faces is None else x_faces
    rim_faces = jnp.concatenate([lower, upper], 1)
    padded = padded_2(rim_faces, (("ex", 1),), 1)
    if ride is not None:
        padded, ride = lax.optimization_barrier((padded, ride))
    values_in = combine(values_in, 3, 1, lower, upper, padded[:, :1], padded[:, 3:])
    lower, upper = faces(values_in, 4)
    rim_faces = jnp.concatenate([lower, upper], 2)
    padded = padded_2(rim_faces, (("ey", 2),), 1)
    values_in = combine(values_in, 4, 2, lower, upper, padded[:, :, :1], padded[:, :, 3:])
    lower, upper = faces(values_in, 5)
    empty = jnp.zeros_like(upper[..., :1])
    return combine(values_in, 5, 5, lower, upper, empty, empty), ride


def split_parts(values, count):
    parts = []
    rest = values
    for _ in range(count - 1):
        part = lax.reduce_precision(rest, exponent_bits=8, mantissa_bits=7)
        parts.append(part)
        rest = rest - part
    parts.append(lax.reduce_precision(rest, exponent_bits=8, mantissa_bits=7))
    return [part.astype(jnp.bfloat16) for part in parts]


def one_hot(index, count):
    return (index[:, None] == lax.broadcasted_iota(jnp.int32, (1, count), 1)).astype(jnp.bfloat16)


def gather_flat(values, picks, lanes, count=3):
    rows = values.shape[0] // lanes
    table = values.reshape(rows, lanes)
    parts = jnp.concatenate(split_parts(table, count), axis=1)
    hit_row_t = (lax.broadcasted_iota(jnp.int32, (rows, 1), 0) == (picks // lanes)[None, :]).astype(jnp.bfloat16)
    picked = lax.dot_general(parts, hit_row_t, (((0,), (0,)), ((), ())), preferred_element_type=jnp.float32)
    total = picked[:lanes]
    for n in range(1, count):
        total = total + picked[n * lanes : (n + 1) * lanes]
    hit_lane_t = lax.broadcasted_iota(jnp.int32, (lanes, 1), 0) == (picks % lanes)[None, :]
    return jnp.sum(jnp.where(hit_lane_t, total, 0.0), axis=0)


def segment_sum(values, ids, bins, lanes, count=3):
    rows = bins // lanes
    hit_row_t = lax.broadcasted_iota(jnp.int32, (rows, 1), 0) == (ids // lanes)[None, :]
    lhs = jnp.concatenate(
        [jnp.where(hit_row_t, part[None, :], jnp.bfloat16(0)) for part in split_parts(values, count)], axis=0
    )
    sums = jnp.dot(lhs, one_hot(ids % lanes, lanes), preferred_element_type=jnp.float32)
    total = sums[:rows]
    for n in range(1, count):
        total = total + sums[n * rows : (n + 1) * rows]
    return total.reshape(-1)


def strip_reduce(partial, strips, strip_size):
    n_ex = lax.axis_size("ex")
    piece = -(-strip_size // n_ex)
    chunks = partial.reshape(2, strips, strip_size)
    if piece * n_ex != strip_size:
        chunks = jnp.pad(chunks, ((0, 0), (0, 0), (0, piece * n_ex - strip_size)))
    chunks = chunks.reshape(2, strips, n_ex, piece).transpose(2, 1, 0, 3)
    chunks = chunks.reshape(n_ex * strips, 2, piece)
    return lax.all_to_all(chunks, ("ex", "ey"), 0, 0, tiled=True).sum(0)


def strip_gather(mine, strip_size):
    n_ex = lax.axis_size("ex")
    count, piece = mine.shape
    spread_out = jnp.broadcast_to(mine[None], (n_ex, 2, piece))
    whole = lax.all_to_all(spread_out, "ex", 0, 0, tiled=True)
    return whole.transpose(1, 0, 2).reshape(2, n_ex * piece)[:, :strip_size]


def on_device(source, metric, fac_point, fac_strip, fac_shell, fac_area):
    weights, stiff = gll_tables()
    high, low = (2.0, 0.2)
    theta = (high + low) / 2.0
    delta = (high - low) / 2.0
    sigma = theta / delta
    rho_now = 1.0 / sigma
    both, _ = assemble(jnp.stack([source, local_diagonal(metric, weights, stiff)]))
    rhs = both[0]
    pinv = 1.0 / both[1]
    pressure = jnp.zeros_like(source)
    resid = rhs
    update = pinv * resid / theta
    picks = fac_point[0]
    areas = fac_area[0]
    strips = lax.axis_size("ey")
    global_ids = fac_strip[0, :, 0] * SHELL_STRIP + fac_shell[0]
    denom = segment_sum(areas, global_ids, strips * SHELL_STRIP, 256)
    for step in range(SWEEPS):
        pressure = pressure + update
        if step + 2 == SWEEPS:
            early = gather_flat(pressure.reshape(-1), picks, 256)
        applied = element_apply(update, metric, weights, stiff)
        x_faces = [face[None] for face in x_faces_apply(update, metric, weights, stiff)]
        if step + 1 == SWEEPS:
            samples = early + gather_flat(update.reshape(-1), picks, 256, 2)
            numer = segment_sum(areas * samples, global_ids, strips * SHELL_STRIP, 256, 2)
            partial = jnp.stack([numer, denom])
            assembled, mine = assemble(applied[None], strip_reduce(partial, strips, SHELL_STRIP), x_faces)
        else:
            assembled, _ = assemble(applied[None], None, x_faces)
        assembled = assembled[0]
        if step + 2 == SWEEPS:
            assembled, early = lax.optimization_barrier((assembled, early))
        if step == 0:
            assembled, denom = lax.optimization_barrier((assembled, denom))
        resid = resid - assembled
        if step + 1 < SWEEPS:
            rho_new = 1.0 / (2.0 * sigma - rho_now)
            update = rho_new * rho_now * update + 2.0 * rho_new / delta * pinv * resid
            rho_now = rho_new
    total = strip_gather(mine, SHELL_STRIP)
    shell_load = total[0] / jnp.maximum(total[1], 1.0)
    return (pressure, resid, shell_load)


def solution(mesh):
    placed = (
        P("ex", "ey", None, None, None, None),
        P(None, "ex", "ey", None),
        P("ex", "ey"),
        P("ex", "ey", None),
        P("ex", "ey"),
        P("ex", "ey"),
    )
    return jax.shard_map(
        on_device,
        mesh=mesh,
        in_specs=placed,
        out_specs=(
            P("ex", "ey", None, None, None, None),
            P("ex", "ey", None, None, None, None),
            P("ey"),
        ),
        check_vma=False,
    )
```

```python
import jax
import jax.numpy as jnp
import numpy as np
from jax import lax
from jax.sharding import PartitionSpec as P

SWEEPS = 4
SHELL_STRIP = 16384


def padded_2(block, sides, width):
    for axis, dim in sides:
        count = lax.axis_size(axis)
        forward = [(i, i + 1) for i in range(count - 1)]
        backward = [(target, source) for source, target in forward]
        low = lax.ppermute(
            lax.slice_in_dim(block, block.shape[dim] - width, None, axis=dim), axis, forward
        )
        high = lax.ppermute(lax.slice_in_dim(block, 0, width, axis=dim), axis, backward)
        block = jnp.concatenate([low, block, high], axis=dim)
    return block


def gll_tables():
    degree = 7
    points = np.array(
        [
            -1.0,
            -0.8717401485096066,
            -0.5917001814331423,
            -0.2092992179024789,
            0.2092992179024789,
            0.5917001814331423,
            0.8717401485096066,
            1.0,
        ]
    )
    previous = points * 0.0 + 1.0
    current = points * 1.0
    for order in range(1, degree):
        following = ((2 * order + 1) * points * current - order * previous) / (order + 1)
        previous = current
        current = following
    weights = 2.0 / (degree * (degree + 1) * current**2)
    count = degree + 1
    same = np.array([[1.0 if row == col else 0.0 for col in range(count)] for row in range(count)])
    between = points[:, None] - points[None, :] + same
    deriv = current[:, None] / current[None, :] / between * (1.0 - same)
    deriv[0, 0] = -degree * (degree + 1) / 4.0
    deriv[-1, -1] = degree * (degree + 1) / 4.0
    stiff = deriv.T @ (weights[:, None] * deriv)
    return (np.asarray(weights, np.float32), np.asarray(stiff, np.float32))


def spread(metric, which):
    return metric[which][:, :, None, None, None, :]


def element_apply(values_in, metric, weights, stiff):
    top = lax.Precision.HIGHEST
    weight_i = weights[None, None, :, None, None, None]
    weight_j = weights[None, None, None, :, None, None]
    weight_k = weights[None, None, None, None, :, None]
    along_x = jnp.einsum("im,abmjkc->abijkc", stiff, values_in, precision=top)
    along_y = jnp.einsum("jm,abimkc->abijkc", stiff, values_in, precision=top)
    along_z = jnp.einsum("km,abijmc->abijkc", stiff, values_in, precision=top)
    return (
        spread(metric, 0) * weight_j * weight_k * along_x
        + spread(metric, 1) * weight_i * weight_k * along_y
        + spread(metric, 2) * weight_i * weight_j * along_z
        + spread(metric, 3) * weight_i * weight_j * weight_k * values_in
    )


def local_diagonal(metric, weights, stiff):
    stiff_diag = np.diagonal(stiff)
    weight_i = weights[None, None, :, None, None, None]
    weight_j = weights[None, None, None, :, None, None]
    weight_k = weights[None, None, None, None, :, None]
    diag_i = stiff_diag[None, None, :, None, None, None]
    diag_j = stiff_diag[None, None, None, :, None, None]
    diag_k = stiff_diag[None, None, None, None, :, None]
    return (
        spread(metric, 0) * diag_i * weight_j * weight_k
        + spread(metric, 1) * weight_i * diag_j * weight_k
        + spread(metric, 2) * weight_i * weight_j * diag_k
        + spread(metric, 3) * weight_i * weight_j * weight_k
    )


def faces(values_in, face_dim):
    last = values_in.shape[face_dim] - 1
    lower = lax.index_in_dim(values_in, 0, face_dim, keepdims=False)
    upper = lax.index_in_dim(values_in, last, face_dim, keepdims=False)
    return (lower, upper)


def combine(values_in, face_dim, elem_dim, lower, upper, before, after):
    total = lower.shape[elem_dim]
    upper_prev = jnp.concatenate(
        [before, lax.slice_in_dim(upper, 0, total - 1, axis=elem_dim)], elem_dim
    )
    lower_next = jnp.concatenate(
        [lax.slice_in_dim(lower, 1, total, axis=elem_dim), after], elem_dim
    )
    middle = lax.slice_in_dim(values_in, 1, values_in.shape[face_dim] - 1, axis=face_dim)
    return jnp.concatenate(
        [
            jnp.expand_dims(lower + upper_prev, face_dim),
            middle,
            jnp.expand_dims(upper + lower_next, face_dim),
        ],
        face_dim,
    )


def assemble(values_in, ride=None):
    lower, upper = faces(values_in, 3)
    rim_faces = jnp.concatenate([lower, upper], 1)
    padded = padded_2(rim_faces, (("ex", 1),), 1)
    if ride is not None:
        padded, ride = lax.optimization_barrier((padded, ride))
    values_in = combine(values_in, 3, 1, lower, upper, padded[:, :1], padded[:, 3:])
    lower, upper = faces(values_in, 4)
    rim_faces = jnp.concatenate([lower, upper], 2)
    padded = padded_2(rim_faces, (("ey", 2),), 1)
    values_in = combine(values_in, 4, 2, lower, upper, padded[:, :, :1], padded[:, :, 3:])
    lower, upper = faces(values_in, 5)
    empty = jnp.zeros_like(upper[..., :1])
    return combine(values_in, 5, 5, lower, upper, empty, empty), ride


def split_parts(values, count):
    parts = []
    rest = values
    for _ in range(count - 1):
        part = lax.reduce_precision(rest, exponent_bits=8, mantissa_bits=7)
        parts.append(part)
        rest = rest - part
    parts.append(lax.reduce_precision(rest, exponent_bits=8, mantissa_bits=7))
    return [part.astype(jnp.bfloat16) for part in parts]


def one_hot(index, count):
    return (index[:, None] == lax.broadcasted_iota(jnp.int32, (1, count), 1)).astype(jnp.bfloat16)


def gather_flat(values, picks, lanes, count=3):
    rows = values.shape[0] // lanes
    table = values.reshape(rows, lanes)
    parts = jnp.concatenate(split_parts(table, count), axis=1)
    hit_row_t = (lax.broadcasted_iota(jnp.int32, (rows, 1), 0) == (picks // lanes)[None, :]).astype(jnp.bfloat16)
    picked = lax.dot_general(parts, hit_row_t, (((0,), (0,)), ((), ())), preferred_element_type=jnp.float32)
    total = picked[:lanes]
    for n in range(1, count):
        total = total + picked[n * lanes : (n + 1) * lanes]
    hit_lane_t = lax.broadcasted_iota(jnp.int32, (lanes, 1), 0) == (picks % lanes)[None, :]
    return jnp.sum(jnp.where(hit_lane_t, total, 0.0), axis=0)


def segment_sum(values, ids, bins, lanes, count=3):
    rows = bins // lanes
    hit_row_t = lax.broadcasted_iota(jnp.int32, (rows, 1), 0) == (ids // lanes)[None, :]
    lhs = jnp.concatenate(
        [jnp.where(hit_row_t, part[None, :], jnp.bfloat16(0)) for part in split_parts(values, count)], axis=0
    )
    sums = jnp.dot(lhs, one_hot(ids % lanes, lanes), preferred_element_type=jnp.float32)
    total = sums[:rows]
    for n in range(1, count):
        total = total + sums[n * rows : (n + 1) * rows]
    return total.reshape(-1)


def strip_reduce(partial, strips, strip_size):
    n_ex = lax.axis_size("ex")
    piece = -(-strip_size // n_ex)
    chunks = partial.reshape(2, strips, strip_size)
    if piece * n_ex != strip_size:
        chunks = jnp.pad(chunks, ((0, 0), (0, 0), (0, piece * n_ex - strip_size)))
    chunks = chunks.reshape(2, strips, n_ex, piece).transpose(2, 1, 0, 3)
    chunks = chunks.reshape(n_ex * strips, 2, piece)
    return lax.all_to_all(chunks, ("ex", "ey"), 0, 0, tiled=True).sum(0)


def strip_gather(mine, strip_size):
    n_ex = lax.axis_size("ex")
    count, piece = mine.shape
    spread_out = jnp.broadcast_to(mine[:, None], (2, n_ex, piece))
    whole = lax.all_to_all(spread_out, "ex", 1, 1, tiled=True)
    return whole.reshape(2, n_ex * piece)[:, :strip_size]


def on_device(source, metric, fac_point, fac_strip, fac_shell, fac_area):
    weights, stiff = gll_tables()
    high, low = (2.0, 0.2)
    theta = (high + low) / 2.0
    delta = (high - low) / 2.0
    sigma = theta / delta
    rho_now = 1.0 / sigma
    both, _ = assemble(jnp.stack([source, local_diagonal(metric, weights, stiff)]))
    rhs = both[0]
    pinv = 1.0 / both[1]
    pressure = jnp.zeros_like(source)
    resid = rhs
    update = pinv * resid / theta
    picks = fac_point[0]
    areas = fac_area[0]
    strips = lax.axis_size("ey")
    global_ids = fac_strip[0, :, 0] * SHELL_STRIP + fac_shell[0]
    denom = segment_sum(areas, global_ids, strips * SHELL_STRIP, 256)
    for step in range(SWEEPS):
        pressure = pressure + update
        if step + 2 == SWEEPS:
            early = gather_flat(pressure.reshape(-1), picks, 256)
        applied = element_apply(update, metric, weights, stiff)
        if step + 1 == SWEEPS:
            samples = early + gather_flat(update.reshape(-1), picks, 256, 2)
            numer = segment_sum(areas * samples, global_ids, strips * SHELL_STRIP, 256, 2)
            partial = jnp.stack([numer, denom])
            assembled, mine = assemble(applied[None], strip_reduce(partial, strips, SHELL_STRIP))
        else:
            assembled, _ = assemble(applied[None])
        assembled = assembled[0]
        if step + 2 == SWEEPS:
            assembled, early = lax.optimization_barrier((assembled, early))
        if step == 0:
            assembled, denom = lax.optimization_barrier((assembled, denom))
        resid = resid - assembled
        if step + 1 < SWEEPS:
            rho_new = 1.0 / (2.0 * sigma - rho_now)
            update = rho_new * rho_now * update + 2.0 * rho_new / delta * pinv * resid
            rho_now = rho_new
    total = strip_gather(mine, SHELL_STRIP)
    shell_load = total[0] / jnp.maximum(total[1], 1.0)
    return (pressure, resid, shell_load)


def solution(mesh):
    placed = (
        P("ex", "ey", None, None, None, None),
        P(None, "ex", "ey", None),
        P("ex", "ey"),
        P("ex", "ey", None),
        P("ex", "ey"),
        P("ex", "ey"),
    )
    return jax.shard_map(
        on_device,
        mesh=mesh,
        in_specs=placed,
        out_specs=(
            P("ex", "ey", None, None, None, None),
            P("ex", "ey", None, None, None, None),
            P("ey"),
        ),
        check_vma=False,
    )
```

```python
import jax
import jax.numpy as jnp
import numpy as np
from jax import lax
from jax.sharding import PartitionSpec as P

SWEEPS = 4
SHELL_STRIP = 16384


def padded_2(block, sides, width):
    for axis, dim in sides:
        count = lax.axis_size(axis)
        forward = [(i, i + 1) for i in range(count - 1)]
        backward = [(target, source) for source, target in forward]
        low = lax.ppermute(
            lax.slice_in_dim(block, block.shape[dim] - width, None, axis=dim), axis, forward
        )
        high = lax.ppermute(lax.slice_in_dim(block, 0, width, axis=dim), axis, backward)
        block = jnp.concatenate([low, block, high], axis=dim)
    return block


def gll_tables():
    degree = 7
    points = np.array(
        [
            -1.0,
            -0.8717401485096066,
            -0.5917001814331423,
            -0.2092992179024789,
            0.2092992179024789,
            0.5917001814331423,
            0.8717401485096066,
            1.0,
        ]
    )
    previous = points * 0.0 + 1.0
    current = points * 1.0
    for order in range(1, degree):
        following = ((2 * order + 1) * points * current - order * previous) / (order + 1)
        previous = current
        current = following
    weights = 2.0 / (degree * (degree + 1) * current**2)
    count = degree + 1
    same = np.array([[1.0 if row == col else 0.0 for col in range(count)] for row in range(count)])
    between = points[:, None] - points[None, :] + same
    deriv = current[:, None] / current[None, :] / between * (1.0 - same)
    deriv[0, 0] = -degree * (degree + 1) / 4.0
    deriv[-1, -1] = degree * (degree + 1) / 4.0
    stiff = deriv.T @ (weights[:, None] * deriv)
    return (np.asarray(weights, np.float32), np.asarray(stiff, np.float32))


def spread(metric, which):
    return metric[which][:, :, None, None, None, :]


def element_apply(values_in, metric, weights, stiff):
    top = lax.Precision.HIGHEST
    weight_i = weights[None, None, :, None, None, None]
    weight_j = weights[None, None, None, :, None, None]
    weight_k = weights[None, None, None, None, :, None]
    along_x = jnp.einsum("im,abmjkc->abijkc", stiff, values_in, precision=top)
    along_y = jnp.einsum("jm,abimkc->abijkc", stiff, values_in, precision=top)
    along_z = jnp.einsum("km,abijmc->abijkc", stiff, values_in, precision=top)
    return (
        spread(metric, 0) * weight_j * weight_k * along_x
        + spread(metric, 1) * weight_i * weight_k * along_y
        + spread(metric, 2) * weight_i * weight_j * along_z
        + spread(metric, 3) * weight_i * weight_j * weight_k * values_in
    )


def local_diagonal(metric, weights, stiff):
    stiff_diag = np.diagonal(stiff)
    weight_i = weights[None, None, :, None, None, None]
    weight_j = weights[None, None, None, :, None, None]
    weight_k = weights[None, None, None, None, :, None]
    diag_i = stiff_diag[None, None, :, None, None, None]
    diag_j = stiff_diag[None, None, None, :, None, None]
    diag_k = stiff_diag[None, None, None, None, :, None]
    return (
        spread(metric, 0) * diag_i * weight_j * weight_k
        + spread(metric, 1) * weight_i * diag_j * weight_k
        + spread(metric, 2) * weight_i * weight_j * diag_k
        + spread(metric, 3) * weight_i * weight_j * weight_k
    )


def faces(values_in, face_dim):
    last = values_in.shape[face_dim] - 1
    lower = lax.index_in_dim(values_in, 0, face_dim, keepdims=False)
    upper = lax.index_in_dim(values_in, last, face_dim, keepdims=False)
    return (lower, upper)


def combine(values_in, face_dim, elem_dim, lower, upper, before, after):
    total = lower.shape[elem_dim]
    upper_prev = jnp.concatenate(
        [before, lax.slice_in_dim(upper, 0, total - 1, axis=elem_dim)], elem_dim
    )
    lower_next = jnp.concatenate(
        [lax.slice_in_dim(lower, 1, total, axis=elem_dim), after], elem_dim
    )
    middle = lax.slice_in_dim(values_in, 1, values_in.shape[face_dim] - 1, axis=face_dim)
    return jnp.concatenate(
        [
            jnp.expand_dims(lower + upper_prev, face_dim),
            middle,
            jnp.expand_dims(upper + lower_next, face_dim),
        ],
        face_dim,
    )


def assemble(values_in, ride=None, then=None):
    lower, upper = faces(values_in, 3)
    rim_faces = jnp.concatenate([lower, upper], 1)
    padded = padded_2(rim_faces, (("ex", 1),), 1)
    if ride is not None:
        padded, ride = lax.optimization_barrier((padded, ride))
    values_in = combine(values_in, 3, 1, lower, upper, padded[:, :1], padded[:, 3:])
    lower, upper = faces(values_in, 4)
    rim_faces = jnp.concatenate([lower, upper], 2)
    if then is not None:
        ride = then(ride)
        rim_faces, ride = lax.optimization_barrier((rim_faces, ride))
    padded = padded_2(rim_faces, (("ey", 2),), 1)
    values_in = combine(values_in, 4, 2, lower, upper, padded[:, :, :1], padded[:, :, 3:])
    lower, upper = faces(values_in, 5)
    empty = jnp.zeros_like(upper[..., :1])
    return combine(values_in, 5, 5, lower, upper, empty, empty), ride


def split_parts(values, count):
    parts = []
    rest = values
    for _ in range(count - 1):
        part = lax.reduce_precision(rest, exponent_bits=8, mantissa_bits=7)
        parts.append(part)
        rest = rest - part
    parts.append(lax.reduce_precision(rest, exponent_bits=8, mantissa_bits=7))
    return [part.astype(jnp.bfloat16) for part in parts]


def one_hot(index, count):
    return (index[:, None] == lax.broadcasted_iota(jnp.int32, (1, count), 1)).astype(jnp.bfloat16)


def gather_flat(values, picks, lanes, count=3):
    rows = values.shape[0] // lanes
    table = values.reshape(rows, lanes)
    parts = jnp.concatenate(split_parts(table, count), axis=1)
    hit_row_t = (lax.broadcasted_iota(jnp.int32, (rows, 1), 0) == (picks // lanes)[None, :]).astype(jnp.bfloat16)
    picked = lax.dot_general(parts, hit_row_t, (((0,), (0,)), ((), ())), preferred_element_type=jnp.float32)
    total = picked[:lanes]
    for n in range(1, count):
        total = total + picked[n * lanes : (n + 1) * lanes]
    hit_lane_t = lax.broadcasted_iota(jnp.int32, (lanes, 1), 0) == (picks % lanes)[None, :]
    return jnp.sum(jnp.where(hit_lane_t, total, 0.0), axis=0)


def segment_sum(values, ids, bins, lanes, count=3):
    rows = bins // lanes
    hit_row_t = lax.broadcasted_iota(jnp.int32, (rows, 1), 0) == (ids // lanes)[None, :]
    lhs = jnp.concatenate(
        [jnp.where(hit_row_t, part[None, :], jnp.bfloat16(0)) for part in split_parts(values, count)], axis=0
    )
    sums = jnp.dot(lhs, one_hot(ids % lanes, lanes), preferred_element_type=jnp.float32)
    total = sums[:rows]
    for n in range(1, count):
        total = total + sums[n * rows : (n + 1) * rows]
    return total.reshape(-1)


def strip_reduce(partial, strips, strip_size):
    n_ex = lax.axis_size("ex")
    piece = -(-strip_size // n_ex)
    chunks = partial.reshape(2, strips, strip_size)
    if piece * n_ex != strip_size:
        chunks = jnp.pad(chunks, ((0, 0), (0, 0), (0, piece * n_ex - strip_size)))
    chunks = chunks.reshape(2, strips, n_ex, piece).transpose(2, 1, 0, 3)
    chunks = chunks.reshape(n_ex * strips, 2, piece)
    return lax.all_to_all(chunks, ("ex", "ey"), 0, 0, tiled=True).sum(0)


def strip_spread(mine):
    return jnp.broadcast_to(mine[None], (lax.axis_size("ex"),) + mine.shape)


def strip_gather(spread_out, strip_size):
    n_ex, count, piece = spread_out.shape
    whole = lax.all_to_all(spread_out, "ex", 0, 0, tiled=True)
    return whole.transpose(1, 0, 2).reshape(2, n_ex * piece)[:, :strip_size]


def on_device(source, metric, fac_point, fac_strip, fac_shell, fac_area):
    weights, stiff = gll_tables()
    high, low = (2.0, 0.2)
    theta = (high + low) / 2.0
    delta = (high - low) / 2.0
    sigma = theta / delta
    rho_now = 1.0 / sigma
    both, _ = assemble(jnp.stack([source, local_diagonal(metric, weights, stiff)]))
    rhs = both[0]
    pinv = 1.0 / both[1]
    pressure = jnp.zeros_like(source)
    resid = rhs
    update = pinv * resid / theta
    picks = fac_point[0]
    areas = fac_area[0]
    strips = lax.axis_size("ey")
    global_ids = fac_strip[0, :, 0] * SHELL_STRIP + fac_shell[0]
    denom = segment_sum(areas, global_ids, strips * SHELL_STRIP, 256)
    for step in range(SWEEPS):
        pressure = pressure + update
        if step + 2 == SWEEPS:
            early = gather_flat(pressure.reshape(-1), picks, 256)
        applied = element_apply(update, metric, weights, stiff)
        if step + 1 == SWEEPS:
            samples = early + gather_flat(update.reshape(-1), picks, 256, 2)
            numer = segment_sum(areas * samples, global_ids, strips * SHELL_STRIP, 256, 2)
            partial = jnp.stack([numer, denom])
            assembled, mine = assemble(applied[None], strip_reduce(partial, strips, SHELL_STRIP), strip_spread)
        else:
            assembled, _ = assemble(applied[None])
        assembled = assembled[0]
        if step + 2 == SWEEPS:
            assembled, early = lax.optimization_barrier((assembled, early))
        if step == 0:
            assembled, denom = lax.optimization_barrier((assembled, denom))
        resid = resid - assembled
        if step + 1 < SWEEPS:
            rho_new = 1.0 / (2.0 * sigma - rho_now)
            update = rho_new * rho_now * update + 2.0 * rho_new / delta * pinv * resid
            rho_now = rho_new
    total = strip_gather(mine, SHELL_STRIP)
    shell_load = total[0] / jnp.maximum(total[1], 1.0)
    return (pressure, resid, shell_load)


def solution(mesh):
    placed = (
        P("ex", "ey", None, None, None, None),
        P(None, "ex", "ey", None),
        P("ex", "ey"),
        P("ex", "ey", None),
        P("ex", "ey"),
        P("ex", "ey"),
    )
    return jax.shard_map(
        on_device,
        mesh=mesh,
        in_specs=placed,
        out_specs=(
            P("ex", "ey", None, None, None, None),
            P("ex", "ey", None, None, None, None),
            P("ey"),
        ),
        check_vma=False,
    )
```

```python
import jax
import jax.numpy as jnp
import numpy as np
from jax import lax
from jax.sharding import PartitionSpec as P

SWEEPS = 4
SHELL_STRIP = 16384


def padded_2(block, sides, width):
    for axis, dim in sides:
        count = lax.axis_size(axis)
        forward = [(i, i + 1) for i in range(count - 1)]
        backward = [(target, source) for source, target in forward]
        low = lax.ppermute(
            lax.slice_in_dim(block, block.shape[dim] - width, None, axis=dim), axis, forward
        )
        high = lax.ppermute(lax.slice_in_dim(block, 0, width, axis=dim), axis, backward)
        block = jnp.concatenate([low, block, high], axis=dim)
    return block


def gll_tables():
    degree = 7
    points = np.array(
        [
            -1.0,
            -0.8717401485096066,
            -0.5917001814331423,
            -0.2092992179024789,
            0.2092992179024789,
            0.5917001814331423,
            0.8717401485096066,
            1.0,
        ]
    )
    previous = points * 0.0 + 1.0
    current = points * 1.0
    for order in range(1, degree):
        following = ((2 * order + 1) * points * current - order * previous) / (order + 1)
        previous = current
        current = following
    weights = 2.0 / (degree * (degree + 1) * current**2)
    count = degree + 1
    same = np.array([[1.0 if row == col else 0.0 for col in range(count)] for row in range(count)])
    between = points[:, None] - points[None, :] + same
    deriv = current[:, None] / current[None, :] / between * (1.0 - same)
    deriv[0, 0] = -degree * (degree + 1) / 4.0
    deriv[-1, -1] = degree * (degree + 1) / 4.0
    stiff = deriv.T @ (weights[:, None] * deriv)
    return (np.asarray(weights, np.float32), np.asarray(stiff, np.float32))


def spread(metric, which):
    return metric[which][:, :, None, None, None, :]


def element_apply(values_in, metric, weights, stiff):
    top = lax.Precision.HIGHEST
    weight_i = weights[None, None, :, None, None, None]
    weight_j = weights[None, None, None, :, None, None]
    weight_k = weights[None, None, None, None, :, None]
    along_x = jnp.einsum("im,abmjkc->abijkc", stiff, values_in, precision=top)
    along_y = jnp.einsum("jm,abimkc->abijkc", stiff, values_in, precision=top)
    along_z = jnp.einsum("km,abijmc->abijkc", stiff, values_in, precision=top)
    return (
        spread(metric, 0) * weight_j * weight_k * along_x
        + spread(metric, 1) * weight_i * weight_k * along_y
        + spread(metric, 2) * weight_i * weight_j * along_z
        + spread(metric, 3) * weight_i * weight_j * weight_k * values_in
    )


def local_diagonal(metric, weights, stiff):
    stiff_diag = np.diagonal(stiff)
    weight_i = weights[None, None, :, None, None, None]
    weight_j = weights[None, None, None, :, None, None]
    weight_k = weights[None, None, None, None, :, None]
    diag_i = stiff_diag[None, None, :, None, None, None]
    diag_j = stiff_diag[None, None, None, :, None, None]
    diag_k = stiff_diag[None, None, None, None, :, None]
    return (
        spread(metric, 0) * diag_i * weight_j * weight_k
        + spread(metric, 1) * weight_i * diag_j * weight_k
        + spread(metric, 2) * weight_i * weight_j * diag_k
        + spread(metric, 3) * weight_i * weight_j * weight_k
    )


def faces(values_in, face_dim):
    last = values_in.shape[face_dim] - 1
    lower = lax.index_in_dim(values_in, 0, face_dim, keepdims=False)
    upper = lax.index_in_dim(values_in, last, face_dim, keepdims=False)
    return (lower, upper)


def combine(values_in, face_dim, elem_dim, lower, upper, before, after):
    total = lower.shape[elem_dim]
    upper_prev = jnp.concatenate(
        [before, lax.slice_in_dim(upper, 0, total - 1, axis=elem_dim)], elem_dim
    )
    lower_next = jnp.concatenate(
        [lax.slice_in_dim(lower, 1, total, axis=elem_dim), after], elem_dim
    )
    middle = lax.slice_in_dim(values_in, 1, values_in.shape[face_dim] - 1, axis=face_dim)
    return jnp.concatenate(
        [
            jnp.expand_dims(lower + upper_prev, face_dim),
            middle,
            jnp.expand_dims(upper + lower_next, face_dim),
        ],
        face_dim,
    )


def assemble(values_in, ride=None, then=None):
    lower, upper = faces(values_in, 3)
    rim_faces = jnp.concatenate([lower, upper], 1)
    padded = padded_2(rim_faces, (("ex", 1),), 1)
    if ride is not None:
        padded, ride = lax.optimization_barrier((padded, ride))
    values_in = combine(values_in, 3, 1, lower, upper, padded[:, :1], padded[:, 3:])
    lower, upper = faces(values_in, 4)
    rim_faces = jnp.concatenate([lower, upper], 2)
    if then is not None:
        ride = then(ride)
        rim_faces, ride = lax.optimization_barrier((rim_faces, ride))
    padded = padded_2(rim_faces, (("ey", 2),), 1)
    values_in = combine(values_in, 4, 2, lower, upper, padded[:, :, :1], padded[:, :, 3:])
    lower, upper = faces(values_in, 5)
    empty = jnp.zeros_like(upper[..., :1])
    return combine(values_in, 5, 5, lower, upper, empty, empty), ride


def split_parts(values, count):
    parts = []
    rest = values
    for _ in range(count - 1):
        part = lax.reduce_precision(rest, exponent_bits=8, mantissa_bits=7)
        parts.append(part)
        rest = rest - part
    parts.append(lax.reduce_precision(rest, exponent_bits=8, mantissa_bits=7))
    return [part.astype(jnp.bfloat16) for part in parts]


def one_hot(index, count):
    return (index[:, None] == lax.broadcasted_iota(jnp.int32, (1, count), 1)).astype(jnp.bfloat16)


def gather_flat(values, picks, lanes, count=3):
    rows = values.shape[0] // lanes
    table = values.reshape(rows, lanes)
    parts = jnp.concatenate(split_parts(table, count), axis=1)
    hit_row_t = (lax.broadcasted_iota(jnp.int32, (rows, 1), 0) == (picks // lanes)[None, :]).astype(jnp.bfloat16)
    picked = lax.dot_general(parts, hit_row_t, (((0,), (0,)), ((), ())), preferred_element_type=jnp.float32)
    total = picked[:lanes]
    for n in range(1, count):
        total = total + picked[n * lanes : (n + 1) * lanes]
    hit_lane_t = lax.broadcasted_iota(jnp.int32, (lanes, 1), 0) == (picks % lanes)[None, :]
    return jnp.sum(jnp.where(hit_lane_t, total, 0.0), axis=0)


def segment_sum(values, ids, bins, lanes, count=3):
    rows = bins // lanes
    hit_row_t = lax.broadcasted_iota(jnp.int32, (rows, 1), 0) == (ids // lanes)[None, :]
    lhs = jnp.concatenate(
        [jnp.where(hit_row_t, part[None, :], jnp.bfloat16(0)) for part in split_parts(values, count)], axis=0
    )
    sums = jnp.dot(lhs, one_hot(ids % lanes, lanes), preferred_element_type=jnp.float32)
    total = sums[:rows]
    for n in range(1, count):
        total = total + sums[n * rows : (n + 1) * rows]
    return total.reshape(-1)


def strip_reduce(partial, strips, strip_size):
    n_ex = lax.axis_size("ex")
    piece = -(-strip_size // n_ex)
    chunks = partial.reshape(2, strips, strip_size)
    if piece * n_ex != strip_size:
        chunks = jnp.pad(chunks, ((0, 0), (0, 0), (0, piece * n_ex - strip_size)))
    chunks = chunks.reshape(2, strips, n_ex, piece).transpose(2, 1, 0, 3)
    chunks = chunks.reshape(n_ex * strips, 2, piece)
    return lax.all_to_all(chunks, ("ex", "ey"), 0, 0, tiled=True).sum(0)


def strip_spread(mine):
    return jnp.broadcast_to(mine[None], (lax.axis_size("ex"),) + mine.shape)


def strip_gather(spread_out, strip_size):
    n_ex, count, piece = spread_out.shape
    whole = lax.all_to_all(spread_out, "ex", 0, 0, tiled=True)
    load = whole[:, 0] / jnp.maximum(whole[:, 1], 1.0)
    return load.reshape(n_ex * piece)[:strip_size]


def on_device(source, metric, fac_point, fac_strip, fac_shell, fac_area):
    weights, stiff = gll_tables()
    high, low = (2.0, 0.2)
    theta = (high + low) / 2.0
    delta = (high - low) / 2.0
    sigma = theta / delta
    rho_now = 1.0 / sigma
    both, _ = assemble(jnp.stack([source, local_diagonal(metric, weights, stiff)]))
    rhs = both[0]
    pinv = 1.0 / both[1]
    pressure = jnp.zeros_like(source)
    resid = rhs
    update = pinv * resid / theta
    picks = fac_point[0]
    areas = fac_area[0]
    strips = lax.axis_size("ey")
    global_ids = fac_strip[0, :, 0] * SHELL_STRIP + fac_shell[0]
    denom = segment_sum(areas, global_ids, strips * SHELL_STRIP, 256)
    for step in range(SWEEPS):
        pressure = pressure + update
        if step + 2 == SWEEPS:
            early = gather_flat(pressure.reshape(-1), picks, 256)
        applied = element_apply(update, metric, weights, stiff)
        if step + 1 == SWEEPS:
            samples = early + gather_flat(update.reshape(-1), picks, 256, 2)
            numer = segment_sum(areas * samples, global_ids, strips * SHELL_STRIP, 256, 2)
            partial = jnp.stack([numer, denom])
            assembled, mine = assemble(applied[None], strip_reduce(partial, strips, SHELL_STRIP), strip_spread)
        else:
            assembled, _ = assemble(applied[None])
        assembled = assembled[0]
        if step + 2 == SWEEPS:
            assembled, early = lax.optimization_barrier((assembled, early))
        if step == 0:
            assembled, denom = lax.optimization_barrier((assembled, denom))
        resid = resid - assembled
        if step + 1 < SWEEPS:
            rho_new = 1.0 / (2.0 * sigma - rho_now)
            update = rho_new * rho_now * update + 2.0 * rho_new / delta * pinv * resid
            rho_now = rho_new
    shell_load = strip_gather(mine, SHELL_STRIP)
    return (pressure, resid, shell_load)


def solution(mesh):
    placed = (
        P("ex", "ey", None, None, None, None),
        P(None, "ex", "ey", None),
        P("ex", "ey"),
        P("ex", "ey", None),
        P("ex", "ey"),
        P("ex", "ey"),
    )
    return jax.shard_map(
        on_device,
        mesh=mesh,
        in_specs=placed,
        out_specs=(
            P("ex", "ey", None, None, None, None),
            P("ex", "ey", None, None, None, None),
            P("ey"),
        ),
        check_vma=False,
    )
```

```python
import jax
import jax.numpy as jnp
import numpy as np
from jax import lax
from jax.sharding import PartitionSpec as P

SWEEPS = 4
SHELL_STRIP = 16384


def padded_2(block, sides, width):
    for axis, dim in sides:
        count = lax.axis_size(axis)
        forward = [(i, i + 1) for i in range(count - 1)]
        backward = [(target, source) for source, target in forward]
        low = lax.ppermute(
            lax.slice_in_dim(block, block.shape[dim] - width, None, axis=dim), axis, forward
        )
        high = lax.ppermute(lax.slice_in_dim(block, 0, width, axis=dim), axis, backward)
        block = jnp.concatenate([low, block, high], axis=dim)
    return block


def gll_tables():
    degree = 7
    points = np.array(
        [
            -1.0,
            -0.8717401485096066,
            -0.5917001814331423,
            -0.2092992179024789,
            0.2092992179024789,
            0.5917001814331423,
            0.8717401485096066,
            1.0,
        ]
    )
    previous = points * 0.0 + 1.0
    current = points * 1.0
    for order in range(1, degree):
        following = ((2 * order + 1) * points * current - order * previous) / (order + 1)
        previous = current
        current = following
    weights = 2.0 / (degree * (degree + 1) * current**2)
    count = degree + 1
    same = np.array([[1.0 if row == col else 0.0 for col in range(count)] for row in range(count)])
    between = points[:, None] - points[None, :] + same
    deriv = current[:, None] / current[None, :] / between * (1.0 - same)
    deriv[0, 0] = -degree * (degree + 1) / 4.0
    deriv[-1, -1] = degree * (degree + 1) / 4.0
    stiff = deriv.T @ (weights[:, None] * deriv)
    return (np.asarray(weights, np.float32), np.asarray(stiff, np.float32))


def spread(metric, which):
    return metric[which][:, :, None, None, None, :]


def element_apply(values_in, metric, weights, stiff):
    top = lax.Precision.HIGHEST
    weight_i = weights[None, None, :, None, None, None]
    weight_j = weights[None, None, None, :, None, None]
    weight_k = weights[None, None, None, None, :, None]
    along_x = jnp.einsum("im,abmjkc->abijkc", stiff, values_in, precision=top)
    along_y = jnp.einsum("jm,abimkc->abijkc", stiff, values_in, precision=top)
    along_z = jnp.einsum("km,abijmc->abijkc", stiff, values_in, precision=top)
    return (
        spread(metric, 0) * weight_j * weight_k * along_x
        + spread(metric, 1) * weight_i * weight_k * along_y
        + spread(metric, 2) * weight_i * weight_j * along_z
        + spread(metric, 3) * weight_i * weight_j * weight_k * values_in
    )


def local_diagonal(metric, weights, stiff):
    stiff_diag = np.diagonal(stiff)
    weight_i = weights[None, None, :, None, None, None]
    weight_j = weights[None, None, None, :, None, None]
    weight_k = weights[None, None, None, None, :, None]
    diag_i = stiff_diag[None, None, :, None, None, None]
    diag_j = stiff_diag[None, None, None, :, None, None]
    diag_k = stiff_diag[None, None, None, None, :, None]
    return (
        spread(metric, 0) * diag_i * weight_j * weight_k
        + spread(metric, 1) * weight_i * diag_j * weight_k
        + spread(metric, 2) * weight_i * weight_j * diag_k
        + spread(metric, 3) * weight_i * weight_j * weight_k
    )


def faces(values_in, face_dim):
    last = values_in.shape[face_dim] - 1
    lower = lax.index_in_dim(values_in, 0, face_dim, keepdims=False)
    upper = lax.index_in_dim(values_in, last, face_dim, keepdims=False)
    return (lower, upper)


def combine(values_in, face_dim, elem_dim, lower, upper, before, after):
    total = lower.shape[elem_dim]
    upper_prev = jnp.concatenate(
        [before, lax.slice_in_dim(upper, 0, total - 1, axis=elem_dim)], elem_dim
    )
    lower_next = jnp.concatenate(
        [lax.slice_in_dim(lower, 1, total, axis=elem_dim), after], elem_dim
    )
    middle = lax.slice_in_dim(values_in, 1, values_in.shape[face_dim] - 1, axis=face_dim)
    return jnp.concatenate(
        [
            jnp.expand_dims(lower + upper_prev, face_dim),
            middle,
            jnp.expand_dims(upper + lower_next, face_dim),
        ],
        face_dim,
    )


def assemble(values_in, ride=None, then=None):
    lower, upper = faces(values_in, 3)
    rim_faces = jnp.concatenate([lower, upper], 1)
    padded = padded_2(rim_faces, (("ex", 1),), 1)
    if ride is not None:
        padded, ride = lax.optimization_barrier((padded, ride))
    values_in = combine(values_in, 3, 1, lower, upper, padded[:, :1], padded[:, 3:])
    lower, upper = faces(values_in, 4)
    rim_faces = jnp.concatenate([lower, upper], 2)
    if then is not None:
        ride = then(ride)
        rim_faces, ride = lax.optimization_barrier((rim_faces, ride))
    padded = padded_2(rim_faces, (("ey", 2),), 1)
    values_in = combine(values_in, 4, 2, lower, upper, padded[:, :, :1], padded[:, :, 3:])
    lower, upper = faces(values_in, 5)
    empty = jnp.zeros_like(upper[..., :1])
    return combine(values_in, 5, 5, lower, upper, empty, empty), ride


def split_parts(values, count):
    parts = []
    rest = values
    for _ in range(count - 1):
        part = lax.reduce_precision(rest, exponent_bits=8, mantissa_bits=7)
        parts.append(part)
        rest = rest - part
    parts.append(lax.reduce_precision(rest, exponent_bits=8, mantissa_bits=7))
    return [part.astype(jnp.bfloat16) for part in parts]


def one_hot(index, count):
    return (index[:, None] == lax.broadcasted_iota(jnp.int32, (1, count), 1)).astype(jnp.bfloat16)


def gather_flat(values, picks, lanes, count=3):
    rows = values.shape[0] // lanes
    table = values.reshape(rows, lanes)
    parts = jnp.concatenate(split_parts(table, count), axis=1)
    hit_row_t = (lax.broadcasted_iota(jnp.int32, (rows, 1), 0) == (picks // lanes)[None, :]).astype(jnp.bfloat16)
    picked = lax.dot_general(parts, hit_row_t, (((0,), (0,)), ((), ())), preferred_element_type=jnp.float32)
    total = picked[:lanes]
    for n in range(1, count):
        total = total + picked[n * lanes : (n + 1) * lanes]
    hit_lane_t = lax.broadcasted_iota(jnp.int32, (lanes, 1), 0) == (picks % lanes)[None, :]
    return jnp.sum(jnp.where(hit_lane_t, total, 0.0), axis=0)


def segment_sum(values, ids, bins, lanes, count=3):
    rows = bins // lanes
    hit_row_t = lax.broadcasted_iota(jnp.int32, (rows, 1), 0) == (ids // lanes)[None, :]
    lhs = jnp.concatenate(
        [jnp.where(hit_row_t, part[None, :], jnp.bfloat16(0)) for part in split_parts(values, count)], axis=0
    )
    sums = jnp.dot(lhs, one_hot(ids % lanes, lanes), preferred_element_type=jnp.float32)
    total = sums[:rows]
    for n in range(1, count):
        total = total + sums[n * rows : (n + 1) * rows]
    return total.reshape(-1)


def strip_reduce(partial, strips, strip_size):
    n_ex = lax.axis_size("ex")
    piece = -(-strip_size // n_ex)
    chunks = partial.reshape(2, strips, strip_size)
    if piece * n_ex != strip_size:
        chunks = jnp.pad(chunks, ((0, 0), (0, 0), (0, piece * n_ex - strip_size)))
    chunks = chunks.reshape(2, strips, n_ex, piece).transpose(2, 1, 0, 3)
    chunks = chunks.reshape(n_ex * strips, 2, piece)
    return lax.all_to_all(chunks, ("ex", "ey"), 0, 0, tiled=True).sum(0)


def strip_spread(mine):
    return jnp.broadcast_to(mine[None], (lax.axis_size("ex"),) + mine.shape)


def strip_gather(spread_out, strip_size):
    n_ex, count, piece = spread_out.shape
    whole = lax.all_to_all(spread_out, "ex", 0, 0, tiled=True)
    load = whole[:, 0] / jnp.maximum(whole[:, 1], 1.0)
    return load.reshape(n_ex * piece)[:strip_size]


def on_device(source, metric, fac_point, fac_strip, fac_shell, fac_area):
    weights, stiff = gll_tables()
    high, low = (2.0, 0.2)
    theta = (high + low) / 2.0
    delta = (high - low) / 2.0
    sigma = theta / delta
    rho_now = 1.0 / sigma
    both, _ = assemble(jnp.stack([source, local_diagonal(metric, weights, stiff)]))
    rhs = both[0]
    pinv = 1.0 / both[1]
    pressure = jnp.zeros_like(source)
    resid = rhs
    update = pinv * resid / theta
    picks = fac_point[0]
    areas = fac_area[0]
    strips = lax.axis_size("ey")
    global_ids = fac_strip[0, :, 0] * SHELL_STRIP + fac_shell[0]
    denom = segment_sum(areas, global_ids, strips * SHELL_STRIP, 256)
    for step in range(SWEEPS):
        pressure = pressure + update
        if step + 2 == SWEEPS:
            early = gather_flat(pressure.reshape(-1), picks, 256)
        applied = element_apply(update, metric, weights, stiff)
        if step + 1 == SWEEPS:
            samples = early + gather_flat(update.reshape(-1), picks, 256, 2)
            numer = segment_sum(areas * samples, global_ids, strips * SHELL_STRIP, 256, 2)
            partial = jnp.stack([numer, denom])
            assembled, mine = assemble(applied[None], strip_reduce(partial, strips, SHELL_STRIP), strip_spread)
        else:
            assembled, _ = assemble(applied[None])
        assembled = assembled[0]
        if step + 2 == SWEEPS:
            assembled, early = lax.optimization_barrier((assembled, early))
        if step == 1:
            assembled, denom = lax.optimization_barrier((assembled, denom))
        resid = resid - assembled
        if step + 1 < SWEEPS:
            rho_new = 1.0 / (2.0 * sigma - rho_now)
            update = rho_new * rho_now * update + 2.0 * rho_new / delta * pinv * resid
            rho_now = rho_new
    shell_load = strip_gather(mine, SHELL_STRIP)
    return (pressure, resid, shell_load)


def solution(mesh):
    placed = (
        P("ex", "ey", None, None, None, None),
        P(None, "ex", "ey", None),
        P("ex", "ey"),
        P("ex", "ey", None),
        P("ex", "ey"),
        P("ex", "ey"),
    )
    return jax.shard_map(
        on_device,
        mesh=mesh,
        in_specs=placed,
        out_specs=(
            P("ex", "ey", None, None, None, None),
            P("ex", "ey", None, None, None, None),
            P("ey"),
        ),
        check_vma=False,
    )
```

```python
import jax
import jax.numpy as jnp
import numpy as np
from jax import lax
from jax.sharding import PartitionSpec as P

SWEEPS = 4
SHELL_STRIP = 16384


def padded_2(block, sides, width):
    for axis, dim in sides:
        count = lax.axis_size(axis)
        forward = [(i, i + 1) for i in range(count - 1)]
        backward = [(target, source) for source, target in forward]
        low = lax.ppermute(
            lax.slice_in_dim(block, block.shape[dim] - width, None, axis=dim), axis, forward
        )
        high = lax.ppermute(lax.slice_in_dim(block, 0, width, axis=dim), axis, backward)
        block = jnp.concatenate([low, block, high], axis=dim)
    return block


def gll_tables():
    degree = 7
    points = np.array(
        [
            -1.0,
            -0.8717401485096066,
            -0.5917001814331423,
            -0.2092992179024789,
            0.2092992179024789,
            0.5917001814331423,
            0.8717401485096066,
            1.0,
        ]
    )
    previous = points * 0.0 + 1.0
    current = points * 1.0
    for order in range(1, degree):
        following = ((2 * order + 1) * points * current - order * previous) / (order + 1)
        previous = current
        current = following
    weights = 2.0 / (degree * (degree + 1) * current**2)
    count = degree + 1
    same = np.array([[1.0 if row == col else 0.0 for col in range(count)] for row in range(count)])
    between = points[:, None] - points[None, :] + same
    deriv = current[:, None] / current[None, :] / between * (1.0 - same)
    deriv[0, 0] = -degree * (degree + 1) / 4.0
    deriv[-1, -1] = degree * (degree + 1) / 4.0
    stiff = deriv.T @ (weights[:, None] * deriv)
    return (np.asarray(weights, np.float32), np.asarray(stiff, np.float32))


def spread(metric, which):
    return metric[which][:, :, None, None, None, :]


def element_apply(values_in, metric, weights, stiff):
    top = lax.Precision.HIGHEST
    weight_i = weights[None, None, :, None, None, None]
    weight_j = weights[None, None, None, :, None, None]
    weight_k = weights[None, None, None, None, :, None]
    along_x = jnp.einsum("im,abmjkc->abijkc", stiff, values_in, precision=top)
    along_y = jnp.einsum("jm,abimkc->abijkc", stiff, values_in, precision=top)
    along_z = jnp.einsum("km,abijmc->abijkc", stiff, values_in, precision=top)
    return (
        spread(metric, 0) * weight_j * weight_k * along_x
        + spread(metric, 1) * weight_i * weight_k * along_y
        + spread(metric, 2) * weight_i * weight_j * along_z
        + spread(metric, 3) * weight_i * weight_j * weight_k * values_in
    )


def local_diagonal(metric, weights, stiff):
    stiff_diag = np.diagonal(stiff)
    weight_i = weights[None, None, :, None, None, None]
    weight_j = weights[None, None, None, :, None, None]
    weight_k = weights[None, None, None, None, :, None]
    diag_i = stiff_diag[None, None, :, None, None, None]
    diag_j = stiff_diag[None, None, None, :, None, None]
    diag_k = stiff_diag[None, None, None, None, :, None]
    return (
        spread(metric, 0) * diag_i * weight_j * weight_k
        + spread(metric, 1) * weight_i * diag_j * weight_k
        + spread(metric, 2) * weight_i * weight_j * diag_k
        + spread(metric, 3) * weight_i * weight_j * weight_k
    )


def faces(values_in, face_dim):
    last = values_in.shape[face_dim] - 1
    lower = lax.index_in_dim(values_in, 0, face_dim, keepdims=False)
    upper = lax.index_in_dim(values_in, last, face_dim, keepdims=False)
    return (lower, upper)


def combine(values_in, face_dim, elem_dim, lower, upper, before, after):
    total = lower.shape[elem_dim]
    upper_prev = jnp.concatenate(
        [before, lax.slice_in_dim(upper, 0, total - 1, axis=elem_dim)], elem_dim
    )
    lower_next = jnp.concatenate(
        [lax.slice_in_dim(lower, 1, total, axis=elem_dim), after], elem_dim
    )
    middle = lax.slice_in_dim(values_in, 1, values_in.shape[face_dim] - 1, axis=face_dim)
    return jnp.concatenate(
        [
            jnp.expand_dims(lower + upper_prev, face_dim),
            middle,
            jnp.expand_dims(upper + lower_next, face_dim),
        ],
        face_dim,
    )


def assemble(values_in, ride=None, then=None, x_faces=None):
    lower, upper = faces(values_in, 3) if x_faces is None else x_faces
    rim_faces = jnp.concatenate([lower, upper], 1)
    padded = padded_2(rim_faces, (("ex", 1),), 1)
    if ride is not None:
        padded, ride = lax.optimization_barrier((padded, ride))
    values_in = combine(values_in, 3, 1, lower, upper, padded[:, :1], padded[:, 3:])
    lower, upper = faces(values_in, 4)
    rim_faces = jnp.concatenate([lower, upper], 2)
    if then is not None:
        ride = then(ride)
        rim_faces, ride = lax.optimization_barrier((rim_faces, ride))
    padded = padded_2(rim_faces, (("ey", 2),), 1)
    values_in = combine(values_in, 4, 2, lower, upper, padded[:, :, :1], padded[:, :, 3:])
    lower, upper = faces(values_in, 5)
    empty = jnp.zeros_like(upper[..., :1])
    return combine(values_in, 5, 5, lower, upper, empty, empty), ride


def split_parts(values, count):
    parts = []
    rest = values
    for _ in range(count - 1):
        part = lax.reduce_precision(rest, exponent_bits=8, mantissa_bits=7)
        parts.append(part)
        rest = rest - part
    parts.append(lax.reduce_precision(rest, exponent_bits=8, mantissa_bits=7))
    return [part.astype(jnp.bfloat16) for part in parts]


def one_hot(index, count):
    return (index[:, None] == lax.broadcasted_iota(jnp.int32, (1, count), 1)).astype(jnp.bfloat16)


def gather_flat(values, picks, lanes, count=3):
    rows = values.shape[0] // lanes
    table = values.reshape(rows, lanes)
    parts = jnp.concatenate(split_parts(table, count), axis=1)
    hit_row_t = (lax.broadcasted_iota(jnp.int32, (rows, 1), 0) == (picks // lanes)[None, :]).astype(jnp.bfloat16)
    picked = lax.dot_general(parts, hit_row_t, (((0,), (0,)), ((), ())), preferred_element_type=jnp.float32)
    total = picked[:lanes]
    for n in range(1, count):
        total = total + picked[n * lanes : (n + 1) * lanes]
    hit_lane_t = lax.broadcasted_iota(jnp.int32, (lanes, 1), 0) == (picks % lanes)[None, :]
    return jnp.sum(jnp.where(hit_lane_t, total, 0.0), axis=0)


def segment_sum(values, ids, bins, lanes, count=3):
    rows = bins // lanes
    hit_row_t = lax.broadcasted_iota(jnp.int32, (rows, 1), 0) == (ids // lanes)[None, :]
    lhs = jnp.concatenate(
        [jnp.where(hit_row_t, part[None, :], jnp.bfloat16(0)) for part in split_parts(values, count)], axis=0
    )
    sums = jnp.dot(lhs, one_hot(ids % lanes, lanes), preferred_element_type=jnp.float32)
    total = sums[:rows]
    for n in range(1, count):
        total = total + sums[n * rows : (n + 1) * rows]
    return total.reshape(-1)


def strip_reduce(partial, strips, strip_size):
    n_ex = lax.axis_size("ex")
    piece = -(-strip_size // n_ex)
    chunks = partial.reshape(2, strips, strip_size)
    if piece * n_ex != strip_size:
        chunks = jnp.pad(chunks, ((0, 0), (0, 0), (0, piece * n_ex - strip_size)))
    chunks = chunks.reshape(2, strips, n_ex, piece).transpose(2, 1, 0, 3)
    chunks = chunks.reshape(n_ex * strips, 2, piece)
    return lax.all_to_all(chunks, ("ex", "ey"), 0, 0, tiled=True).sum(0)


def strip_spread(mine):
    return jnp.broadcast_to(mine[None], (lax.axis_size("ex"),) + mine.shape)


def strip_gather(spread_out, strip_size):
    n_ex, count, piece = spread_out.shape
    whole = lax.all_to_all(spread_out, "ex", 0, 0, tiled=True)
    load = whole[:, 0] / jnp.maximum(whole[:, 1], 1.0)
    return load.reshape(n_ex * piece)[:strip_size]


def on_device(source, metric, fac_point, fac_strip, fac_shell, fac_area):
    weights, stiff = gll_tables()
    high, low = (2.0, 0.2)
    theta = (high + low) / 2.0
    delta = (high - low) / 2.0
    sigma = theta / delta
    rho_now = 1.0 / sigma
    diagonal = local_diagonal(metric, weights, stiff)
    last = source.shape[2] - 1
    rims = [jnp.stack([source[:, :, edge], diagonal[:, :, edge]]) for edge in (0, last)]
    both, _ = assemble(jnp.stack([source, diagonal]), x_faces=rims)
    rhs = both[0]
    pinv = 1.0 / both[1]
    pressure = jnp.zeros_like(source)
    resid = rhs
    update = pinv * resid / theta
    picks = fac_point[0]
    areas = fac_area[0]
    strips = lax.axis_size("ey")
    global_ids = fac_strip[0, :, 0] * SHELL_STRIP + fac_shell[0]
    denom = segment_sum(areas, global_ids, strips * SHELL_STRIP, 256)
    for step in range(SWEEPS):
        pressure = pressure + update
        if step + 2 == SWEEPS:
            early = gather_flat(pressure.reshape(-1), picks, 256)
        applied = element_apply(update, metric, weights, stiff)
        if step + 1 == SWEEPS:
            samples = early + gather_flat(update.reshape(-1), picks, 256, 2)
            numer = segment_sum(areas * samples, global_ids, strips * SHELL_STRIP, 256, 2)
            partial = jnp.stack([numer, denom])
            assembled, mine = assemble(applied[None], strip_reduce(partial, strips, SHELL_STRIP), strip_spread)
        else:
            assembled, _ = assemble(applied[None])
        assembled = assembled[0]
        if step + 2 == SWEEPS:
            assembled, early = lax.optimization_barrier((assembled, early))
        if step == 0:
            assembled, denom = lax.optimization_barrier((assembled, denom))
        resid = resid - assembled
        if step + 1 < SWEEPS:
            rho_new = 1.0 / (2.0 * sigma - rho_now)
            update = rho_new * rho_now * update + 2.0 * rho_new / delta * pinv * resid
            rho_now = rho_new
    shell_load = strip_gather(mine, SHELL_STRIP)
    return (pressure, resid, shell_load)


def solution(mesh):
    placed = (
        P("ex", "ey", None, None, None, None),
        P(None, "ex", "ey", None),
        P("ex", "ey"),
        P("ex", "ey", None),
        P("ex", "ey"),
        P("ex", "ey"),
    )
    return jax.shard_map(
        on_device,
        mesh=mesh,
        in_specs=placed,
        out_specs=(
            P("ex", "ey", None, None, None, None),
            P("ex", "ey", None, None, None, None),
            P("ey"),
        ),
        check_vma=False,
    )
```

```python
import jax
import jax.numpy as jnp
import numpy as np
from jax import lax
from jax.sharding import PartitionSpec as P

SWEEPS = 4
SHELL_STRIP = 16384


def padded_2(block, sides, width):
    for axis, dim in sides:
        count = lax.axis_size(axis)
        forward = [(i, i + 1) for i in range(count - 1)]
        backward = [(target, source) for source, target in forward]
        low = lax.ppermute(
            lax.slice_in_dim(block, block.shape[dim] - width, None, axis=dim), axis, forward
        )
        high = lax.ppermute(lax.slice_in_dim(block, 0, width, axis=dim), axis, backward)
        block = jnp.concatenate([low, block, high], axis=dim)
    return block


def gll_tables():
    degree = 7
    points = np.array(
        [
            -1.0,
            -0.8717401485096066,
            -0.5917001814331423,
            -0.2092992179024789,
            0.2092992179024789,
            0.5917001814331423,
            0.8717401485096066,
            1.0,
        ]
    )
    previous = points * 0.0 + 1.0
    current = points * 1.0
    for order in range(1, degree):
        following = ((2 * order + 1) * points * current - order * previous) / (order + 1)
        previous = current
        current = following
    weights = 2.0 / (degree * (degree + 1) * current**2)
    count = degree + 1
    same = np.array([[1.0 if row == col else 0.0 for col in range(count)] for row in range(count)])
    between = points[:, None] - points[None, :] + same
    deriv = current[:, None] / current[None, :] / between * (1.0 - same)
    deriv[0, 0] = -degree * (degree + 1) / 4.0
    deriv[-1, -1] = degree * (degree + 1) / 4.0
    stiff = deriv.T @ (weights[:, None] * deriv)
    return (np.asarray(weights, np.float32), np.asarray(stiff, np.float32))


def spread(metric, which):
    return metric[which][:, :, None, None, None, :]


def element_apply(values_in, metric, weights, stiff):
    top = lax.Precision.HIGHEST
    weight_i = weights[None, None, :, None, None, None]
    weight_j = weights[None, None, None, :, None, None]
    weight_k = weights[None, None, None, None, :, None]
    along_x = jnp.einsum("im,abmjkc->abijkc", stiff, values_in, precision=top)
    along_y = jnp.einsum("jm,abimkc->abijkc", stiff, values_in, precision=top)
    along_z = jnp.einsum("km,abijmc->abijkc", stiff, values_in, precision=top)
    return (
        spread(metric, 0) * weight_j * weight_k * along_x
        + spread(metric, 1) * weight_i * weight_k * along_y
        + spread(metric, 2) * weight_i * weight_j * along_z
        + spread(metric, 3) * weight_i * weight_j * weight_k * values_in
    )


def local_diagonal(metric, weights, stiff):
    stiff_diag = np.diagonal(stiff)
    weight_i = weights[None, None, :, None, None, None]
    weight_j = weights[None, None, None, :, None, None]
    weight_k = weights[None, None, None, None, :, None]
    diag_i = stiff_diag[None, None, :, None, None, None]
    diag_j = stiff_diag[None, None, None, :, None, None]
    diag_k = stiff_diag[None, None, None, None, :, None]
    return (
        spread(metric, 0) * diag_i * weight_j * weight_k
        + spread(metric, 1) * weight_i * diag_j * weight_k
        + spread(metric, 2) * weight_i * weight_j * diag_k
        + spread(metric, 3) * weight_i * weight_j * weight_k
    )


def faces(values_in, face_dim):
    last = values_in.shape[face_dim] - 1
    lower = lax.index_in_dim(values_in, 0, face_dim, keepdims=False)
    upper = lax.index_in_dim(values_in, last, face_dim, keepdims=False)
    return (lower, upper)


def combine(values_in, face_dim, elem_dim, lower, upper, before, after):
    total = lower.shape[elem_dim]
    upper_prev = jnp.concatenate(
        [before, lax.slice_in_dim(upper, 0, total - 1, axis=elem_dim)], elem_dim
    )
    lower_next = jnp.concatenate(
        [lax.slice_in_dim(lower, 1, total, axis=elem_dim), after], elem_dim
    )
    middle = lax.slice_in_dim(values_in, 1, values_in.shape[face_dim] - 1, axis=face_dim)
    return jnp.concatenate(
        [
            jnp.expand_dims(lower + upper_prev, face_dim),
            middle,
            jnp.expand_dims(upper + lower_next, face_dim),
        ],
        face_dim,
    )


def assemble(values_in, ride=None, then=None, x_faces=None):
    lower, upper = faces(values_in, 3) if x_faces is None else x_faces
    rim_faces = jnp.concatenate([lower, upper], 1)
    padded = padded_2(rim_faces, (("ex", 1),), 1)
    if ride is not None:
        padded, ride = lax.optimization_barrier((padded, ride))
    values_in = combine(values_in, 3, 1, lower, upper, padded[:, :1], padded[:, 3:])
    lower, upper = faces(values_in, 4)
    rim_faces = jnp.concatenate([lower, upper], 2)
    if then is not None:
        ride = then(ride)
        rim_faces, ride = lax.optimization_barrier((rim_faces, ride))
    padded = padded_2(rim_faces, (("ey", 2),), 1)
    values_in = combine(values_in, 4, 2, lower, upper, padded[:, :, :1], padded[:, :, 3:])
    lower, upper = faces(values_in, 5)
    empty = jnp.zeros_like(upper[..., :1])
    return combine(values_in, 5, 5, lower, upper, empty, empty), ride


def split_parts(values, count):
    parts = []
    rest = values
    for _ in range(count - 1):
        part = lax.reduce_precision(rest, exponent_bits=8, mantissa_bits=7)
        parts.append(part)
        rest = rest - part
    parts.append(lax.reduce_precision(rest, exponent_bits=8, mantissa_bits=7))
    return [part.astype(jnp.bfloat16) for part in parts]


def one_hot(index, count):
    return (index[:, None] == lax.broadcasted_iota(jnp.int32, (1, count), 1)).astype(jnp.bfloat16)


def gather_flat(values, picks, lanes, count=3):
    rows = values.shape[0] // lanes
    table = values.reshape(rows, lanes)
    parts = jnp.concatenate(split_parts(table, count), axis=1)
    hit_row_t = (lax.broadcasted_iota(jnp.int32, (rows, 1), 0) == (picks // lanes)[None, :]).astype(jnp.bfloat16)
    picked = lax.dot_general(parts, hit_row_t, (((0,), (0,)), ((), ())), preferred_element_type=jnp.float32)
    total = picked[:lanes]
    for n in range(1, count):
        total = total + picked[n * lanes : (n + 1) * lanes]
    hit_lane_t = lax.broadcasted_iota(jnp.int32, (lanes, 1), 0) == (picks % lanes)[None, :]
    return jnp.sum(jnp.where(hit_lane_t, total, 0.0), axis=0)


def segment_sum(values, ids, bins, lanes, count=3):
    rows = bins // lanes
    hit_row_t = lax.broadcasted_iota(jnp.int32, (rows, 1), 0) == (ids // lanes)[None, :]
    lhs = jnp.concatenate(
        [jnp.where(hit_row_t, part[None, :], jnp.bfloat16(0)) for part in split_parts(values, count)], axis=0
    )
    sums = jnp.dot(lhs, one_hot(ids % lanes, lanes), preferred_element_type=jnp.float32)
    total = sums[:rows]
    for n in range(1, count):
        total = total + sums[n * rows : (n + 1) * rows]
    return total.reshape(-1)


def strip_reduce(partial, strips, strip_size):
    n_ex = lax.axis_size("ex")
    piece = -(-strip_size // n_ex)
    chunks = partial.reshape(2, strips, strip_size)
    if piece * n_ex != strip_size:
        chunks = jnp.pad(chunks, ((0, 0), (0, 0), (0, piece * n_ex - strip_size)))
    chunks = chunks.reshape(2, strips, n_ex, piece).transpose(2, 1, 0, 3)
    chunks = chunks.reshape(n_ex * strips, 2, piece)
    return lax.all_to_all(chunks, ("ex", "ey"), 0, 0, tiled=True).sum(0)


def strip_spread(mine):
    return jnp.broadcast_to(mine[None], (lax.axis_size("ex"),) + mine.shape)


def strip_gather(spread_out, strip_size):
    n_ex, count, piece = spread_out.shape
    whole = lax.all_to_all(spread_out, "ex", 0, 0, tiled=True)
    load = whole[:, 0] / jnp.maximum(whole[:, 1], 1.0)
    return load.reshape(n_ex * piece)[:strip_size]


def on_device(source, metric, fac_point, fac_strip, fac_shell, fac_area):
    weights, stiff = gll_tables()
    high, low = (2.0, 0.2)
    theta = (high + low) / 2.0
    delta = (high - low) / 2.0
    sigma = theta / delta
    rho_now = 1.0 / sigma
    diagonal = local_diagonal(metric, weights, stiff)
    last = source.shape[2] - 1
    rims = [jnp.stack([source[:, :, edge], diagonal[:, :, edge]]) for edge in (0, last)]
    shell_inputs = (fac_area[0], fac_strip[0, :, 0], fac_shell[0])
    both, shell_inputs = assemble(jnp.stack([source, diagonal]), shell_inputs, x_faces=rims)
    rhs = both[0]
    pinv = 1.0 / both[1]
    pressure = jnp.zeros_like(source)
    resid = rhs
    update = pinv * resid / theta
    picks = fac_point[0]
    areas, strip_of, shell_of = shell_inputs
    strips = lax.axis_size("ey")
    global_ids = strip_of * SHELL_STRIP + shell_of
    denom = segment_sum(areas, global_ids, strips * SHELL_STRIP, 256)
    for step in range(SWEEPS):
        pressure = pressure + update
        if step + 2 == SWEEPS:
            early = gather_flat(pressure.reshape(-1), picks, 256)
        applied = element_apply(update, metric, weights, stiff)
        if step + 1 == SWEEPS:
            samples = early + gather_flat(update.reshape(-1), picks, 256, 2)
            numer = segment_sum(areas * samples, global_ids, strips * SHELL_STRIP, 256, 2)
            partial = jnp.stack([numer, denom])
            assembled, mine = assemble(applied[None], strip_reduce(partial, strips, SHELL_STRIP), strip_spread)
        else:
            assembled, _ = assemble(applied[None])
        assembled = assembled[0]
        if step + 2 == SWEEPS:
            assembled, early = lax.optimization_barrier((assembled, early))
        if step == 0:
            assembled, denom = lax.optimization_barrier((assembled, denom))
        resid = resid - assembled
        if step + 1 < SWEEPS:
            rho_new = 1.0 / (2.0 * sigma - rho_now)
            update = rho_new * rho_now * update + 2.0 * rho_new / delta * pinv * resid
            rho_now = rho_new
    shell_load = strip_gather(mine, SHELL_STRIP)
    return (pressure, resid, shell_load)


def solution(mesh):
    placed = (
        P("ex", "ey", None, None, None, None),
        P(None, "ex", "ey", None),
        P("ex", "ey"),
        P("ex", "ey", None),
        P("ex", "ey"),
        P("ex", "ey"),
    )
    return jax.shard_map(
        on_device,
        mesh=mesh,
        in_specs=placed,
        out_specs=(
            P("ex", "ey", None, None, None, None),
            P("ex", "ey", None, None, None, None),
            P("ey"),
        ),
        check_vma=False,
    )
```

```python
import jax
import jax.numpy as jnp
import numpy as np
from jax import lax
from jax.sharding import PartitionSpec as P

SWEEPS = 4
SHELL_STRIP = 16384


def padded_2(block, sides, width):
    for axis, dim in sides:
        count = lax.axis_size(axis)
        forward = [(i, i + 1) for i in range(count - 1)]
        backward = [(target, source) for source, target in forward]
        low = lax.ppermute(
            lax.slice_in_dim(block, block.shape[dim] - width, None, axis=dim), axis, forward
        )
        high = lax.ppermute(lax.slice_in_dim(block, 0, width, axis=dim), axis, backward)
        block = jnp.concatenate([low, block, high], axis=dim)
    return block


def gll_tables():
    degree = 7
    points = np.array(
        [
            -1.0,
            -0.8717401485096066,
            -0.5917001814331423,
            -0.2092992179024789,
            0.2092992179024789,
            0.5917001814331423,
            0.8717401485096066,
            1.0,
        ]
    )
    previous = points * 0.0 + 1.0
    current = points * 1.0
    for order in range(1, degree):
        following = ((2 * order + 1) * points * current - order * previous) / (order + 1)
        previous = current
        current = following
    weights = 2.0 / (degree * (degree + 1) * current**2)
    count = degree + 1
    same = np.array([[1.0 if row == col else 0.0 for col in range(count)] for row in range(count)])
    between = points[:, None] - points[None, :] + same
    deriv = current[:, None] / current[None, :] / between * (1.0 - same)
    deriv[0, 0] = -degree * (degree + 1) / 4.0
    deriv[-1, -1] = degree * (degree + 1) / 4.0
    stiff = deriv.T @ (weights[:, None] * deriv)
    return (np.asarray(weights, np.float32), np.asarray(stiff, np.float32))


def spread(metric, which):
    return metric[which][:, :, None, None, None, :]


def element_apply(values_in, metric, weights, stiff):
    top = lax.Precision.HIGHEST
    weight_i = weights[None, None, :, None, None, None]
    weight_j = weights[None, None, None, :, None, None]
    weight_k = weights[None, None, None, None, :, None]
    along_x = jnp.einsum("im,abmjkc->abijkc", stiff, values_in, precision=top)
    along_y = jnp.einsum("jm,abimkc->abijkc", stiff, values_in, precision=top)
    along_z = jnp.einsum("km,abijmc->abijkc", stiff, values_in, precision=top)
    return (
        spread(metric, 0) * weight_j * weight_k * along_x
        + spread(metric, 1) * weight_i * weight_k * along_y
        + spread(metric, 2) * weight_i * weight_j * along_z
        + spread(metric, 3) * weight_i * weight_j * weight_k * values_in
    )


def local_diagonal(metric, weights, stiff):
    stiff_diag = np.diagonal(stiff)
    weight_i = weights[None, None, :, None, None, None]
    weight_j = weights[None, None, None, :, None, None]
    weight_k = weights[None, None, None, None, :, None]
    diag_i = stiff_diag[None, None, :, None, None, None]
    diag_j = stiff_diag[None, None, None, :, None, None]
    diag_k = stiff_diag[None, None, None, None, :, None]
    return (
        spread(metric, 0) * diag_i * weight_j * weight_k
        + spread(metric, 1) * weight_i * diag_j * weight_k
        + spread(metric, 2) * weight_i * weight_j * diag_k
        + spread(metric, 3) * weight_i * weight_j * weight_k
    )


def faces(values_in, face_dim):
    last = values_in.shape[face_dim] - 1
    lower = lax.index_in_dim(values_in, 0, face_dim, keepdims=False)
    upper = lax.index_in_dim(values_in, last, face_dim, keepdims=False)
    return (lower, upper)


def combine(values_in, face_dim, elem_dim, lower, upper, before, after):
    total = lower.shape[elem_dim]
    upper_prev = jnp.concatenate(
        [before, lax.slice_in_dim(upper, 0, total - 1, axis=elem_dim)], elem_dim
    )
    lower_next = jnp.concatenate(
        [lax.slice_in_dim(lower, 1, total, axis=elem_dim), after], elem_dim
    )
    middle = lax.slice_in_dim(values_in, 1, values_in.shape[face_dim] - 1, axis=face_dim)
    return jnp.concatenate(
        [
            jnp.expand_dims(lower + upper_prev, face_dim),
            middle,
            jnp.expand_dims(upper + lower_next, face_dim),
        ],
        face_dim,
    )


def assemble(values_in, ride=None, then=None, x_faces=None):
    lower, upper = faces(values_in, 3) if x_faces is None else x_faces
    rim_faces = jnp.concatenate([lower, upper], 1)
    padded = padded_2(rim_faces, (("ex", 1),), 1)
    if ride is not None:
        padded, ride = lax.optimization_barrier((padded, ride))
    values_in = combine(values_in, 3, 1, lower, upper, padded[:, :1], padded[:, 3:])
    lower, upper = faces(values_in, 4)
    rim_faces = jnp.concatenate([lower, upper], 2)
    if then is not None:
        ride = then(ride)
        rim_faces, ride = lax.optimization_barrier((rim_faces, ride))
    padded = padded_2(rim_faces, (("ey", 2),), 1)
    values_in = combine(values_in, 4, 2, lower, upper, padded[:, :, :1], padded[:, :, 3:])
    lower, upper = faces(values_in, 5)
    empty = jnp.zeros_like(upper[..., :1])
    return combine(values_in, 5, 5, lower, upper, empty, empty), ride


def split_parts(values, count):
    parts = []
    rest = values
    for _ in range(count - 1):
        part = lax.reduce_precision(rest, exponent_bits=8, mantissa_bits=7)
        parts.append(part)
        rest = rest - part
    parts.append(lax.reduce_precision(rest, exponent_bits=8, mantissa_bits=7))
    return [part.astype(jnp.bfloat16) for part in parts]


def one_hot(index, count):
    return (index[:, None] == lax.broadcasted_iota(jnp.int32, (1, count), 1)).astype(jnp.bfloat16)


def gather_flat(values, picks, lanes, count=3):
    rows = values.shape[0] // lanes
    table = values.reshape(rows, lanes)
    parts = jnp.concatenate(split_parts(table, count), axis=1)
    hit_row_t = (lax.broadcasted_iota(jnp.int32, (rows, 1), 0) == (picks // lanes)[None, :]).astype(jnp.bfloat16)
    picked = lax.dot_general(parts, hit_row_t, (((0,), (0,)), ((), ())), preferred_element_type=jnp.float32)
    total = picked[:lanes]
    for n in range(1, count):
        total = total + picked[n * lanes : (n + 1) * lanes]
    hit_lane_t = lax.broadcasted_iota(jnp.int32, (lanes, 1), 0) == (picks % lanes)[None, :]
    return jnp.sum(jnp.where(hit_lane_t, total, 0.0), axis=0)


def segment_sum(values, ids, bins, lanes, count=3):
    rows = bins // lanes
    hit_row_t = lax.broadcasted_iota(jnp.int32, (rows, 1), 0) == (ids // lanes)[None, :]
    lhs = jnp.concatenate(
        [jnp.where(hit_row_t, part[None, :], jnp.bfloat16(0)) for part in split_parts(values, count)], axis=0
    )
    sums = jnp.dot(lhs, one_hot(ids % lanes, lanes), preferred_element_type=jnp.float32)
    total = sums[:rows]
    for n in range(1, count):
        total = total + sums[n * rows : (n + 1) * rows]
    return total.reshape(-1)


def strip_reduce(partial, strips, strip_size):
    n_ex = lax.axis_size("ex")
    piece = -(-strip_size // n_ex)
    chunks = partial.reshape(2, strips, strip_size)
    if piece * n_ex != strip_size:
        chunks = jnp.pad(chunks, ((0, 0), (0, 0), (0, piece * n_ex - strip_size)))
    chunks = chunks.reshape(2, strips, n_ex, piece).transpose(2, 1, 0, 3)
    chunks = chunks.reshape(n_ex * strips, 2, piece)
    return lax.all_to_all(chunks, ("ex", "ey"), 0, 0, tiled=True).sum(0)


def strip_spread(mine):
    return jnp.broadcast_to(mine[None], (lax.axis_size("ex"),) + mine.shape)


def strip_gather(spread_out, strip_size):
    n_ex, count, piece = spread_out.shape
    whole = lax.all_to_all(spread_out, "ex", 0, 0, tiled=True)
    load = whole[:, 0] / jnp.maximum(whole[:, 1], 1.0)
    return load.reshape(n_ex * piece)[:strip_size]


def on_device(source, metric, fac_point, fac_strip, fac_shell, fac_area):
    weights, stiff = gll_tables()
    high, low = (2.0, 0.2)
    theta = (high + low) / 2.0
    delta = (high - low) / 2.0
    sigma = theta / delta
    rho_now = 1.0 / sigma
    diagonal = local_diagonal(metric, weights, stiff)
    last = source.shape[2] - 1
    rims = [jnp.stack([source[:, :, edge], diagonal[:, :, edge]]) for edge in (0, last)]
    shell_inputs = (fac_area[0], fac_strip[0, :, 0], fac_shell[0])
    both, shell_inputs = assemble(jnp.stack([source, diagonal]), shell_inputs, x_faces=rims)
    picks = fac_point[0]
    areas, strip_of, shell_of = shell_inputs
    strips = lax.axis_size("ey")
    global_ids = strip_of * SHELL_STRIP + shell_of
    denom = segment_sum(areas, global_ids, strips * SHELL_STRIP, 256)
    both, denom = lax.optimization_barrier((both, denom))
    rhs = both[0]
    pinv = 1.0 / both[1]
    pressure = jnp.zeros_like(source)
    resid = rhs
    update = pinv * resid / theta
    for step in range(SWEEPS):
        pressure = pressure + update
        if step + 2 == SWEEPS:
            early = gather_flat(pressure.reshape(-1), picks, 256)
        applied = element_apply(update, metric, weights, stiff)
        if step + 1 == SWEEPS:
            samples = early + gather_flat(update.reshape(-1), picks, 256, 2)
            numer = segment_sum(areas * samples, global_ids, strips * SHELL_STRIP, 256, 2)
            partial = jnp.stack([numer, denom])
            assembled, mine = assemble(applied[None], strip_reduce(partial, strips, SHELL_STRIP), strip_spread)
        else:
            assembled, _ = assemble(applied[None])
        assembled = assembled[0]
        if step + 2 == SWEEPS:
            assembled, early = lax.optimization_barrier((assembled, early))
        resid = resid - assembled
        if step + 1 < SWEEPS:
            rho_new = 1.0 / (2.0 * sigma - rho_now)
            update = rho_new * rho_now * update + 2.0 * rho_new / delta * pinv * resid
            rho_now = rho_new
    shell_load = strip_gather(mine, SHELL_STRIP)
    return (pressure, resid, shell_load)


def solution(mesh):
    placed = (
        P("ex", "ey", None, None, None, None),
        P(None, "ex", "ey", None),
        P("ex", "ey"),
        P("ex", "ey", None),
        P("ex", "ey"),
        P("ex", "ey"),
    )
    return jax.shard_map(
        on_device,
        mesh=mesh,
        in_specs=placed,
        out_specs=(
            P("ex", "ey", None, None, None, None),
            P("ex", "ey", None, None, None, None),
            P("ey"),
        ),
        check_vma=False,
    )
```

```python
import jax
import jax.numpy as jnp
import numpy as np
from jax import lax
from jax.sharding import PartitionSpec as P

SWEEPS = 4
SHELL_STRIP = 16384


def padded_2(block, sides, width):
    for axis, dim in sides:
        count = lax.axis_size(axis)
        forward = [(i, i + 1) for i in range(count - 1)]
        backward = [(target, source) for source, target in forward]
        low = lax.ppermute(
            lax.slice_in_dim(block, block.shape[dim] - width, None, axis=dim), axis, forward
        )
        high = lax.ppermute(lax.slice_in_dim(block, 0, width, axis=dim), axis, backward)
        block = jnp.concatenate([low, block, high], axis=dim)
    return block


def gll_tables():
    degree = 7
    points = np.array(
        [
            -1.0,
            -0.8717401485096066,
            -0.5917001814331423,
            -0.2092992179024789,
            0.2092992179024789,
            0.5917001814331423,
            0.8717401485096066,
            1.0,
        ]
    )
    previous = points * 0.0 + 1.0
    current = points * 1.0
    for order in range(1, degree):
        following = ((2 * order + 1) * points * current - order * previous) / (order + 1)
        previous = current
        current = following
    weights = 2.0 / (degree * (degree + 1) * current**2)
    count = degree + 1
    same = np.array([[1.0 if row == col else 0.0 for col in range(count)] for row in range(count)])
    between = points[:, None] - points[None, :] + same
    deriv = current[:, None] / current[None, :] / between * (1.0 - same)
    deriv[0, 0] = -degree * (degree + 1) / 4.0
    deriv[-1, -1] = degree * (degree + 1) / 4.0
    stiff = deriv.T @ (weights[:, None] * deriv)
    return (np.asarray(weights, np.float32), np.asarray(stiff, np.float32))


def spread(metric, which):
    return metric[which][:, :, None, None, None, :]


def element_apply(values_in, metric, weights, stiff):
    top = lax.Precision.HIGHEST
    weight_i = weights[None, None, :, None, None, None]
    weight_j = weights[None, None, None, :, None, None]
    weight_k = weights[None, None, None, None, :, None]
    along_x = jnp.einsum("im,abmjkc->abijkc", stiff, values_in, precision=top)
    along_y = jnp.einsum("jm,abimkc->abijkc", stiff, values_in, precision=top)
    along_z = jnp.einsum("km,abijmc->abijkc", stiff, values_in, precision=top)
    return (
        spread(metric, 0) * weight_j * weight_k * along_x
        + spread(metric, 1) * weight_i * weight_k * along_y
        + spread(metric, 2) * weight_i * weight_j * along_z
        + spread(metric, 3) * weight_i * weight_j * weight_k * values_in
    )


def local_diagonal(metric, weights, stiff):
    stiff_diag = np.diagonal(stiff)
    weight_i = weights[None, None, :, None, None, None]
    weight_j = weights[None, None, None, :, None, None]
    weight_k = weights[None, None, None, None, :, None]
    diag_i = stiff_diag[None, None, :, None, None, None]
    diag_j = stiff_diag[None, None, None, :, None, None]
    diag_k = stiff_diag[None, None, None, None, :, None]
    return (
        spread(metric, 0) * diag_i * weight_j * weight_k
        + spread(metric, 1) * weight_i * diag_j * weight_k
        + spread(metric, 2) * weight_i * weight_j * diag_k
        + spread(metric, 3) * weight_i * weight_j * weight_k
    )


def faces(values_in, face_dim):
    last = values_in.shape[face_dim] - 1
    lower = lax.index_in_dim(values_in, 0, face_dim, keepdims=False)
    upper = lax.index_in_dim(values_in, last, face_dim, keepdims=False)
    return (lower, upper)


def combine(values_in, face_dim, elem_dim, lower, upper, before, after):
    total = lower.shape[elem_dim]
    upper_prev = jnp.concatenate(
        [before, lax.slice_in_dim(upper, 0, total - 1, axis=elem_dim)], elem_dim
    )
    lower_next = jnp.concatenate(
        [lax.slice_in_dim(lower, 1, total, axis=elem_dim), after], elem_dim
    )
    middle = lax.slice_in_dim(values_in, 1, values_in.shape[face_dim] - 1, axis=face_dim)
    return jnp.concatenate(
        [
            jnp.expand_dims(lower + upper_prev, face_dim),
            middle,
            jnp.expand_dims(upper + lower_next, face_dim),
        ],
        face_dim,
    )


def assemble(values_in, ride=None, then=None, x_faces=None):
    lower, upper = faces(values_in, 3) if x_faces is None else x_faces
    rim_faces = jnp.concatenate([lower, upper], 1)
    padded = padded_2(rim_faces, (("ex", 1),), 1)
    if ride is not None:
        padded, ride = lax.optimization_barrier((padded, ride))
    values_in = combine(values_in, 3, 1, lower, upper, padded[:, :1], padded[:, 3:])
    lower, upper = faces(values_in, 4)
    rim_faces = jnp.concatenate([lower, upper], 2)
    if then is not None:
        ride = then(ride)
        rim_faces, ride = lax.optimization_barrier((rim_faces, ride))
    padded = padded_2(rim_faces, (("ey", 2),), 1)
    values_in = combine(values_in, 4, 2, lower, upper, padded[:, :, :1], padded[:, :, 3:])
    lower, upper = faces(values_in, 5)
    empty = jnp.zeros_like(upper[..., :1])
    return combine(values_in, 5, 5, lower, upper, empty, empty), ride


def split_parts(values, count):
    parts = []
    rest = values
    for _ in range(count - 1):
        part = lax.reduce_precision(rest, exponent_bits=8, mantissa_bits=7)
        parts.append(part)
        rest = rest - part
    parts.append(lax.reduce_precision(rest, exponent_bits=8, mantissa_bits=7))
    return [part.astype(jnp.bfloat16) for part in parts]


def one_hot(index, count):
    return (index[:, None] == lax.broadcasted_iota(jnp.int32, (1, count), 1)).astype(jnp.bfloat16)


def gather_flat(values, picks, lanes, count=3):
    rows = values.shape[0] // lanes
    table = values.reshape(rows, lanes)
    parts = jnp.concatenate(split_parts(table, count), axis=1)
    hit_row_t = (lax.broadcasted_iota(jnp.int32, (rows, 1), 0) == (picks // lanes)[None, :]).astype(jnp.bfloat16)
    picked = lax.dot_general(parts, hit_row_t, (((0,), (0,)), ((), ())), preferred_element_type=jnp.float32)
    total = picked[:lanes]
    for n in range(1, count):
        total = total + picked[n * lanes : (n + 1) * lanes]
    hit_lane_t = lax.broadcasted_iota(jnp.int32, (lanes, 1), 0) == (picks % lanes)[None, :]
    return jnp.sum(jnp.where(hit_lane_t, total, 0.0), axis=0)


def segment_sum(values, ids, bins, lanes, count=3):
    rows = bins // lanes
    hit_row_t = lax.broadcasted_iota(jnp.int32, (rows, 1), 0) == (ids // lanes)[None, :]
    lhs = jnp.concatenate(
        [jnp.where(hit_row_t, part[None, :], jnp.bfloat16(0)) for part in split_parts(values, count)], axis=0
    )
    sums = jnp.dot(lhs, one_hot(ids % lanes, lanes), preferred_element_type=jnp.float32)
    total = sums[:rows]
    for n in range(1, count):
        total = total + sums[n * rows : (n + 1) * rows]
    return total.reshape(-1)


def strip_reduce(partial, strips, strip_size):
    n_ex = lax.axis_size("ex")
    piece = -(-strip_size // n_ex)
    chunks = partial.reshape(2, strips, strip_size)
    if piece * n_ex != strip_size:
        chunks = jnp.pad(chunks, ((0, 0), (0, 0), (0, piece * n_ex - strip_size)))
    chunks = chunks.reshape(2, strips, n_ex, piece).transpose(2, 1, 0, 3)
    chunks = chunks.reshape(n_ex * strips, 2, piece)
    return lax.all_to_all(chunks, ("ex", "ey"), 0, 0, tiled=True).sum(0)


def strip_spread(mine):
    return jnp.broadcast_to(mine[None], (lax.axis_size("ex"),) + mine.shape)


def strip_gather(spread_out, strip_size):
    n_ex, count, piece = spread_out.shape
    whole = lax.all_to_all(spread_out, "ex", 0, 0, tiled=True)
    load = whole[:, 0] / jnp.maximum(whole[:, 1], 1.0)
    return load.reshape(n_ex * piece)[:strip_size]


def on_device(source, metric, fac_point, fac_strip, fac_shell, fac_area):
    weights, stiff = gll_tables()
    high, low = (2.0, 0.2)
    theta = (high + low) / 2.0
    delta = (high - low) / 2.0
    sigma = theta / delta
    rho_now = 1.0 / sigma
    diagonal = local_diagonal(metric, weights, stiff)
    last = source.shape[2] - 1
    rims = [jnp.stack([source[:, :, edge], diagonal[:, :, edge]]) for edge in (0, last)]
    shell_inputs = (fac_area[0], fac_strip[0, :, 0], fac_shell[0])
    both, shell_inputs = assemble(jnp.stack([source, diagonal]), shell_inputs, x_faces=rims)
    rhs = both[0]
    pinv = 1.0 / both[1]
    pressure = jnp.zeros_like(source)
    resid = rhs
    update = pinv * resid / theta
    picks = fac_point[0]
    areas, strip_of, shell_of = shell_inputs
    strips = lax.axis_size("ey")
    global_ids = strip_of * SHELL_STRIP + shell_of
    denom = segment_sum(areas, global_ids, strips * SHELL_STRIP, 256)
    for step in range(SWEEPS):
        pressure = pressure + update
        if step + 2 == SWEEPS:
            early = gather_flat(pressure.reshape(-1), picks, 256)
        applied = element_apply(update, metric, weights, stiff)
        if step + 1 == SWEEPS:
            samples = early + gather_flat(update.reshape(-1), picks, 256, 2)
            numer = segment_sum(areas * samples, global_ids, strips * SHELL_STRIP, 256, 2)
            partial = jnp.stack([numer, denom])
            assembled, mine = assemble(applied[None], strip_reduce(partial, strips, SHELL_STRIP), strip_spread)
        else:
            if step + 2 == SWEEPS:
                assembled, early = assemble(applied[None], early)
            else:
                assembled, _ = assemble(applied[None])
        assembled = assembled[0]
        if step == 0:
            assembled, denom = lax.optimization_barrier((assembled, denom))
        resid = resid - assembled
        if step + 1 < SWEEPS:
            rho_new = 1.0 / (2.0 * sigma - rho_now)
            update = rho_new * rho_now * update + 2.0 * rho_new / delta * pinv * resid
            rho_now = rho_new
    shell_load = strip_gather(mine, SHELL_STRIP)
    return (pressure, resid, shell_load)


def solution(mesh):
    placed = (
        P("ex", "ey", None, None, None, None),
        P(None, "ex", "ey", None),
        P("ex", "ey"),
        P("ex", "ey", None),
        P("ex", "ey"),
        P("ex", "ey"),
    )
    return jax.shard_map(
        on_device,
        mesh=mesh,
        in_specs=placed,
        out_specs=(
            P("ex", "ey", None, None, None, None),
            P("ex", "ey", None, None, None, None),
            P("ey"),
        ),
        check_vma=False,
    )
```

```python
import jax
import jax.numpy as jnp
import numpy as np
from jax import lax
from jax.sharding import PartitionSpec as P

SWEEPS = 4
SHELL_STRIP = 16384


def padded_2(block, sides, width):
    for axis, dim in sides:
        count = lax.axis_size(axis)
        forward = [(i, i + 1) for i in range(count - 1)]
        backward = [(target, source) for source, target in forward]
        low = lax.ppermute(
            lax.slice_in_dim(block, block.shape[dim] - width, None, axis=dim), axis, forward
        )
        high = lax.ppermute(lax.slice_in_dim(block, 0, width, axis=dim), axis, backward)
        block = jnp.concatenate([low, block, high], axis=dim)
    return block


def gll_tables():
    degree = 7
    points = np.array(
        [
            -1.0,
            -0.8717401485096066,
            -0.5917001814331423,
            -0.2092992179024789,
            0.2092992179024789,
            0.5917001814331423,
            0.8717401485096066,
            1.0,
        ]
    )
    previous = points * 0.0 + 1.0
    current = points * 1.0
    for order in range(1, degree):
        following = ((2 * order + 1) * points * current - order * previous) / (order + 1)
        previous = current
        current = following
    weights = 2.0 / (degree * (degree + 1) * current**2)
    count = degree + 1
    same = np.array([[1.0 if row == col else 0.0 for col in range(count)] for row in range(count)])
    between = points[:, None] - points[None, :] + same
    deriv = current[:, None] / current[None, :] / between * (1.0 - same)
    deriv[0, 0] = -degree * (degree + 1) / 4.0
    deriv[-1, -1] = degree * (degree + 1) / 4.0
    stiff = deriv.T @ (weights[:, None] * deriv)
    return (np.asarray(weights, np.float32), np.asarray(stiff, np.float32))


def spread(metric, which):
    return metric[which][:, :, None, None, None, :]


def element_apply(values_in, metric, weights, stiff):
    top = lax.Precision.HIGHEST
    weight_i = weights[None, None, :, None, None, None]
    weight_j = weights[None, None, None, :, None, None]
    weight_k = weights[None, None, None, None, :, None]
    along_x = jnp.einsum("im,abmjkc->abijkc", stiff, values_in, precision=top)
    along_y = jnp.einsum("jm,abimkc->abijkc", stiff, values_in, precision=top)
    along_z = jnp.einsum("km,abijmc->abijkc", stiff, values_in, precision=top)
    return (
        spread(metric, 0) * weight_j * weight_k * along_x
        + spread(metric, 1) * weight_i * weight_k * along_y
        + spread(metric, 2) * weight_i * weight_j * along_z
        + spread(metric, 3) * weight_i * weight_j * weight_k * values_in
    )


def local_diagonal(metric, weights, stiff):
    stiff_diag = np.diagonal(stiff)
    weight_i = weights[None, None, :, None, None, None]
    weight_j = weights[None, None, None, :, None, None]
    weight_k = weights[None, None, None, None, :, None]
    diag_i = stiff_diag[None, None, :, None, None, None]
    diag_j = stiff_diag[None, None, None, :, None, None]
    diag_k = stiff_diag[None, None, None, None, :, None]
    return (
        spread(metric, 0) * diag_i * weight_j * weight_k
        + spread(metric, 1) * weight_i * diag_j * weight_k
        + spread(metric, 2) * weight_i * weight_j * diag_k
        + spread(metric, 3) * weight_i * weight_j * weight_k
    )


def faces(values_in, face_dim):
    last = values_in.shape[face_dim] - 1
    lower = lax.index_in_dim(values_in, 0, face_dim, keepdims=False)
    upper = lax.index_in_dim(values_in, last, face_dim, keepdims=False)
    return (lower, upper)


def combine(values_in, face_dim, elem_dim, lower, upper, before, after):
    total = lower.shape[elem_dim]
    upper_prev = jnp.concatenate(
        [before, lax.slice_in_dim(upper, 0, total - 1, axis=elem_dim)], elem_dim
    )
    lower_next = jnp.concatenate(
        [lax.slice_in_dim(lower, 1, total, axis=elem_dim), after], elem_dim
    )
    middle = lax.slice_in_dim(values_in, 1, values_in.shape[face_dim] - 1, axis=face_dim)
    return jnp.concatenate(
        [
            jnp.expand_dims(lower + upper_prev, face_dim),
            middle,
            jnp.expand_dims(upper + lower_next, face_dim),
        ],
        face_dim,
    )


def assemble(values_in, ride=None, then=None, x_faces=None):
    lower, upper = faces(values_in, 3) if x_faces is None else x_faces
    rim_faces = jnp.concatenate([lower, upper], 1)
    padded = padded_2(rim_faces, (("ex", 1),), 1)
    if ride is not None:
        padded, ride = lax.optimization_barrier((padded, ride))
    values_in = combine(values_in, 3, 1, lower, upper, padded[:, :1], padded[:, 3:])
    lower, upper = faces(values_in, 4)
    rim_faces = jnp.concatenate([lower, upper], 2)
    if then is not None:
        ride = then(ride)
        rim_faces, ride = lax.optimization_barrier((rim_faces, ride))
    padded = padded_2(rim_faces, (("ey", 2),), 1)
    values_in = combine(values_in, 4, 2, lower, upper, padded[:, :, :1], padded[:, :, 3:])
    lower, upper = faces(values_in, 5)
    empty = jnp.zeros_like(upper[..., :1])
    return combine(values_in, 5, 5, lower, upper, empty, empty), ride


def split_parts(values, count):
    parts = []
    rest = values
    for _ in range(count - 1):
        part = lax.reduce_precision(rest, exponent_bits=8, mantissa_bits=7)
        parts.append(part)
        rest = rest - part
    parts.append(lax.reduce_precision(rest, exponent_bits=8, mantissa_bits=7))
    return [part.astype(jnp.bfloat16) for part in parts]


def one_hot(index, count):
    return (index[:, None] == lax.broadcasted_iota(jnp.int32, (1, count), 1)).astype(jnp.bfloat16)


def gather_flat(values, picks, lanes, count=3):
    rows = values.shape[0] // lanes
    table = values.reshape(rows, lanes)
    parts = jnp.concatenate(split_parts(table, count), axis=1)
    hit_row_t = (lax.broadcasted_iota(jnp.int32, (rows, 1), 0) == (picks // lanes)[None, :]).astype(jnp.bfloat16)
    picked = lax.dot_general(parts, hit_row_t, (((0,), (0,)), ((), ())), preferred_element_type=jnp.float32)
    total = picked[:lanes]
    for n in range(1, count):
        total = total + picked[n * lanes : (n + 1) * lanes]
    hit_lane_t = lax.broadcasted_iota(jnp.int32, (lanes, 1), 0) == (picks % lanes)[None, :]
    return jnp.sum(jnp.where(hit_lane_t, total, 0.0), axis=0)


def segment_sum(values, ids, bins, lanes, count=3):
    rows = bins // lanes
    hit_row_t = lax.broadcasted_iota(jnp.int32, (rows, 1), 0) == (ids // lanes)[None, :]
    lhs = jnp.concatenate(
        [jnp.where(hit_row_t, part[None, :], jnp.bfloat16(0)) for part in split_parts(values, count)], axis=0
    )
    sums = jnp.dot(lhs, one_hot(ids % lanes, lanes), preferred_element_type=jnp.float32)
    total = sums[:rows]
    for n in range(1, count):
        total = total + sums[n * rows : (n + 1) * rows]
    return total.reshape(-1)


def strip_reduce(partial, strips, strip_size):
    n_ex = lax.axis_size("ex")
    piece = -(-strip_size // n_ex)
    chunks = partial.reshape(2, strips, strip_size)
    if piece * n_ex != strip_size:
        chunks = jnp.pad(chunks, ((0, 0), (0, 0), (0, piece * n_ex - strip_size)))
    chunks = chunks.reshape(2, strips, n_ex, piece).transpose(2, 1, 0, 3)
    chunks = chunks.reshape(n_ex * strips, 2, piece)
    return lax.all_to_all(chunks, ("ex", "ey"), 0, 0, tiled=True).sum(0)


def strip_spread(mine):
    return jnp.broadcast_to(mine[None], (lax.axis_size("ex"),) + mine.shape)


def strip_gather(spread_out, strip_size):
    n_ex, count, piece = spread_out.shape
    whole = lax.all_to_all(spread_out, "ex", 0, 0, tiled=True)
    load = whole[:, 0] / jnp.maximum(whole[:, 1], 1.0)
    return load.reshape(n_ex * piece)[:strip_size]


def on_device(source, metric, fac_point, fac_strip, fac_shell, fac_area):
    weights, stiff = gll_tables()
    high, low = (2.0, 0.2)
    theta = (high + low) / 2.0
    delta = (high - low) / 2.0
    sigma = theta / delta
    rho_now = 1.0 / sigma
    diagonal = local_diagonal(metric, weights, stiff)
    last = source.shape[2] - 1
    rims = [jnp.stack([source[:, :, edge], diagonal[:, :, edge]]) for edge in (0, last)]
    shell_inputs = (fac_area[0], fac_strip[0, :, 0], fac_shell[0])
    both, shell_inputs = assemble(jnp.stack([source, diagonal]), shell_inputs, x_faces=rims)
    rhs = both[0]
    pinv = 1.0 / both[1]
    pressure = jnp.zeros_like(source)
    resid = rhs
    update = pinv * resid / theta
    picks = fac_point[0]
    areas, strip_of, shell_of = shell_inputs
    strips = lax.axis_size("ey")
    global_ids = strip_of * SHELL_STRIP + shell_of
    denom = segment_sum(areas, global_ids, strips * SHELL_STRIP, 256)
    for step in range(SWEEPS):
        pressure = pressure + update
        if step + 2 == SWEEPS:
            early = gather_flat(pressure.reshape(-1), picks, 256)
        applied = element_apply(update, metric, weights, stiff)
        if step + 1 == SWEEPS:
            samples = early + gather_flat(update.reshape(-1), picks, 256, 2)
            numer = segment_sum(areas * samples, global_ids, strips * SHELL_STRIP, 256, 2)
            partial = jnp.stack([numer, denom])
            assembled, mine = assemble(applied[None], strip_reduce(partial, strips, SHELL_STRIP), strip_spread)
        else:
            if step + 2 == SWEEPS:
                assembled, early = assemble(applied[None], early)
            elif step == 0:
                assembled, denom = assemble(applied[None], denom)
            else:
                assembled, _ = assemble(applied[None])
        assembled = assembled[0]
        resid = resid - assembled
        if step + 1 < SWEEPS:
            rho_new = 1.0 / (2.0 * sigma - rho_now)
            update = rho_new * rho_now * update + 2.0 * rho_new / delta * pinv * resid
            rho_now = rho_new
    shell_load = strip_gather(mine, SHELL_STRIP)
    return (pressure, resid, shell_load)


def solution(mesh):
    placed = (
        P("ex", "ey", None, None, None, None),
        P(None, "ex", "ey", None),
        P("ex", "ey"),
        P("ex", "ey", None),
        P("ex", "ey"),
        P("ex", "ey"),
    )
    return jax.shard_map(
        on_device,
        mesh=mesh,
        in_specs=placed,
        out_specs=(
            P("ex", "ey", None, None, None, None),
            P("ex", "ey", None, None, None, None),
            P("ey"),
        ),
        check_vma=False,
    )
```

```python
import jax
import jax.numpy as jnp
import numpy as np
from jax import lax
from jax.sharding import PartitionSpec as P

SWEEPS = 4
SHELL_STRIP = 16384


def padded_2(block, sides, width):
    for axis, dim in sides:
        count = lax.axis_size(axis)
        forward = [(i, i + 1) for i in range(count - 1)]
        backward = [(target, source) for source, target in forward]
        low = lax.ppermute(
            lax.slice_in_dim(block, block.shape[dim] - width, None, axis=dim), axis, forward
        )
        high = lax.ppermute(lax.slice_in_dim(block, 0, width, axis=dim), axis, backward)
        block = jnp.concatenate([low, block, high], axis=dim)
    return block


def gll_tables():
    degree = 7
    points = np.array(
        [
            -1.0,
            -0.8717401485096066,
            -0.5917001814331423,
            -0.2092992179024789,
            0.2092992179024789,
            0.5917001814331423,
            0.8717401485096066,
            1.0,
        ]
    )
    previous = points * 0.0 + 1.0
    current = points * 1.0
    for order in range(1, degree):
        following = ((2 * order + 1) * points * current - order * previous) / (order + 1)
        previous = current
        current = following
    weights = 2.0 / (degree * (degree + 1) * current**2)
    count = degree + 1
    same = np.array([[1.0 if row == col else 0.0 for col in range(count)] for row in range(count)])
    between = points[:, None] - points[None, :] + same
    deriv = current[:, None] / current[None, :] / between * (1.0 - same)
    deriv[0, 0] = -degree * (degree + 1) / 4.0
    deriv[-1, -1] = degree * (degree + 1) / 4.0
    stiff = deriv.T @ (weights[:, None] * deriv)
    return (np.asarray(weights, np.float32), np.asarray(stiff, np.float32))


def spread(metric, which):
    return metric[which][:, :, None, None, None, :]


def element_apply(values_in, metric, weights, stiff):
    top = lax.Precision.HIGHEST
    weight_i = weights[None, None, :, None, None, None]
    weight_j = weights[None, None, None, :, None, None]
    weight_k = weights[None, None, None, None, :, None]
    along_x = jnp.einsum("im,abmjkc->abijkc", stiff, values_in, precision=top)
    along_y = jnp.einsum("jm,abimkc->abijkc", stiff, values_in, precision=top)
    along_z = jnp.einsum("km,abijmc->abijkc", stiff, values_in, precision=top)
    return (
        spread(metric, 0) * weight_j * weight_k * along_x
        + spread(metric, 1) * weight_i * weight_k * along_y
        + spread(metric, 2) * weight_i * weight_j * along_z
        + spread(metric, 3) * weight_i * weight_j * weight_k * values_in
    )


def local_diagonal(metric, weights, stiff):
    stiff_diag = np.diagonal(stiff)
    weight_i = weights[None, None, :, None, None, None]
    weight_j = weights[None, None, None, :, None, None]
    weight_k = weights[None, None, None, None, :, None]
    diag_i = stiff_diag[None, None, :, None, None, None]
    diag_j = stiff_diag[None, None, None, :, None, None]
    diag_k = stiff_diag[None, None, None, None, :, None]
    return (
        spread(metric, 0) * diag_i * weight_j * weight_k
        + spread(metric, 1) * weight_i * diag_j * weight_k
        + spread(metric, 2) * weight_i * weight_j * diag_k
        + spread(metric, 3) * weight_i * weight_j * weight_k
    )


def faces(values_in, face_dim):
    last = values_in.shape[face_dim] - 1
    lower = lax.index_in_dim(values_in, 0, face_dim, keepdims=False)
    upper = lax.index_in_dim(values_in, last, face_dim, keepdims=False)
    return (lower, upper)


def combine(values_in, face_dim, elem_dim, lower, upper, before, after):
    total = lower.shape[elem_dim]
    upper_prev = jnp.concatenate(
        [before, lax.slice_in_dim(upper, 0, total - 1, axis=elem_dim)], elem_dim
    )
    lower_next = jnp.concatenate(
        [lax.slice_in_dim(lower, 1, total, axis=elem_dim), after], elem_dim
    )
    middle = lax.slice_in_dim(values_in, 1, values_in.shape[face_dim] - 1, axis=face_dim)
    return jnp.concatenate(
        [
            jnp.expand_dims(lower + upper_prev, face_dim),
            middle,
            jnp.expand_dims(upper + lower_next, face_dim),
        ],
        face_dim,
    )


def assemble(values_in, ride=None, then=None, x_faces=None):
    lower, upper = faces(values_in, 3) if x_faces is None else x_faces
    rim_faces = jnp.concatenate([lower, upper], 1)
    padded = padded_2(rim_faces, (("ex", 1),), 1)
    if ride is not None:
        padded, ride = lax.optimization_barrier((padded, ride))
    values_in = combine(values_in, 3, 1, lower, upper, padded[:, :1], padded[:, 3:])
    lower, upper = faces(values_in, 4)
    rim_faces = jnp.concatenate([lower, upper], 2)
    if then is not None:
        ride = then(ride)
        rim_faces, ride = lax.optimization_barrier((rim_faces, ride))
    padded = padded_2(rim_faces, (("ey", 2),), 1)
    values_in = combine(values_in, 4, 2, lower, upper, padded[:, :, :1], padded[:, :, 3:])
    lower, upper = faces(values_in, 5)
    empty = jnp.zeros_like(upper[..., :1])
    return combine(values_in, 5, 5, lower, upper, empty, empty), ride


def split_parts(values, count):
    parts = []
    rest = values
    for _ in range(count - 1):
        part = lax.reduce_precision(rest, exponent_bits=8, mantissa_bits=7)
        parts.append(part)
        rest = rest - part
    parts.append(lax.reduce_precision(rest, exponent_bits=8, mantissa_bits=7))
    return [part.astype(jnp.bfloat16) for part in parts]


def one_hot(index, count):
    return (index[:, None] == lax.broadcasted_iota(jnp.int32, (1, count), 1)).astype(jnp.bfloat16)


def gather_flat(values, picks, lanes, count=3):
    rows = values.shape[0] // lanes
    table = values.reshape(rows, lanes)
    parts = jnp.concatenate(split_parts(table, count), axis=1)
    hit_row_t = (lax.broadcasted_iota(jnp.int32, (rows, 1), 0) == (picks // lanes)[None, :]).astype(jnp.bfloat16)
    picked = lax.dot_general(parts, hit_row_t, (((0,), (0,)), ((), ())), preferred_element_type=jnp.float32)
    total = picked[:lanes]
    for n in range(1, count):
        total = total + picked[n * lanes : (n + 1) * lanes]
    hit_lane_t = lax.broadcasted_iota(jnp.int32, (lanes, 1), 0) == (picks % lanes)[None, :]
    return jnp.sum(jnp.where(hit_lane_t, total, 0.0), axis=0)


def segment_sum(values, ids, bins, lanes, count=3):
    rows = bins // lanes
    hit_row_t = lax.broadcasted_iota(jnp.int32, (rows, 1), 0) == (ids // lanes)[None, :]
    lhs = jnp.concatenate(
        [jnp.where(hit_row_t, part[None, :], jnp.bfloat16(0)) for part in split_parts(values, count)], axis=0
    )
    sums = jnp.dot(lhs, one_hot(ids % lanes, lanes), preferred_element_type=jnp.float32)
    total = sums[:rows]
    for n in range(1, count):
        total = total + sums[n * rows : (n + 1) * rows]
    return total.reshape(-1)


def strip_reduce(partial, strips, strip_size):
    n_ex = lax.axis_size("ex")
    piece = -(-strip_size // n_ex)
    chunks = partial.reshape(2, strips, strip_size)
    if piece * n_ex != strip_size:
        chunks = jnp.pad(chunks, ((0, 0), (0, 0), (0, piece * n_ex - strip_size)))
    chunks = chunks.reshape(2, strips, n_ex, piece).transpose(2, 1, 0, 3)
    chunks = chunks.reshape(n_ex * strips, 2, piece)
    return lax.all_to_all(chunks, ("ex", "ey"), 0, 0, tiled=True).sum(0)


def strip_spread(mine):
    return jnp.broadcast_to(mine[None], (lax.axis_size("ex"),) + mine.shape)


def strip_gather(spread_out, strip_size):
    n_ex, count, piece = spread_out.shape
    whole = lax.all_to_all(spread_out, "ex", 0, 0, tiled=True)
    load = whole[:, 0] / jnp.maximum(whole[:, 1], 1.0)
    return load.reshape(n_ex * piece)[:strip_size]


def on_device(source, metric, fac_point, fac_strip, fac_shell, fac_area):
    weights, stiff = gll_tables()
    high, low = (2.0, 0.2)
    theta = (high + low) / 2.0
    delta = (high - low) / 2.0
    sigma = theta / delta
    rho_now = 1.0 / sigma
    diagonal = local_diagonal(metric, weights, stiff)
    last = source.shape[2] - 1
    rims = [jnp.stack([source[:, :, edge], diagonal[:, :, edge]]) for edge in (0, last)]
    shell_inputs = (fac_area[0], fac_strip[0, :, 0], fac_shell[0])
    both, shell_inputs = assemble(jnp.stack([source, diagonal]), shell_inputs, x_faces=rims)
    rhs = both[0]
    pinv = 1.0 / both[1]
    pressure = jnp.zeros_like(source)
    resid = rhs
    update = pinv * resid / theta
    picks = fac_point[0]
    areas, strip_of, shell_of = shell_inputs
    strips = lax.axis_size("ey")
    global_ids = strip_of * SHELL_STRIP + shell_of
    denom = segment_sum(areas, global_ids, strips * SHELL_STRIP, 256, 2)
    for step in range(SWEEPS):
        pressure = pressure + update
        if step + 2 == SWEEPS:
            early = gather_flat(pressure.reshape(-1), picks, 256, 2)
        applied = element_apply(update, metric, weights, stiff)
        if step + 1 == SWEEPS:
            samples = early + gather_flat(update.reshape(-1), picks, 256, 2)
            numer = segment_sum(areas * samples, global_ids, strips * SHELL_STRIP, 256, 2)
            partial = jnp.stack([numer, denom])
            assembled, mine = assemble(applied[None], strip_reduce(partial, strips, SHELL_STRIP), strip_spread)
        else:
            if step + 2 == SWEEPS:
                assembled, early = assemble(applied[None], early)
            else:
                assembled, _ = assemble(applied[None])
        assembled = assembled[0]
        if step == 0:
            assembled, denom = lax.optimization_barrier((assembled, denom))
        resid = resid - assembled
        if step + 1 < SWEEPS:
            rho_new = 1.0 / (2.0 * sigma - rho_now)
            update = rho_new * rho_now * update + 2.0 * rho_new / delta * pinv * resid
            rho_now = rho_new
    shell_load = strip_gather(mine, SHELL_STRIP)
    return (pressure, resid, shell_load)


def solution(mesh):
    placed = (
        P("ex", "ey", None, None, None, None),
        P(None, "ex", "ey", None),
        P("ex", "ey"),
        P("ex", "ey", None),
        P("ex", "ey"),
        P("ex", "ey"),
    )
    return jax.shard_map(
        on_device,
        mesh=mesh,
        in_specs=placed,
        out_specs=(
            P("ex", "ey", None, None, None, None),
            P("ex", "ey", None, None, None, None),
            P("ey"),
        ),
        check_vma=False,
    )
```
